32 devices in a mesh: comp: 2 (over core), gx: 4 (over z), gy: 4 (over y, x).
Axes of the slice: x: 2, y: 2, z: 4, core: 2. Of those that a mesh axis runs over, the one named last changes fastest.
Arguments:
- adjoint_in: float32 [2, 4, 32, 32, 512], P('comp', None, None, 'gx', 'gy'), may hold values from -6 to 6
- u_east: float32 [2, 32, 32, 512], P('comp', None, 'gx', 'gy'), may hold values from -0.4 to 0.4
- u_north: float32 [2, 32, 32, 512], P('comp', None, 'gx', 'gy'), may hold values from -0.4 to 0.4
- diffusivity: float32 [2, 4, 32, 32, 512], P('comp', None, None, 'gx', 'gy'), may hold values from 0.1 to 10
- wet_mask: int32 [2, 32, 512], P('comp', 'gx', 'gy'), may hold values 0 or 1
- dest_tile: int32 [2, 4, 4, 32, 1], P('comp', 'gx', 'gy'), may hold values from 0 to 15; in each aligned block of 32 rows (0 to 31, 32 to 63, ..., all dimensions but the last counted through in order) at most 4 rows name the same one
- src_row: int32 [2, 4, 4, 32], P('comp', 'gx', 'gy'), may hold values from 0 to 7
- dst_row: int32 [2, 4, 4, 32], P('comp', 'gx', 'gy'), may hold values from 0 to 7
- area_weight: float32 [2, 4, 4, 32, 128], P('comp', 'gx', 'gy'), may hold values from 0.2 to 0.8
Outputs:
- adjoint_out: float32 [2, 4, 32, 32, 512], P('comp', None, None, 'gx', 'gy')
The draws below stay inside these ranges and needn't reach their ends.
Inputs may be any that keep to these rules, and one draw needn't show every extreme that they name: `dest_tile`: among the rows of one device no tile is named more than 4 times, and some device names some tile exactly 4 times.
All inputs are finite; a program needn't handle non-finite values. No bound on the sum of `wet_mask` on one device may be relied on, other than what follows from the above.
Results may differ from the reference program's by a relative error of at most 0.0001.
Values sent between devices are 32-bit elements; how exact they have to be, the bound alone decides.
No kernel may reach another device: no remote copies, remote signals or barrier semaphores. Data moves between devices by JAX's collectives and lax.ppermute only.
A program may use at most 64 MiB of HBM per device.

```python
import math
import jax
import jax.numpy as jnp
import numpy as np
from jax import lax

F = 4
L = 32
CX = 8
CY = 128
CAP = 4
BLOCKS = 32
NX = 32
NY = 512
N_GX = 4
N_GY = 4


def plant(values, stream_key, least, largest):
    spot = [jax.random.randint(jax.random.fold_in(stream_key, axis), (), 0, length) for axis, length in enumerate(values.shape)]
    longest = values.shape.index(max(values.shape))
    beside = spot[:longest] + [(spot[longest] + 1) % values.shape[longest]] + spot[longest + 1:]
    return values.at[tuple(spot)].set(least).at[tuple(beside)].set(largest)


def block_scale(key, extent, split, smallest, high):
    level = 1.0
    for dim, parts in split:
        draws = jax.random.uniform(jax.random.fold_in(jax.random.fold_in(key, 6), dim), (parts,), jnp.float32, smallest / len(split), high / len(split))
        level = level * jnp.repeat(jnp.exp(draws), extent[dim] // parts).reshape((-1,) + (1,) * (len(extent) - 1 - dim))
    return level


def deal_out(rng, own, number, rows, amount, top, limit, slope):
    ranking = jax.random.permutation(rng, amount)
    crowded, usual = load_shares(amount, rows * top, limit, slope, True), load_shares(amount, rows * top, limit, slope, False)
    places = jnp.arange(amount)

    def named(sizes, rotation):
        used = int((sizes > 0).sum())
        fixed = max(1, used // 4)
        moved = fixed + (places - fixed + rotation * (used - fixed)) % max(1, amount - fixed)
        return jnp.zeros((amount,), jnp.int32).at[ranking[jnp.where(places < fixed, places, moved)]].set(jnp.asarray(sizes, jnp.int32))

    sizes = jnp.where(number % 4 == 0, named(crowded, number // 4), named(usual, number - number // 4 - 1))
    mixed = jax.random.permutation(jax.random.fold_in(own, 3), amount)
    source_of, sink = mixed[0:amount // 2 * 2:2], mixed[1:amount // 2 * 2:2]
    room = jnp.minimum(sizes[source_of] - 1, limit - sizes[sink]) // 2
    room = jnp.where((source_of == ranking[0]) | (sink == ranking[0]) | (sizes[sink] == 0), 0, jnp.maximum(room, 0))
    moved = jax.random.randint(jax.random.fold_in(own, 4), (amount // 2,), 0, 1 << 20) % (room + 1)
    sizes = sizes.at[source_of].add(-moved).at[sink].add(moved)
    labels = jnp.searchsorted(jnp.cumsum(sizes), jnp.arange(rows * top), side="right").astype(jnp.int32)
    listing = labels.reshape(top, rows).T
    listing = listing[jax.random.permutation(jax.random.fold_in(own, 1), rows)]
    rotation = jax.random.randint(jax.random.fold_in(own, 2), (rows, 1), 0, top)
    return jnp.take_along_axis(listing, (jnp.arange(top)[None, :] + rotation) % top, axis=1)


def load_shares(number_of, total, limit, lean, full):
    portions = [(1 << 20) // math.isqrt(rank ** lean) + 1 for rank in range(1, number_of + 1)]
    largest = limit if full else min(limit, max(-(-total // number_of), total * portions[0] // sum(portions)))
    least = 1 if total - largest >= number_of - 1 else 0
    counts, spare = [largest] + [least] * (number_of - 1), total - largest - least * (number_of - 1)
    while spare > 0:
        free = [i for i in range(1, number_of) if counts[i] < largest] or [i for i in range(1, number_of) if counts[i] < limit]
        whole, budget = sum([portions[i] for i in free]), spare
        for i in free:
            addition = min(limit - counts[i], max(1, budget * portions[i] // whole), spare)
            counts[i] = counts[i] + addition
            spare = spare - addition
    return np.array(counts)


def centred(own_key, extent, spread, bound, split=(), kind=jnp.bfloat16):
    entries = jax.random.normal(own_key, extent, jnp.float32) * spread
    if len(split) > 0:
        entries = block_scale(own_key, extent, split, -0.22, 0.18) * entries
    return jnp.clip(entries, min=-bound, max=bound).astype(kind)


def setup_inputs(seed: int = 0) -> dict:
    key_of = jax.random.split(jax.random.key(seed), 10)
    adjoint_in = centred(key_of[0], (2, F, L, NX, NY), 1.0, 6.0, ((0, 2), (3, 4), (4, 4)), jnp.float32)
    u_east = jnp.clip(jax.random.uniform(key_of[1], (2, L, NX, NY), jnp.float32, -0.4, 0.4) * block_scale(key_of[1], (2, L, NX, NY), ((0, 2), (2, 4), (3, 4)), -0.4, 0.0), -0.4, 0.4)
    u_north = jnp.clip(jax.random.uniform(key_of[2], (2, L, NX, NY), jnp.float32, -0.4, 0.4) * block_scale(key_of[2], (2, L, NX, NY), ((0, 2), (2, 4), (3, 4)), -0.4, 0.0), -0.4, 0.4)
    diffusivity = jnp.clip(jnp.exp(math.log(10.0) - 4.6051702 * jax.random.uniform(key_of[3], (2, F, L, NX, NY), jnp.float32) ** block_scale(key_of[3], (2, F, L, NX, NY), ((0, 2), (3, 4), (4, 4)), -0.2, 0.2)), 0.1, 10.0)
    wet_mask = plant((jax.random.randint(key_of[4], (2, NX, NY), 0, 4) < 3).astype(jnp.int32), jax.random.fold_in(key_of[4], 1), 0, 1)
    dest_tile_keys = jax.random.split(jax.random.fold_in(key_of[5], 1), 2 * N_GX * N_GY * BLOCKS // BLOCKS)
    dest_tile_turns = jax.random.permutation(jax.random.fold_in(key_of[5], 3), 2 * N_GX * N_GY * BLOCKS // BLOCKS)
    dest_tile = jax.vmap(lambda own, number: deal_out(jax.random.fold_in(key_of[5], 2), own, number, BLOCKS, N_GX * N_GY, 1, CAP, 2))(dest_tile_keys, dest_tile_turns).reshape((2, N_GX, N_GY, BLOCKS, 1))
    src_row = plant(jax.random.randint(key_of[6], (2, N_GX, N_GY, BLOCKS), 0, CX), jax.random.fold_in(key_of[6], 1), 0, CX - 1).astype(jnp.int32)
    dst_row = plant(jax.random.randint(key_of[7], (2, N_GX, N_GY, BLOCKS), 0, CX), jax.random.fold_in(key_of[7], 1), 0, CX - 1).astype(jnp.int32)
    area_weight = jnp.clip(0.2 + 0.6 * jax.random.uniform(key_of[8], (2, N_GX, N_GY, BLOCKS, CY), jnp.float32) ** block_scale(key_of[8], (2, N_GX, N_GY, BLOCKS, CY), ((0, 2), (1, 4), (2, 4)), -0.2, 0.2), 0.2, 0.8)
    return {"adjoint_in": adjoint_in, "u_east": u_east, "u_north": u_north, "diffusivity": diffusivity, "wet_mask": wet_mask, "dest_tile": dest_tile, "src_row": src_row, "dst_row": dst_row, "area_weight": area_weight}


diffusion = 0.2


def stencil_core(values, east_flux, north_flux):
    centre = values[..., 1:-1, 1:-1]
    laplace = values[..., 2:, 1:-1] + values[..., :-2, 1:-1] + values[..., 1:-1, 2:] + values[..., 1:-1, :-2] - 4.0 * centre
    advect = 0.5 * (east_flux[..., :-2, 1:-1] - east_flux[..., 2:, 1:-1]) + 0.5 * (north_flux[..., 1:-1, :-2] - north_flux[..., 1:-1, 2:])
    return centre + diffusion * laplace + advect


def column_solve(right_side, coeffs):
    levels = right_side.shape[-3]
    cprime = []
    dprime = []
    for depth_index in range(levels):
        diagonal = 1.0 + jnp.zeros_like(right_side[..., 0, :, :])
        if depth_index < levels - 1:
            diagonal = diagonal + coeffs[..., depth_index, :, :]
        if depth_index > 0:
            coupling_dn = coeffs[..., depth_index - 1, :, :]
            divisor = diagonal + coupling_dn + coupling_dn * cprime[depth_index - 1]
            numerator = right_side[..., depth_index, :, :] + coupling_dn * dprime[depth_index - 1]
        else:
            divisor = diagonal
            numerator = right_side[..., 0, :, :]
        if depth_index < levels - 1:
            cprime.append(-coeffs[..., depth_index, :, :] / divisor)
        dprime.append(numerator / divisor)
    result = [None] * levels
    result[levels - 1] = dprime[levels - 1]
    for depth_index in range(levels - 2, -1, -1):
        result[depth_index] = dprime[depth_index] - cprime[depth_index] * result[depth_index + 1]
    return jnp.stack(result, axis=-3)


def reference(adjoint_in, u_east, u_north, diffusivity, wet_mask, dest_tile, src_row, dst_row, area_weight):
    fields = adjoint_in.shape[1]
    surface = jnp.transpose(adjoint_in[:, :, 0], (0, 2, 1, 3)).reshape(2, NX, fields, N_GY, CY)
    surface = jnp.transpose(surface, (0, 1, 3, 2, 4))
    section = lax.broadcasted_iota(jnp.int32, src_row.shape, 0)
    tile_x = lax.broadcasted_iota(jnp.int32, src_row.shape, 1)
    tile_y = lax.broadcasted_iota(jnp.int32, src_row.shape, 2)
    source_rows = tile_x * CX + src_row
    picked = surface[section, source_rows, tile_y]
    payload = picked * area_weight[..., None, :]
    target = dest_tile[..., 0]
    target_key = ((1 - section) * NX + (target // N_GY) * CX + dst_row) * N_GY + target % N_GY
    increment = jax.ops.segment_sum(payload.reshape(-1, fields, CY), target_key.reshape(-1), num_segments=2 * NX * N_GY)
    increment = jnp.transpose(increment.reshape(2, NX, N_GY, fields, CY), (0, 3, 1, 2, 4)).reshape(2, fields, NX, NY)
    adjoint = adjoint_in.at[:, :, 0].add(increment)
    wet = wet_mask.astype(adjoint.dtype)[:, None, None]
    east = u_east[:, None]
    north = u_north[:, None]
    padding = ((0, 0), (0, 0), (0, 0), (1, 1), (1, 1))
    for window_step in range(2):
        horizontal = stencil_core(jnp.pad(adjoint, padding), jnp.pad(east * adjoint, padding), jnp.pad(north * adjoint, padding))
        adjoint = column_solve(horizontal, diffusivity) * wet
    return adjoint
```

```python
import jax
import jax.numpy as jnp
from jax import lax
from jax.experimental import pallas as pl
from jax.experimental.pallas import tpu as pltpu
from jax.sharding import PartitionSpec as P

CAP = 4


diffusion = 0.2


def shift(block, axis, step):
    count = lax.axis_size(axis)
    route = [(i, i + step) for i in range(count) if 0 <= i + step < count]
    return lax.ppermute(block, axis, route)


def step_kernel(fields, levels, rows, cols, coupled):
    def kernel(*refs):
        if coupled:
            (a_ref, up_ref, dn_ref, lf_ref, rt_ref, cu_ref, cd_ref, cl_ref, cr_ref, ue_ref, un_ref,
             k_ref, wet_ref, inc_ref, iu_ref, id_ref, il_ref, ir_ref, out_ref, c_ref) = refs
        else:
            (a_ref, up_ref, dn_ref, lf_ref, rt_ref, cu_ref, cd_ref, cl_ref, cr_ref, ue_ref, un_ref,
             k_ref, wet_ref, out_ref, c_ref) = refs
        row = lax.broadcasted_iota(jnp.int32, (rows, cols), 0)
        col = lax.broadcasted_iota(jnp.int32, (rows, cols), 1)
        top = row == 0
        bottom = row == rows - 1
        left = col == 0
        right = col == cols - 1
        cprev = [None] * fields
        dprev = [None] * fields
        for l in range(levels):
            ue = ue_ref[l]
            un = un_ref[l]
            ue_m = jnp.where(top, cu_ref[fields, l], pltpu.roll(ue, 1, 0))
            ue_p = jnp.where(bottom, cd_ref[fields, l], pltpu.roll(ue, rows - 1, 0))
            un_m = jnp.where(left, cl_ref[fields, l], pltpu.roll(un, 1, 1))
            un_p = jnp.where(right, cr_ref[fields, l], pltpu.roll(un, cols - 1, 1))
            for f in range(fields):
                a = a_ref[f, l]
                up = up_ref[f, l]
                dn = dn_ref[f, l]
                lf = lf_ref[f, l]
                rt = rt_ref[f, l]
                if coupled and l == 0:
                    a = a + inc_ref[f]
                    up = up + iu_ref[f]
                    dn = dn + id_ref[f]
                    lf = lf + il_ref[f]
                    rt = rt + ir_ref[f]
                a_im = jnp.where(top, up, pltpu.roll(a, 1, 0))
                a_ip = jnp.where(bottom, dn, pltpu.roll(a, rows - 1, 0))
                a_jm = jnp.where(left, lf, pltpu.roll(a, 1, 1))
                a_jp = jnp.where(right, rt, pltpu.roll(a, cols - 1, 1))
                laplace = a_ip + a_im + a_jp + a_jm - 4.0 * a
                advect = 0.5 * (ue_m * a_im - ue_p * a_ip) + 0.5 * (un_m * a_jm - un_p * a_jp)
                h = a + diffusion * laplace + advect
                if l < levels - 1:
                    kd = k_ref[f, l]
                    diagonal = 1.0 + kd
                else:
                    diagonal = 1.0
                if l > 0:
                    kp = k_ref[f, l - 1]
                    divisor = diagonal + kp + kp * cprev[f]
                    numerator = h + kp * dprev[f]
                else:
                    divisor = diagonal
                    numerator = h
                if l < levels - 1:
                    cprev[f] = -kd / divisor
                    c_ref[f, l] = cprev[f]
                dprev[f] = numerator / divisor
                out_ref[f, l] = dprev[f]
        wet = wet_ref[...]
        for f in range(fields):
            r = dprev[f]
            out_ref[f, levels - 1] = r * wet
            for l in range(levels - 2, -1, -1):
                r = out_ref[f, l] - c_ref[f, l] * r
                out_ref[f, l] = r * wet

    return kernel


def run_step(a, halos, coef_halos, ue, un, coeffs, wet, inc=None):
    fields, levels, rows, cols = a.shape
    coupled = inc is not None
    operands = [a, *halos, *coef_halos, ue, un, coeffs, wet]
    if coupled:
        operands += list(inc)
    return pl.pallas_call(
        step_kernel(fields, levels, rows, cols, coupled),
        out_shape=jax.ShapeDtypeStruct(a.shape, jnp.float32),
        scratch_shapes=[pltpu.VMEM(a.shape, jnp.float32)],
    )(*operands)


def edges(value):
    rows, cols = value.shape[-2:]
    return (
        value[..., rows - 1 : rows, :],
        value[..., 0:1, :],
        value[..., :, cols - 1 : cols],
        value[..., :, 0:1],
    )


def exchange(value):
    last_row, first_row, last_col, first_col = edges(value)
    return (
        shift(last_row, "gx", 1),
        shift(first_row, "gx", -1),
        shift(last_col, "gy", 1),
        shift(first_col, "gy", -1),
    )


def shards(
    adjoint_in, u_east, u_north, diffusivity, wet_mask, dest_tile, src_row, dst_row, area_weight
):
    adjoint = adjoint_in[0]
    fields, levels, rows_x, cols_y = adjoint.shape
    sections = lax.axis_size("comp")
    tiles_x = lax.axis_size("gx")
    tiles_y = lax.axis_size("gy")
    tiles = tiles_x * tiles_y
    east = u_east[0]
    north = u_north[0]
    coeffs = diffusivity[0]
    wet = wet_mask[0].astype(jnp.float32)

    last_row, first_row, last_col, first_col = edges(adjoint)
    e_last, e_first, _, _ = edges(east)
    _, _, n_last, n_first = edges(north)
    start_halos = (
        shift(jnp.concatenate([last_row, e_last[None]], 0), "gx", 1),
        shift(jnp.concatenate([first_row, e_first[None]], 0), "gx", -1),
        shift(jnp.concatenate([last_col, n_last[None]], 0), "gy", 1),
        shift(jnp.concatenate([first_col, n_first[None]], 0), "gy", -1),
    )

    targets = dest_tile[0, 0, 0, :, 0]
    sources = src_row[0, 0, 0]
    landing = dst_row[0, 0, 0]
    weights = area_weight[0, 0, 0]
    count = targets.shape[0]
    surface_rows = jnp.transpose(adjoint[:, 0], (1, 0, 2)).reshape(rows_x, fields * cols_y)
    pick_table = (sources[:, None] == jnp.arange(rows_x, dtype=jnp.int32)[None, :]).astype(
        jnp.float32
    )
    payload = jnp.dot(
        pick_table,
        surface_rows,
        precision=lax.Precision.HIGHEST,
        preferred_element_type=jnp.float32,
    )
    payload = (payload.reshape(count, fields, cols_y) * weights[:, None, :]).reshape(
        count, fields * cols_y
    )
    tag = jnp.broadcast_to((landing + 1).astype(jnp.float32)[:, None], (count, cols_y))
    tagged = jnp.concatenate([payload, tag], axis=1)
    order_ids = jnp.arange(count, dtype=jnp.int32)
    earlier = (targets[:, None] == targets[None, :]) & (order_ids[None, :] < order_ids[:, None])
    rank_in = jnp.sum(earlier.astype(jnp.int32), axis=1)
    slot_ids = targets * CAP + rank_in
    placing = slot_ids[:, None] == jnp.arange(tiles * CAP, dtype=jnp.int32)[None, :]
    send_data = jnp.dot(
        placing.astype(jnp.float32).T,
        tagged,
        precision=lax.Precision.HIGHEST,
        preferred_element_type=jnp.float32,
    )
    width = (fields + 1) * cols_y
    got = lax.all_to_all(
        send_data.reshape(tiles, CAP, width), ("gx", "gy"), split_axis=0, concat_axis=0, tiled=True
    ).reshape(tiles * CAP, width)
    got_rows = got[:, fields * cols_y]
    row_table = (
        got_rows[None, :] == (jnp.arange(rows_x, dtype=jnp.int32) + 1).astype(jnp.float32)[:, None]
    ).astype(jnp.float32)
    increment = jnp.dot(
        row_table,
        got[:, : fields * cols_y],
        precision=lax.Precision.HIGHEST,
        preferred_element_type=jnp.float32,
    )
    increment = jnp.transpose(increment.reshape(rows_x, fields, cols_y), (1, 0, 2))

    def linear(c, x, y):
        return (c * tiles_x + x) * tiles_y + y

    def cross(block, dx, dy):
        route = []
        for c in range(sections):
            for x in range(tiles_x):
                for y in range(tiles_y):
                    if 0 <= x + dx < tiles_x and 0 <= y + dy < tiles_y:
                        route.append((linear(c, x, y), linear(sections - 1 - c, x + dx, y + dy)))
        return lax.ppermute(block, ("comp", "gx", "gy"), route)

    i_last_row, i_first_row, i_last_col, i_first_col = edges(increment)
    inc = (
        cross(increment, 0, 0),
        cross(i_last_row, 1, 0),
        cross(i_first_row, -1, 0),
        cross(i_last_col, 0, 1),
        cross(i_first_col, 0, -1),
    )

    middle = run_step(adjoint, start_halos, start_halos, east, north, coeffs, wet, inc)
    step_halos = exchange(middle)
    result = run_step(middle, step_halos, start_halos, east, north, coeffs, wet)
    return result[None]


def solution(mesh):
    placed = (
        P("comp", None, None, "gx", "gy"),
        P("comp", None, "gx", "gy"),
        P("comp", None, "gx", "gy"),
        P("comp", None, None, "gx", "gy"),
        P("comp", "gx", "gy"),
        P("comp", "gx", "gy", None, None),
        P("comp", "gx", "gy", None),
        P("comp", "gx", "gy", None),
        P("comp", "gx", "gy", None, None),
    )
    return jax.shard_map(
        shards,
        mesh=mesh,
        in_specs=placed,
        out_specs=P("comp", None, None, "gx", "gy"),
        check_vma=False,
    )
```

```python
import jax
import jax.numpy as jnp
from jax import lax
from jax.experimental import pallas as pl
from jax.experimental.pallas import tpu as pltpu
from jax.sharding import PartitionSpec as P

CAP = 4


diffusion = 0.2


def shift(block, axis, step):
    count = lax.axis_size(axis)
    route = [(i, i + step) for i in range(count) if 0 <= i + step < count]
    return lax.ppermute(block, axis, route)


def step_kernel(fields, levels, rows, cols, coupled, emit):
    planes = fields * levels

    def kernel(*refs):
        refs = list(refs)
        a_ref, up_ref, dn_ref, lf_ref, rt_ref, cu_ref, cd_ref, cl_ref, cr_ref = refs[:9]
        ue_ref, un_ref, k_ref, wet_ref = refs[9:13]
        refs = refs[13:]
        if coupled:
            inc_ref = refs.pop(0)
        out_ref = refs.pop(0)
        if emit:
            eu_ref, ed_ref, el_ref, er_ref = refs[:4]
            refs = refs[4:]
        c_ref = refs[0]
        row = lax.broadcasted_iota(jnp.int32, (rows, cols), 0)
        col = lax.broadcasted_iota(jnp.int32, (rows, cols), 1)
        top = row == 0
        bottom = row == rows - 1
        left = col == 0
        right = col == cols - 1
        cprev = [None] * fields
        dprev = [None] * fields
        for l in range(levels):
            ue = ue_ref[l]
            un = un_ref[l]
            ci = planes + l
            ue_m = jnp.where(top, cu_ref[pl.ds(ci, 1), :], pltpu.roll(ue, 1, 0))
            ue_p = jnp.where(bottom, cd_ref[pl.ds(ci, 1), :], pltpu.roll(ue, rows - 1, 0))
            un_m = jnp.where(left, cl_ref[:, pl.ds(ci, 1)], pltpu.roll(un, 1, 1))
            un_p = jnp.where(right, cr_ref[:, pl.ds(ci, 1)], pltpu.roll(un, cols - 1, 1))
            for f in range(fields):
                k = f * levels + l
                a = a_ref[f, l]
                if coupled and l == 0:
                    a = a + inc_ref[f]
                a_im = jnp.where(top, up_ref[pl.ds(k, 1), :], pltpu.roll(a, 1, 0))
                a_ip = jnp.where(bottom, dn_ref[pl.ds(k, 1), :], pltpu.roll(a, rows - 1, 0))
                a_jm = jnp.where(left, lf_ref[:, pl.ds(k, 1)], pltpu.roll(a, 1, 1))
                a_jp = jnp.where(right, rt_ref[:, pl.ds(k, 1)], pltpu.roll(a, cols - 1, 1))
                laplace = a_ip + a_im + a_jp + a_jm - 4.0 * a
                advect = 0.5 * (ue_m * a_im - ue_p * a_ip) + 0.5 * (un_m * a_jm - un_p * a_jp)
                h = a + diffusion * laplace + advect
                if l < levels - 1:
                    kd = k_ref[f, l]
                    diagonal = 1.0 + kd
                else:
                    diagonal = 1.0
                if l > 0:
                    kp = k_ref[f, l - 1]
                    divisor = diagonal + kp + kp * cprev[f]
                    numerator = h + kp * dprev[f]
                else:
                    divisor = diagonal
                    numerator = h
                if l < levels - 1:
                    cprev[f] = -kd / divisor
                    c_ref[f, l] = cprev[f]
                dprev[f] = numerator / divisor
                out_ref[f, l] = dprev[f]
        wet = wet_ref[...]
        if emit:
            sub = lax.broadcasted_iota(jnp.int32, (8, cols), 0)
            lane = lax.broadcasted_iota(jnp.int32, (rows, planes), 1)
            last_cols = jnp.zeros((rows, planes), jnp.float32)
            first_cols = jnp.zeros((rows, planes), jnp.float32)
            last_rows = jnp.zeros((8, cols), jnp.float32)
            first_rows = jnp.zeros((8, cols), jnp.float32)
        for f in range(fields):
            r = dprev[f]
            for l in range(levels - 1, -1, -1):
                if l < levels - 1:
                    r = out_ref[f, l] - c_ref[f, l] * r
                v = r * wet
                out_ref[f, l] = v
                if emit:
                    k = f * levels + l
                    last_rows = jnp.where(sub == k % 8, v[rows - 1 : rows, :], last_rows)
                    first_rows = jnp.where(sub == k % 8, v[0:1, :], first_rows)
                    last_cols = jnp.where(lane == k, v[:, cols - 1 : cols], last_cols)
                    first_cols = jnp.where(lane == k, v[:, 0:1], first_cols)
                    if k % 8 == 0:
                        eu_ref[pl.ds(k, 8), :] = last_rows
                        ed_ref[pl.ds(k, 8), :] = first_rows
        if emit:
            el_ref[...] = last_cols
            er_ref[...] = first_cols

    return kernel


def run_step(a, halos, coef_halos, ue, un, coeffs, wet, inc=None, emit=False):
    fields, levels, rows, cols = a.shape
    planes = fields * levels
    coupled = inc is not None
    operands = [a, *halos, *coef_halos, ue, un, coeffs, wet]
    if coupled:
        operands.append(inc)
    shapes = [jax.ShapeDtypeStruct(a.shape, jnp.float32)]
    if emit:
        shapes += [jax.ShapeDtypeStruct((planes, cols), jnp.float32)] * 2
        shapes += [jax.ShapeDtypeStruct((rows, planes), jnp.float32)] * 2
    return pl.pallas_call(
        step_kernel(fields, levels, rows, cols, coupled, emit),
        out_shape=shapes,
        scratch_shapes=[pltpu.VMEM(a.shape, jnp.float32)],
    )(*operands)


def shards(
    adjoint_in, u_east, u_north, diffusivity, wet_mask, dest_tile, src_row, dst_row, area_weight
):
    adjoint = adjoint_in[0]
    fields, levels, rows_x, cols_y = adjoint.shape
    planes = fields * levels
    sections = lax.axis_size("comp")
    tiles_x = lax.axis_size("gx")
    tiles_y = lax.axis_size("gy")
    tiles = tiles_x * tiles_y
    section = lax.axis_index("comp")
    east = u_east[0]
    north = u_north[0]
    coeffs = diffusivity[0]
    wet = wet_mask[0].astype(jnp.float32)

    targets = dest_tile[0, 0, 0, :, 0]
    sources = src_row[0, 0, 0]
    landing = dst_row[0, 0, 0]
    weights = area_weight[0, 0, 0]
    count = targets.shape[0]
    surface_rows = jnp.transpose(adjoint[:, 0], (1, 0, 2)).reshape(rows_x, fields * cols_y)
    pick_table = (sources[:, None] == jnp.arange(rows_x, dtype=jnp.int32)[None, :]).astype(
        jnp.float32
    )
    payload = jnp.dot(
        pick_table,
        surface_rows,
        precision=lax.Precision.HIGHEST,
        preferred_element_type=jnp.float32,
    )
    payload = (payload.reshape(count, fields, cols_y) * weights[:, None, :]).reshape(
        count, fields * cols_y
    )
    tag = jnp.broadcast_to((landing + 1).astype(jnp.float32)[:, None], (count, cols_y))
    tagged = jnp.concatenate([payload, tag], axis=1)
    order_ids = jnp.arange(count, dtype=jnp.int32)
    earlier = (targets[:, None] == targets[None, :]) & (order_ids[None, :] < order_ids[:, None])
    rank_in = jnp.sum(earlier.astype(jnp.int32), axis=1)
    slot_ids = ((sections - 1 - section) * tiles + targets) * CAP + rank_in
    placing = slot_ids[:, None] == jnp.arange(sections * tiles * CAP, dtype=jnp.int32)[None, :]
    send_data = jnp.dot(
        placing.astype(jnp.float32).T,
        tagged,
        precision=lax.Precision.HIGHEST,
        preferred_element_type=jnp.float32,
    )
    width = (fields + 1) * cols_y
    got = lax.all_to_all(
        send_data.reshape(sections * tiles, CAP, width),
        ("comp", "gx", "gy"),
        split_axis=0,
        concat_axis=0,
        tiled=True,
    ).reshape(sections * tiles * CAP, width)
    got_rows = got[:, fields * cols_y]
    row_table = (
        got_rows[None, :] == (jnp.arange(rows_x, dtype=jnp.int32) + 1).astype(jnp.float32)[:, None]
    ).astype(jnp.float32)
    increment = jnp.dot(
        row_table,
        got[:, : fields * cols_y],
        precision=lax.Precision.HIGHEST,
        preferred_element_type=jnp.float32,
    )
    increment = jnp.transpose(increment.reshape(rows_x, fields, cols_y), (1, 0, 2))

    def row_edge(index):
        field_rows = adjoint[:, :, index, :].at[:, 0].add(increment[:, index, :])
        return jnp.concatenate([field_rows.reshape(planes, cols_y), east[:, index, :]], 0)

    def col_edge(index):
        field_cols = adjoint[:, :, :, index].at[:, 0].add(increment[:, :, index])
        field_cols = jnp.transpose(field_cols, (2, 0, 1)).reshape(rows_x, planes)
        return jnp.concatenate([field_cols, north[:, :, index].T], 1)

    halos = (
        shift(row_edge(rows_x - 1), "gx", 1),
        shift(row_edge(0), "gx", -1),
        shift(col_edge(cols_y - 1), "gy", 1),
        shift(col_edge(0), "gy", -1),
    )

    middle, last_rows, first_rows, last_cols, first_cols = run_step(
        adjoint, halos, halos, east, north, coeffs, wet, inc=increment, emit=True
    )
    step_halos = (
        shift(last_rows, "gx", 1),
        shift(first_rows, "gx", -1),
        shift(last_cols, "gy", 1),
        shift(first_cols, "gy", -1),
    )
    (result,) = run_step(middle, step_halos, halos, east, north, coeffs, wet)
    return result[None]


def solution(mesh):
    placed = (
        P("comp", None, None, "gx", "gy"),
        P("comp", None, "gx", "gy"),
        P("comp", None, "gx", "gy"),
        P("comp", None, None, "gx", "gy"),
        P("comp", "gx", "gy"),
        P("comp", "gx", "gy", None, None),
        P("comp", "gx", "gy", None),
        P("comp", "gx", "gy", None),
        P("comp", "gx", "gy", None, None),
    )
    return jax.shard_map(
        shards,
        mesh=mesh,
        in_specs=placed,
        out_specs=P("comp", None, None, "gx", "gy"),
        check_vma=False,
    )
```

```python
import jax
import jax.numpy as jnp
from jax import lax
from jax.experimental import pallas as pl
from jax.experimental.pallas import tpu as pltpu
from jax.sharding import PartitionSpec as P

CAP = 4


diffusion = 0.2


def shift(block, axis, step):
    count = lax.axis_size(axis)
    route = [(i, i + step) for i in range(count) if 0 <= i + step < count]
    return lax.ppermute(block, axis, route)


def step_kernel(fields, levels, rows, cols, coupled, emit):
    planes = fields * levels

    def kernel(*refs):
        refs = list(refs)
        a_ref, up_ref, dn_ref, lf_ref, rt_ref, cu_ref, cd_ref, cl_ref, cr_ref = refs[:9]
        ue_ref, un_ref, k_ref, wet_ref = refs[9:13]
        refs = refs[13:]
        if coupled:
            inc_ref = refs.pop(0)
            ic_ref = refs.pop(0)
        out_ref = refs.pop(0)
        if emit:
            eu_ref, ed_ref, el_ref, er_ref = refs[:4]
            refs = refs[4:]
        c_ref = refs[0]
        row = lax.broadcasted_iota(jnp.int32, (rows, cols), 0)
        col = lax.broadcasted_iota(jnp.int32, (rows, cols), 1)
        top = row == 0
        bottom = row == rows - 1
        left = col == 0
        right = col == cols - 1
        cprev = [None] * fields
        dprev = [None] * fields
        for l in range(levels):
            ue = ue_ref[l]
            un = un_ref[l]
            ci = planes + l
            ue_m = jnp.where(top, cu_ref[pl.ds(ci, 1), :], pltpu.roll(ue, 1, 0))
            ue_p = jnp.where(bottom, cd_ref[pl.ds(ci, 1), :], pltpu.roll(ue, rows - 1, 0))
            un_m = jnp.where(left, cl_ref[:, pl.ds(ci, 1)], pltpu.roll(un, 1, 1))
            un_p = jnp.where(right, cr_ref[:, pl.ds(ci, 1)], pltpu.roll(un, cols - 1, 1))
            for f in range(fields):
                k = f * levels + l
                a = a_ref[f, l]
                up = up_ref[pl.ds(k, 1), :]
                dn = dn_ref[pl.ds(k, 1), :]
                lf = lf_ref[:, pl.ds(k, 1)]
                rt = rt_ref[:, pl.ds(k, 1)]
                if coupled and l == 0:
                    lanes = pl.ds(f * cols, cols)
                    a = a + inc_ref[pl.ds(0, rows), lanes]
                    up = up + inc_ref[pl.ds(rows, 1), lanes]
                    dn = dn + inc_ref[pl.ds(rows + 1, 1), lanes]
                    lf = lf + ic_ref[:, pl.ds(f, 1)]
                    rt = rt + ic_ref[:, pl.ds(fields + f, 1)]
                a_im = jnp.where(top, up, pltpu.roll(a, 1, 0))
                a_ip = jnp.where(bottom, dn, pltpu.roll(a, rows - 1, 0))
                a_jm = jnp.where(left, lf, pltpu.roll(a, 1, 1))
                a_jp = jnp.where(right, rt, pltpu.roll(a, cols - 1, 1))
                laplace = a_ip + a_im + a_jp + a_jm - 4.0 * a
                advect = 0.5 * (ue_m * a_im - ue_p * a_ip) + 0.5 * (un_m * a_jm - un_p * a_jp)
                h = a + diffusion * laplace + advect
                if l < levels - 1:
                    kd = k_ref[f, l]
                    diagonal = 1.0 + kd
                else:
                    diagonal = 1.0
                if l > 0:
                    kp = k_ref[f, l - 1]
                    divisor = diagonal + kp + kp * cprev[f]
                    numerator = h + kp * dprev[f]
                else:
                    divisor = diagonal
                    numerator = h
                if l < levels - 1:
                    cprev[f] = -kd / divisor
                    c_ref[f, l] = cprev[f]
                dprev[f] = numerator / divisor
                out_ref[f, l] = dprev[f]
        wet = wet_ref[...]
        if emit:
            sub = lax.broadcasted_iota(jnp.int32, (8, cols), 0)
            lane = lax.broadcasted_iota(jnp.int32, (rows, planes), 1)
            last_cols = jnp.zeros((rows, planes), jnp.float32)
            first_cols = jnp.zeros((rows, planes), jnp.float32)
            last_rows = jnp.zeros((8, cols), jnp.float32)
            first_rows = jnp.zeros((8, cols), jnp.float32)
        for f in range(fields):
            r = dprev[f]
            for l in range(levels - 1, -1, -1):
                if l < levels - 1:
                    r = out_ref[f, l] - c_ref[f, l] * r
                v = r * wet
                out_ref[f, l] = v
                if emit:
                    k = f * levels + l
                    last_rows = jnp.where(sub == k % 8, v[rows - 1 : rows, :], last_rows)
                    first_rows = jnp.where(sub == k % 8, v[0:1, :], first_rows)
                    last_cols = jnp.where(lane == k, v[:, cols - 1 : cols], last_cols)
                    first_cols = jnp.where(lane == k, v[:, 0:1], first_cols)
                    if k % 8 == 0:
                        eu_ref[pl.ds(k, 8), :] = last_rows
                        ed_ref[pl.ds(k, 8), :] = first_rows
        if emit:
            el_ref[...] = last_cols
            er_ref[...] = first_cols

    return kernel


def run_step(a, halos, coef_halos, ue, un, coeffs, wet, inc=None, emit=False):
    fields, levels, rows, cols = a.shape
    planes = fields * levels
    coupled = inc is not None
    operands = [a, *halos, *coef_halos, ue, un, coeffs, wet]
    if coupled:
        operands += list(inc)
    shapes = [jax.ShapeDtypeStruct(a.shape, jnp.float32)]
    if emit:
        shapes += [jax.ShapeDtypeStruct((planes, cols), jnp.float32)] * 2
        shapes += [jax.ShapeDtypeStruct((rows, planes), jnp.float32)] * 2
    return pl.pallas_call(
        step_kernel(fields, levels, rows, cols, coupled, emit),
        out_shape=shapes,
        scratch_shapes=[pltpu.VMEM(a.shape, jnp.float32)],
    )(*operands)


def shards(
    adjoint_in, u_east, u_north, diffusivity, wet_mask, dest_tile, src_row, dst_row, area_weight
):
    adjoint = adjoint_in[0]
    fields, levels, rows_x, cols_y = adjoint.shape
    planes = fields * levels
    sections = lax.axis_size("comp")
    tiles_x = lax.axis_size("gx")
    tiles_y = lax.axis_size("gy")
    tiles = tiles_x * tiles_y
    section = lax.axis_index("comp")
    east = u_east[0]
    north = u_north[0]
    coeffs = diffusivity[0]
    wet = wet_mask[0].astype(jnp.float32)

    def row_edge(index):
        field_rows = adjoint[:, :, index, :].reshape(planes, cols_y)
        return jnp.concatenate([field_rows, east[:, index, :]], 0)

    def col_edge(index):
        field_cols = jnp.transpose(adjoint[:, :, :, index], (2, 0, 1)).reshape(rows_x, planes)
        return jnp.concatenate([field_cols, north[:, :, index].T], 1)

    halos = (
        shift(row_edge(rows_x - 1), "gx", 1),
        shift(row_edge(0), "gx", -1),
        shift(col_edge(cols_y - 1), "gy", 1),
        shift(col_edge(0), "gy", -1),
    )

    targets = dest_tile[0, 0, 0, :, 0]
    sources = src_row[0, 0, 0]
    landing = dst_row[0, 0, 0]
    weights = area_weight[0, 0, 0]
    count = targets.shape[0]
    surface_rows = jnp.transpose(adjoint[:, 0], (1, 0, 2)).reshape(rows_x, fields * cols_y)
    pick_table = (sources[:, None] == jnp.arange(rows_x, dtype=jnp.int32)[None, :]).astype(
        jnp.float32
    )
    payload = jnp.dot(
        pick_table,
        surface_rows,
        precision=lax.Precision.HIGHEST,
        preferred_element_type=jnp.float32,
    )
    payload = (payload.reshape(count, fields, cols_y) * weights[:, None, :]).reshape(
        count, fields * cols_y
    )
    keys = targets * rows_x + landing
    placing = (
        keys[None, :] == jnp.arange(tiles * rows_x, dtype=jnp.int32)[:, None]
    ).astype(jnp.float32)
    summed = jnp.dot(
        placing, payload, precision=lax.Precision.HIGHEST, preferred_element_type=jnp.float32
    ).reshape(tiles_x, tiles_y, rows_x, fields, cols_y)
    zero_x = jnp.zeros((1, tiles_y, fields, cols_y), jnp.float32)
    up_rows = jnp.concatenate([zero_x, summed[:-1, :, rows_x - 1]], 0)
    dn_rows = jnp.concatenate([summed[1:, :, 0], zero_x], 0)
    zero_y = jnp.zeros((tiles_x, 1, rows_x, fields), jnp.float32)
    lf_cols = jnp.concatenate([zero_y, summed[:, :-1, :, :, cols_y - 1]], 1)
    rt_cols = jnp.concatenate([summed[:, 1:, :, :, 0], zero_y], 1)
    side = jnp.concatenate([lf_cols, rt_cols], 3).reshape(tiles_x, tiles_y, 2 * rows_x * fields)
    side = jnp.pad(side, ((0, 0), (0, 0), (0, fields * cols_y - 2 * rows_x * fields)))
    depth = rows_x + 3
    chunks = jnp.concatenate(
        [
            summed.reshape(tiles, rows_x, fields * cols_y),
            up_rows.reshape(tiles, 1, fields * cols_y),
            dn_rows.reshape(tiles, 1, fields * cols_y),
            side.reshape(tiles, 1, fields * cols_y),
        ],
        1,
    )
    send_data = lax.dynamic_update_slice(
        jnp.zeros((sections * tiles, depth, fields * cols_y), jnp.float32),
        chunks,
        ((sections - 1 - section) * tiles, 0, 0),
    )
    got = lax.all_to_all(
        send_data, ("comp", "gx", "gy"), split_axis=0, concat_axis=0, tiled=True
    )
    got = jnp.sum(got, axis=0)
    inc_cols = got[rows_x + 2, : 2 * rows_x * fields].reshape(rows_x, 2 * fields)
    inc = (got[: rows_x + 2], inc_cols)

    middle, last_rows, first_rows, last_cols, first_cols = run_step(
        adjoint, halos, halos, east, north, coeffs, wet, inc=inc, emit=True
    )
    step_halos = (
        shift(last_rows, "gx", 1),
        shift(first_rows, "gx", -1),
        shift(last_cols, "gy", 1),
        shift(first_cols, "gy", -1),
    )
    (result,) = run_step(middle, step_halos, halos, east, north, coeffs, wet)
    return result[None]


def solution(mesh):
    placed = (
        P("comp", None, None, "gx", "gy"),
        P("comp", None, "gx", "gy"),
        P("comp", None, "gx", "gy"),
        P("comp", None, None, "gx", "gy"),
        P("comp", "gx", "gy"),
        P("comp", "gx", "gy", None, None),
        P("comp", "gx", "gy", None),
        P("comp", "gx", "gy", None),
        P("comp", "gx", "gy", None, None),
    )
    return jax.shard_map(
        shards,
        mesh=mesh,
        in_specs=placed,
        out_specs=P("comp", None, None, "gx", "gy"),
        check_vma=False,
    )
```

```python
import jax
import jax.numpy as jnp
from jax import lax
from jax.experimental import pallas as pl
from jax.experimental.pallas import tpu as pltpu
from jax.sharding import PartitionSpec as P

CAP = 4


diffusion = 0.2


def shift(block, axis, step):
    count = lax.axis_size(axis)
    route = [(i, i + step) for i in range(count) if 0 <= i + step < count]
    return lax.ppermute(block, axis, route)


def step_kernel(fields, levels, rows, cols, coupled, emit):
    planes = fields * levels

    def kernel(*refs):
        refs = list(refs)
        a_ref, up_ref, dn_ref, lf_ref, rt_ref, cu_ref, cd_ref, cl_ref, cr_ref = refs[:9]
        ue_ref, un_ref, k_ref, wet_ref = refs[9:13]
        refs = refs[13:]
        if coupled:
            inc_ref = refs.pop(0)
            ic_ref = refs.pop(0)
        out_ref = refs.pop(0)
        if emit:
            eu_ref, ed_ref, el_ref, er_ref = refs[:4]
            refs = refs[4:]
        c_ref = refs[0]
        row = lax.broadcasted_iota(jnp.int32, (rows, cols), 0)
        col = lax.broadcasted_iota(jnp.int32, (rows, cols), 1)
        top = row == 0
        bottom = row == rows - 1
        left = col == 0
        right = col == cols - 1
        cprev = [None] * fields
        dprev = [None] * fields
        for l in range(levels):
            ue = ue_ref[l]
            un = un_ref[l]
            ci = planes + l
            ue_m = jnp.where(top, cu_ref[pl.ds(ci, 1), :], pltpu.roll(ue, 1, 0))
            ue_p = jnp.where(bottom, cd_ref[pl.ds(ci, 1), :], pltpu.roll(ue, rows - 1, 0))
            un_m = jnp.where(left, cl_ref[:, pl.ds(ci, 1)], pltpu.roll(un, 1, 1))
            un_p = jnp.where(right, cr_ref[:, pl.ds(ci, 1)], pltpu.roll(un, cols - 1, 1))
            for f in range(fields):
                k = f * levels + l
                a = a_ref[f, l]
                up = up_ref[pl.ds(k, 1), :]
                dn = dn_ref[pl.ds(k, 1), :]
                lf = lf_ref[:, pl.ds(k, 1)]
                rt = rt_ref[:, pl.ds(k, 1)]
                if coupled and l == 0:
                    lanes = pl.ds(f * cols, cols)
                    a = a + inc_ref[pl.ds(0, rows), lanes]
                    up = up + inc_ref[pl.ds(rows, 1), lanes]
                    dn = dn + inc_ref[pl.ds(rows + 1, 1), lanes]
                    lf = lf + ic_ref[:, pl.ds(f, 1)]
                    rt = rt + ic_ref[:, pl.ds(fields + f, 1)]
                a_im = jnp.where(top, up, pltpu.roll(a, 1, 0))
                a_ip = jnp.where(bottom, dn, pltpu.roll(a, rows - 1, 0))
                a_jm = jnp.where(left, lf, pltpu.roll(a, 1, 1))
                a_jp = jnp.where(right, rt, pltpu.roll(a, cols - 1, 1))
                laplace = a_ip + a_im + a_jp + a_jm - 4.0 * a
                advect = 0.5 * (ue_m * a_im - ue_p * a_ip) + 0.5 * (un_m * a_jm - un_p * a_jp)
                h = a + diffusion * laplace + advect
                if l < levels - 1:
                    kd = k_ref[f, l]
                    diagonal = 1.0 + kd
                else:
                    diagonal = 1.0
                if l > 0:
                    kp = k_ref[f, l - 1]
                    divisor = diagonal + kp + kp * cprev[f]
                    numerator = h + kp * dprev[f]
                else:
                    divisor = diagonal
                    numerator = h
                if l < levels - 1:
                    cprev[f] = -kd / divisor
                    c_ref[f, l] = cprev[f]
                dprev[f] = numerator / divisor
                out_ref[f, l] = dprev[f]
        wet = wet_ref[...]
        if emit:
            sub = lax.broadcasted_iota(jnp.int32, (8, cols), 0)
            lane = lax.broadcasted_iota(jnp.int32, (rows, planes), 1)
            last_cols = jnp.zeros((rows, planes), jnp.float32)
            first_cols = jnp.zeros((rows, planes), jnp.float32)
            last_rows = jnp.zeros((8, cols), jnp.float32)
            first_rows = jnp.zeros((8, cols), jnp.float32)
        for f in range(fields):
            r = dprev[f]
            for l in range(levels - 1, -1, -1):
                if l < levels - 1:
                    r = out_ref[f, l] - c_ref[f, l] * r
                v = r * wet
                out_ref[f, l] = v
                if emit:
                    k = f * levels + l
                    last_rows = jnp.where(sub == k % 8, v[rows - 1 : rows, :], last_rows)
                    first_rows = jnp.where(sub == k % 8, v[0:1, :], first_rows)
                    last_cols = jnp.where(lane == k, v[:, cols - 1 : cols], last_cols)
                    first_cols = jnp.where(lane == k, v[:, 0:1], first_cols)
                    if k % 8 == 0:
                        eu_ref[pl.ds(k, 8), :] = last_rows
                        ed_ref[pl.ds(k, 8), :] = first_rows
        if emit:
            el_ref[...] = last_cols
            er_ref[...] = first_cols

    return kernel


def run_step(a, halos, coef_halos, ue, un, coeffs, wet, inc=None, emit=False):
    fields, levels, rows, cols = a.shape
    planes = fields * levels
    coupled = inc is not None
    operands = [a, *halos, *coef_halos, ue, un, coeffs, wet]
    if coupled:
        operands += list(inc)
    shapes = [jax.ShapeDtypeStruct(a.shape, jnp.float32)]
    if emit:
        shapes += [jax.ShapeDtypeStruct((planes, cols), jnp.float32)] * 2
        shapes += [jax.ShapeDtypeStruct((rows, planes), jnp.float32)] * 2
    return pl.pallas_call(
        step_kernel(fields, levels, rows, cols, coupled, emit),
        out_shape=shapes,
        scratch_shapes=[pltpu.VMEM(a.shape, jnp.float32)],
    )(*operands)


def shards(
    adjoint_in, u_east, u_north, diffusivity, wet_mask, dest_tile, src_row, dst_row, area_weight
):
    adjoint = adjoint_in[0]
    fields, levels, rows_x, cols_y = adjoint.shape
    planes = fields * levels
    sections = lax.axis_size("comp")
    tiles_x = lax.axis_size("gx")
    tiles_y = lax.axis_size("gy")
    tiles = tiles_x * tiles_y
    section = lax.axis_index("comp")
    east = u_east[0]
    north = u_north[0]
    coeffs = diffusivity[0]
    wet = wet_mask[0].astype(jnp.float32)

    def row_edge(index):
        field_rows = adjoint[:, :, index, :].reshape(planes, cols_y)
        return jnp.concatenate([field_rows, east[:, index, :]], 0)

    def col_edge(index):
        field_cols = jnp.transpose(adjoint[:, :, :, index], (2, 0, 1)).reshape(rows_x, planes)
        return jnp.concatenate([field_cols, north[:, :, index].T], 1)

    halos = (
        shift(row_edge(rows_x - 1), "gx", 1),
        shift(row_edge(0), "gx", -1),
        shift(col_edge(cols_y - 1), "gy", 1),
        shift(col_edge(0), "gy", -1),
    )

    targets = dest_tile[0, 0, 0, :, 0]
    sources = src_row[0, 0, 0]
    landing = dst_row[0, 0, 0]
    weights = area_weight[0, 0, 0]
    count = targets.shape[0]
    surface_rows = jnp.transpose(adjoint[:, 0], (1, 0, 2)).reshape(rows_x, fields * cols_y)
    pick_table = (sources[:, None] == jnp.arange(rows_x, dtype=jnp.int32)[None, :]).astype(
        jnp.float32
    )
    payload = jnp.dot(
        pick_table,
        surface_rows,
        precision=lax.Precision.HIGHEST,
        preferred_element_type=jnp.float32,
    )
    payload = (payload.reshape(count, fields, cols_y) * weights[:, None, :]).reshape(
        count, fields * cols_y
    )
    keys = targets * rows_x + landing
    placing = (
        keys[None, :] == jnp.arange(tiles * rows_x, dtype=jnp.int32)[:, None]
    ).astype(jnp.float32)
    summed = jnp.dot(
        placing, payload, precision=lax.Precision.HIGHEST, preferred_element_type=jnp.float32
    ).reshape(tiles_x, tiles_y, rows_x, fields, cols_y)
    order_ids = jnp.arange(count, dtype=jnp.int32)
    earlier = (targets[:, None] == targets[None, :]) & (order_ids[None, :] < order_ids[:, None])
    rank_in = jnp.sum(earlier.astype(jnp.int32), axis=1)
    slot_ids = targets * CAP + rank_in
    slotting = (
        slot_ids[None, :] == jnp.arange(tiles * CAP, dtype=jnp.int32)[:, None]
    ).astype(jnp.float32)
    tagged = jnp.concatenate([payload, (landing + 1).astype(jnp.float32)[:, None]], 1)
    slots = jnp.dot(
        slotting, tagged, precision=lax.Precision.HIGHEST, preferred_element_type=jnp.float32
    )
    tags = slots[:, fields * cols_y].reshape(tiles_x, tiles_y, CAP)
    slots = slots[:, : fields * cols_y].reshape(tiles, CAP, fields * cols_y)
    zero_x = jnp.zeros((1, tiles_y, fields, cols_y), jnp.float32)
    up_rows = jnp.concatenate([zero_x, summed[:-1, :, rows_x - 1]], 0)
    dn_rows = jnp.concatenate([summed[1:, :, 0], zero_x], 0)
    zero_y = jnp.zeros((tiles_x, 1, rows_x, fields), jnp.float32)
    lf_cols = jnp.concatenate([zero_y, summed[:, :-1, :, :, cols_y - 1]], 1)
    rt_cols = jnp.concatenate([summed[:, 1:, :, :, 0], zero_y], 1)
    ring = 2 * rows_x * fields
    side = jnp.concatenate([lf_cols, rt_cols], 3).reshape(tiles_x, tiles_y, ring)
    side = jnp.concatenate([side, tags], 2)
    side = jnp.pad(side, ((0, 0), (0, 0), (0, fields * cols_y - ring - CAP)))
    send_data = jnp.concatenate(
        [
            slots,
            up_rows.reshape(tiles, 1, fields * cols_y),
            dn_rows.reshape(tiles, 1, fields * cols_y),
            side.reshape(tiles, 1, fields * cols_y),
        ],
        1,
    )
    got = lax.all_to_all(send_data, ("gx", "gy"), split_axis=0, concat_axis=0, tiled=True)
    got_tags = got[:, CAP + 2, ring : ring + CAP].reshape(tiles * CAP)
    row_table = (
        got_tags[None, :] == (jnp.arange(rows_x, dtype=jnp.int32) + 1).astype(jnp.float32)[:, None]
    ).astype(jnp.float32)
    increment = jnp.dot(
        row_table,
        got[:, :CAP].reshape(tiles * CAP, fields * cols_y),
        precision=lax.Precision.HIGHEST,
        preferred_element_type=jnp.float32,
    )
    edges_sum = jnp.sum(got[:, CAP:], axis=0)
    packed = jnp.concatenate([increment, edges_sum], 0)
    packed = lax.ppermute(packed, "comp", [(c, sections - 1 - c) for c in range(sections)])
    inc_cols = packed[rows_x + 2, :ring].reshape(rows_x, 2 * fields)
    inc = (packed[: rows_x + 2], inc_cols)

    middle, last_rows, first_rows, last_cols, first_cols = run_step(
        adjoint, halos, halos, east, north, coeffs, wet, inc=inc, emit=True
    )
    step_halos = (
        shift(last_rows, "gx", 1),
        shift(first_rows, "gx", -1),
        shift(last_cols, "gy", 1),
        shift(first_cols, "gy", -1),
    )
    (result,) = run_step(middle, step_halos, halos, east, north, coeffs, wet)
    return result[None]


def solution(mesh):
    placed = (
        P("comp", None, None, "gx", "gy"),
        P("comp", None, "gx", "gy"),
        P("comp", None, "gx", "gy"),
        P("comp", None, None, "gx", "gy"),
        P("comp", "gx", "gy"),
        P("comp", "gx", "gy", None, None),
        P("comp", "gx", "gy", None),
        P("comp", "gx", "gy", None),
        P("comp", "gx", "gy", None, None),
    )
    return jax.shard_map(
        shards,
        mesh=mesh,
        in_specs=placed,
        out_specs=P("comp", None, None, "gx", "gy"),
        check_vma=False,
    )
```

```python
import jax
import jax.numpy as jnp
from jax import lax
from jax.experimental import pallas as pl
from jax.experimental.pallas import tpu as pltpu
from jax.sharding import PartitionSpec as P

CAP = 4


diffusion = 0.2


def shift(block, axis, step):
    count = lax.axis_size(axis)
    route = [(i, i + step) for i in range(count) if 0 <= i + step < count]
    return lax.ppermute(block, axis, route)


def step_kernel(fields, levels, rows, cols, coupled, emit):
    planes = fields * levels

    def kernel(*refs):
        refs = list(refs)
        a_ref, up_ref, dn_ref, lf_ref, rt_ref, cu_ref, cd_ref, cl_ref, cr_ref = refs[:9]
        ue_ref, un_ref, k_ref, wet_ref = refs[9:13]
        refs = refs[13:]
        if coupled:
            inc_ref = refs.pop(0)
            ic_ref = refs.pop(0)
        out_ref = refs.pop(0)
        if emit:
            eu_ref, ed_ref, el_ref, er_ref = refs[:4]
            refs = refs[4:]
        c_ref = refs[0]
        row = lax.broadcasted_iota(jnp.int32, (rows, cols), 0)
        col = lax.broadcasted_iota(jnp.int32, (rows, cols), 1)
        top = row == 0
        bottom = row == rows - 1
        left = col == 0
        right = col == cols - 1
        cprev = [None] * fields
        dprev = [None] * fields
        for l in range(levels):
            ue = ue_ref[l]
            un = un_ref[l]
            ci = planes + l
            ue_m = jnp.where(top, cu_ref[pl.ds(ci, 1), :], pltpu.roll(ue, 1, 0))
            ue_p = jnp.where(bottom, cd_ref[pl.ds(ci, 1), :], pltpu.roll(ue, rows - 1, 0))
            un_m = jnp.where(left, cl_ref[:, pl.ds(ci, 1)], pltpu.roll(un, 1, 1))
            un_p = jnp.where(right, cr_ref[:, pl.ds(ci, 1)], pltpu.roll(un, cols - 1, 1))
            for f in range(fields):
                k = f * levels + l
                a = a_ref[f, l]
                up = up_ref[pl.ds(k, 1), :]
                dn = dn_ref[pl.ds(k, 1), :]
                lf = lf_ref[:, pl.ds(k, 1)]
                rt = rt_ref[:, pl.ds(k, 1)]
                if coupled and l == 0:
                    lanes = pl.ds(f * cols, cols)
                    a = a + inc_ref[pl.ds(0, rows), lanes]
                    up = up + inc_ref[pl.ds(rows, 1), lanes]
                    dn = dn + inc_ref[pl.ds(rows + 1, 1), lanes]
                    lf = lf + ic_ref[:, pl.ds(f, 1)]
                    rt = rt + ic_ref[:, pl.ds(fields + f, 1)]
                a_im = jnp.where(top, up, pltpu.roll(a, 1, 0))
                a_ip = jnp.where(bottom, dn, pltpu.roll(a, rows - 1, 0))
                a_jm = jnp.where(left, lf, pltpu.roll(a, 1, 1))
                a_jp = jnp.where(right, rt, pltpu.roll(a, cols - 1, 1))
                laplace = a_ip + a_im + a_jp + a_jm - 4.0 * a
                advect = 0.5 * (ue_m * a_im - ue_p * a_ip) + 0.5 * (un_m * a_jm - un_p * a_jp)
                h = a + diffusion * laplace + advect
                if l < levels - 1:
                    kd = k_ref[f, l]
                    diagonal = 1.0 + kd
                else:
                    diagonal = 1.0
                if l > 0:
                    kp = k_ref[f, l - 1]
                    divisor = diagonal + kp + kp * cprev[f]
                    numerator = h + kp * dprev[f]
                else:
                    divisor = diagonal
                    numerator = h
                if l < levels - 1:
                    cprev[f] = -kd / divisor
                    c_ref[f, l] = cprev[f]
                dprev[f] = numerator / divisor
                out_ref[f, l] = dprev[f]
        wet = wet_ref[...]
        if emit:
            sub = lax.broadcasted_iota(jnp.int32, (8, cols), 0)
            lane = lax.broadcasted_iota(jnp.int32, (rows, planes), 1)
            last_cols = jnp.zeros((rows, planes), jnp.float32)
            first_cols = jnp.zeros((rows, planes), jnp.float32)
            last_rows = jnp.zeros((8, cols), jnp.float32)
            first_rows = jnp.zeros((8, cols), jnp.float32)
        for f in range(fields):
            r = dprev[f]
            for l in range(levels - 1, -1, -1):
                if l < levels - 1:
                    r = out_ref[f, l] - c_ref[f, l] * r
                v = r * wet
                out_ref[f, l] = v
                if emit:
                    k = f * levels + l
                    last_rows = jnp.where(sub == k % 8, v[rows - 1 : rows, :], last_rows)
                    first_rows = jnp.where(sub == k % 8, v[0:1, :], first_rows)
                    last_cols = jnp.where(lane == k, v[:, cols - 1 : cols], last_cols)
                    first_cols = jnp.where(lane == k, v[:, 0:1], first_cols)
                    if k % 8 == 0:
                        eu_ref[pl.ds(k, 8), :] = last_rows
                        ed_ref[pl.ds(k, 8), :] = first_rows
        if emit:
            el_ref[...] = last_cols
            er_ref[...] = first_cols

    return kernel


def run_step(a, halos, coef_halos, ue, un, coeffs, wet, inc=None, emit=False):
    fields, levels, rows, cols = a.shape
    planes = fields * levels
    coupled = inc is not None
    operands = [a, *halos, *coef_halos, ue, un, coeffs, wet]
    if coupled:
        operands += list(inc)
    shapes = [jax.ShapeDtypeStruct(a.shape, jnp.float32)]
    if emit:
        shapes += [jax.ShapeDtypeStruct((planes, cols), jnp.float32)] * 2
        shapes += [jax.ShapeDtypeStruct((rows, planes), jnp.float32)] * 2
    return pl.pallas_call(
        step_kernel(fields, levels, rows, cols, coupled, emit),
        out_shape=shapes,
        scratch_shapes=[pltpu.VMEM(a.shape, jnp.float32)],
    )(*operands)


def shards(
    adjoint_in, u_east, u_north, diffusivity, wet_mask, dest_tile, src_row, dst_row, area_weight
):
    adjoint = adjoint_in[0]
    fields, levels, rows_x, cols_y = adjoint.shape
    planes = fields * levels
    sections = lax.axis_size("comp")
    tiles_x = lax.axis_size("gx")
    tiles_y = lax.axis_size("gy")
    tiles = tiles_x * tiles_y
    section = lax.axis_index("comp")
    east = u_east[0]
    north = u_north[0]
    coeffs = diffusivity[0]
    wet = wet_mask[0].astype(jnp.float32)

    def row_edge(index):
        field_rows = adjoint[:, :, index, :].reshape(planes, cols_y)
        return jnp.concatenate([field_rows, east[:, index, :]], 0)

    def col_edge(index):
        field_cols = jnp.transpose(adjoint[:, :, :, index], (2, 0, 1)).reshape(rows_x, planes)
        return jnp.concatenate([field_cols, north[:, :, index].T], 1)


    targets = dest_tile[0, 0, 0, :, 0]
    sources = src_row[0, 0, 0]
    landing = dst_row[0, 0, 0]
    weights = area_weight[0, 0, 0]
    count = targets.shape[0]
    surface_rows = jnp.transpose(adjoint[:, 0], (1, 0, 2)).reshape(rows_x, fields * cols_y)
    pick_table = (sources[:, None] == jnp.arange(rows_x, dtype=jnp.int32)[None, :]).astype(
        jnp.float32
    )
    payload = jnp.dot(
        pick_table,
        surface_rows,
        precision=lax.Precision.HIGHEST,
        preferred_element_type=jnp.float32,
    )
    payload = (payload.reshape(count, fields, cols_y) * weights[:, None, :]).reshape(
        count, fields * cols_y
    )
    keys = targets * rows_x + landing
    placing = (
        keys[None, :] == jnp.arange(tiles * rows_x, dtype=jnp.int32)[:, None]
    ).astype(jnp.float32)
    summed = jnp.dot(
        placing, payload, precision=lax.Precision.HIGHEST, preferred_element_type=jnp.float32
    ).reshape(tiles_x, tiles_y, rows_x, fields, cols_y)
    order_ids = jnp.arange(count, dtype=jnp.int32)
    earlier = (targets[:, None] == targets[None, :]) & (order_ids[None, :] < order_ids[:, None])
    rank_in = jnp.sum(earlier.astype(jnp.int32), axis=1)
    slot_ids = targets * CAP + rank_in
    slotting = (
        slot_ids[None, :] == jnp.arange(tiles * CAP, dtype=jnp.int32)[:, None]
    ).astype(jnp.float32)
    tagged = jnp.concatenate([payload, (landing + 1).astype(jnp.float32)[:, None]], 1)
    slots = jnp.dot(
        slotting, tagged, precision=lax.Precision.HIGHEST, preferred_element_type=jnp.float32
    )
    tags = slots[:, fields * cols_y].reshape(tiles_x, tiles_y, CAP)
    slots = slots[:, : fields * cols_y].reshape(tiles, CAP, fields * cols_y)
    zero_x = jnp.zeros((1, tiles_y, fields, cols_y), jnp.float32)
    up_rows = jnp.concatenate([zero_x, summed[:-1, :, rows_x - 1]], 0)
    dn_rows = jnp.concatenate([summed[1:, :, 0], zero_x], 0)
    zero_y = jnp.zeros((tiles_x, 1, rows_x, fields), jnp.float32)
    lf_cols = jnp.concatenate([zero_y, summed[:, :-1, :, :, cols_y - 1]], 1)
    rt_cols = jnp.concatenate([summed[:, 1:, :, :, 0], zero_y], 1)
    ring = 2 * rows_x * fields
    side = jnp.concatenate([lf_cols, rt_cols], 3).reshape(tiles_x, tiles_y, ring)
    side = jnp.concatenate([side, tags], 2)
    side = jnp.pad(side, ((0, 0), (0, 0), (0, fields * cols_y - ring - CAP)))
    send_data = jnp.concatenate(
        [
            slots,
            up_rows.reshape(tiles, 1, fields * cols_y),
            dn_rows.reshape(tiles, 1, fields * cols_y),
            side.reshape(tiles, 1, fields * cols_y),
        ],
        1,
    )
    send_data, *outgoing = lax.optimization_barrier(
        (send_data, row_edge(rows_x - 1), row_edge(0), col_edge(cols_y - 1), col_edge(0))
    )
    got = lax.all_to_all(send_data, ("gx", "gy"), split_axis=0, concat_axis=0, tiled=True)
    halos = (
        shift(outgoing[0], "gx", 1),
        shift(outgoing[1], "gx", -1),
        shift(outgoing[2], "gy", 1),
        shift(outgoing[3], "gy", -1),
    )
    got_tags = got[:, CAP + 2, ring : ring + CAP].reshape(tiles * CAP)
    row_table = (
        got_tags[None, :] == (jnp.arange(rows_x, dtype=jnp.int32) + 1).astype(jnp.float32)[:, None]
    ).astype(jnp.float32)
    increment = jnp.dot(
        row_table,
        got[:, :CAP].reshape(tiles * CAP, fields * cols_y),
        precision=lax.Precision.HIGHEST,
        preferred_element_type=jnp.float32,
    )
    edges_sum = jnp.sum(got[:, CAP:], axis=0)
    packed = jnp.concatenate([increment, edges_sum], 0)
    packed = lax.ppermute(packed, "comp", [(c, sections - 1 - c) for c in range(sections)])
    inc_cols = packed[rows_x + 2, :ring].reshape(rows_x, 2 * fields)
    inc = (packed[: rows_x + 2], inc_cols)

    middle, last_rows, first_rows, last_cols, first_cols = run_step(
        adjoint, halos, halos, east, north, coeffs, wet, inc=inc, emit=True
    )
    step_halos = (
        shift(last_rows, "gx", 1),
        shift(first_rows, "gx", -1),
        shift(last_cols, "gy", 1),
        shift(first_cols, "gy", -1),
    )
    (result,) = run_step(middle, step_halos, halos, east, north, coeffs, wet)
    return result[None]


def solution(mesh):
    placed = (
        P("comp", None, None, "gx", "gy"),
        P("comp", None, "gx", "gy"),
        P("comp", None, "gx", "gy"),
        P("comp", None, None, "gx", "gy"),
        P("comp", "gx", "gy"),
        P("comp", "gx", "gy", None, None),
        P("comp", "gx", "gy", None),
        P("comp", "gx", "gy", None),
        P("comp", "gx", "gy", None, None),
    )
    return jax.shard_map(
        shards,
        mesh=mesh,
        in_specs=placed,
        out_specs=P("comp", None, None, "gx", "gy"),
        check_vma=False,
    )
```

```python
import jax
import jax.numpy as jnp
from jax import lax
from jax.experimental import pallas as pl
from jax.experimental.pallas import tpu as pltpu
from jax.sharding import PartitionSpec as P

CAP = 4


diffusion = 0.2


def shift(block, axis, step):
    count = lax.axis_size(axis)
    route = [(i, i + step) for i in range(count) if 0 <= i + step < count]
    return lax.ppermute(block, axis, route)


def step_kernel(fields, levels, rows, cols, coupled, emit):
    planes = fields * levels

    def kernel(*refs):
        refs = list(refs)
        a_ref, up_ref, dn_ref, lf_ref, rt_ref, cu_ref, cd_ref, cl_ref, cr_ref = refs[:9]
        ue_ref, un_ref, k_ref, wet_ref = refs[9:13]
        refs = refs[13:]
        if coupled:
            inc_ref = refs.pop(0)
            ic_ref = refs.pop(0)
        out_ref = refs.pop(0)
        if emit:
            eu_ref, ed_ref, el_ref, er_ref = refs[:4]
            refs = refs[4:]
        c_ref = refs[0]
        row = lax.broadcasted_iota(jnp.int32, (rows, cols), 0)
        col = lax.broadcasted_iota(jnp.int32, (rows, cols), 1)
        top = row == 0
        bottom = row == rows - 1
        left = col == 0
        right = col == cols - 1
        cprev = [None] * fields
        dprev = [None] * fields
        for l in range(levels):
            ue = ue_ref[l]
            un = un_ref[l]
            ci = planes + l
            ue_m = jnp.where(top, cu_ref[pl.ds(ci, 1), :], pltpu.roll(ue, 1, 0))
            ue_p = jnp.where(bottom, cd_ref[pl.ds(ci, 1), :], pltpu.roll(ue, rows - 1, 0))
            un_m = jnp.where(left, cl_ref[:, pl.ds(ci, 1)], pltpu.roll(un, 1, 1))
            un_p = jnp.where(right, cr_ref[:, pl.ds(ci, 1)], pltpu.roll(un, cols - 1, 1))
            for f in range(fields):
                k = f * levels + l
                a = a_ref[f, l]
                up = up_ref[pl.ds(k, 1), :]
                dn = dn_ref[pl.ds(k, 1), :]
                lf = lf_ref[:, pl.ds(k, 1)]
                rt = rt_ref[:, pl.ds(k, 1)]
                if coupled and l == 0:
                    lanes = pl.ds(f * cols, cols)
                    a = a + inc_ref[pl.ds(0, rows), lanes]
                    up = up + inc_ref[pl.ds(rows, 1), lanes]
                    dn = dn + inc_ref[pl.ds(rows + 1, 1), lanes]
                    lf = lf + ic_ref[:, pl.ds(f, 1)]
                    rt = rt + ic_ref[:, pl.ds(fields + f, 1)]
                a_im = jnp.where(top, up, pltpu.roll(a, 1, 0))
                a_ip = jnp.where(bottom, dn, pltpu.roll(a, rows - 1, 0))
                a_jm = jnp.where(left, lf, pltpu.roll(a, 1, 1))
                a_jp = jnp.where(right, rt, pltpu.roll(a, cols - 1, 1))
                laplace = a_ip + a_im + a_jp + a_jm - 4.0 * a
                advect = 0.5 * (ue_m * a_im - ue_p * a_ip) + 0.5 * (un_m * a_jm - un_p * a_jp)
                h = a + diffusion * laplace + advect
                if l < levels - 1:
                    kd = k_ref[f, l]
                    diagonal = 1.0 + kd
                else:
                    diagonal = 1.0
                if l > 0:
                    kp = k_ref[f, l - 1]
                    divisor = diagonal + kp + kp * cprev[f]
                    numerator = h + kp * dprev[f]
                else:
                    divisor = diagonal
                    numerator = h
                inverse = 1.0 / divisor
                if l < levels - 1:
                    cprev[f] = -kd * inverse
                    c_ref[f, l] = cprev[f]
                dprev[f] = numerator * inverse
                out_ref[f, l] = dprev[f]
        wet = wet_ref[...].astype(jnp.float32)
        if emit:
            sub = lax.broadcasted_iota(jnp.int32, (8, cols), 0)
            lane = lax.broadcasted_iota(jnp.int32, (rows, planes), 1)
            last_cols = jnp.zeros((rows, planes), jnp.float32)
            first_cols = jnp.zeros((rows, planes), jnp.float32)
            last_rows = jnp.zeros((8, cols), jnp.float32)
            first_rows = jnp.zeros((8, cols), jnp.float32)
        for f in range(fields):
            r = dprev[f]
            for l in range(levels - 1, -1, -1):
                if l < levels - 1:
                    r = out_ref[f, l] - c_ref[f, l] * r
                v = r * wet
                out_ref[f, l] = v
                if emit:
                    k = f * levels + l
                    last_rows = jnp.where(sub == k % 8, v[rows - 1 : rows, :], last_rows)
                    first_rows = jnp.where(sub == k % 8, v[0:1, :], first_rows)
                    last_cols = jnp.where(lane == k, v[:, cols - 1 : cols], last_cols)
                    first_cols = jnp.where(lane == k, v[:, 0:1], first_cols)
                    if k % 8 == 0:
                        eu_ref[pl.ds(k, 8), :] = last_rows
                        ed_ref[pl.ds(k, 8), :] = first_rows
        if emit:
            el_ref[...] = last_cols
            er_ref[...] = first_cols

    return kernel


def run_step(a, halos, coef_halos, ue, un, coeffs, wet, inc=None, emit=False):
    fields, levels, rows, cols = a.shape
    planes = fields * levels
    coupled = inc is not None
    operands = [a, *halos, *coef_halos, ue, un, coeffs, wet]
    if coupled:
        operands += list(inc)
    shapes = [jax.ShapeDtypeStruct(a.shape, jnp.float32)]
    if emit:
        shapes += [jax.ShapeDtypeStruct((planes, cols), jnp.float32)] * 2
        shapes += [jax.ShapeDtypeStruct((rows, planes), jnp.float32)] * 2
    return pl.pallas_call(
        step_kernel(fields, levels, rows, cols, coupled, emit),
        out_shape=shapes,
        scratch_shapes=[pltpu.VMEM(a.shape, jnp.float32)],
    )(*operands)


def shards(
    adjoint_in, u_east, u_north, diffusivity, wet_mask, dest_tile, src_row, dst_row, area_weight
):
    adjoint = adjoint_in[0]
    fields, levels, rows_x, cols_y = adjoint.shape
    planes = fields * levels
    sections = lax.axis_size("comp")
    tiles_x = lax.axis_size("gx")
    tiles_y = lax.axis_size("gy")
    tiles = tiles_x * tiles_y
    section = lax.axis_index("comp")
    east = u_east[0]
    north = u_north[0]
    coeffs = diffusivity[0]
    wet = wet_mask[0]

    def row_edge(index):
        field_rows = adjoint[:, :, index, :].reshape(planes, cols_y)
        return jnp.concatenate([field_rows, east[:, index, :]], 0)

    def col_edge(index):
        field_cols = jnp.transpose(adjoint[:, :, :, index], (2, 0, 1)).reshape(rows_x, planes)
        return jnp.concatenate([field_cols, north[:, :, index].T], 1)


    targets = dest_tile[0, 0, 0, :, 0]
    sources = src_row[0, 0, 0]
    landing = dst_row[0, 0, 0]
    weights = area_weight[0, 0, 0]
    count = targets.shape[0]
    surface_rows = jnp.transpose(adjoint[:, 0], (1, 0, 2)).reshape(rows_x, fields * cols_y)
    pick_table = (sources[:, None] == jnp.arange(rows_x, dtype=jnp.int32)[None, :]).astype(
        jnp.float32
    )
    payload = jnp.dot(
        pick_table,
        surface_rows,
        precision=lax.Precision.HIGHEST,
        preferred_element_type=jnp.float32,
    )
    payload = (payload.reshape(count, fields, cols_y) * weights[:, None, :]).reshape(
        count, fields * cols_y
    )
    keys = targets * rows_x + landing
    placing = (
        keys[None, :] == jnp.arange(tiles * rows_x, dtype=jnp.int32)[:, None]
    ).astype(jnp.float32)
    summed = jnp.dot(
        placing, payload, precision=lax.Precision.HIGHEST, preferred_element_type=jnp.float32
    ).reshape(tiles_x, tiles_y, rows_x, fields, cols_y)
    order_ids = jnp.arange(count, dtype=jnp.int32)
    earlier = (targets[:, None] == targets[None, :]) & (order_ids[None, :] < order_ids[:, None])
    rank_in = jnp.sum(earlier.astype(jnp.int32), axis=1)
    slot_ids = targets * CAP + rank_in
    slotting = slot_ids[None, :] == jnp.arange(tiles * CAP, dtype=jnp.int32)[:, None]
    slots = jnp.dot(
        slotting.astype(jnp.float32),
        payload,
        precision=lax.Precision.HIGHEST,
        preferred_element_type=jnp.float32,
    ).reshape(tiles, CAP, fields * cols_y)
    tags = jnp.sum(slotting.astype(jnp.int32) * (landing + 1)[None, :], axis=1)
    tags = tags.astype(jnp.float32).reshape(tiles_x, tiles_y, CAP)
    zero_x = jnp.zeros((1, tiles_y, fields, cols_y), jnp.float32)
    up_rows = jnp.concatenate([zero_x, summed[:-1, :, rows_x - 1]], 0)
    dn_rows = jnp.concatenate([summed[1:, :, 0], zero_x], 0)
    zero_y = jnp.zeros((tiles_x, 1, rows_x, fields), jnp.float32)
    lf_cols = jnp.concatenate([zero_y, summed[:, :-1, :, :, cols_y - 1]], 1)
    rt_cols = jnp.concatenate([summed[:, 1:, :, :, 0], zero_y], 1)
    ring = 2 * rows_x * fields
    side = jnp.concatenate([lf_cols, rt_cols], 3).reshape(tiles_x, tiles_y, ring)
    side = jnp.concatenate([side, tags], 2)
    side = jnp.pad(side, ((0, 0), (0, 0), (0, fields * cols_y - ring - CAP)))
    send_data = jnp.concatenate(
        [
            slots,
            up_rows.reshape(tiles, 1, fields * cols_y),
            dn_rows.reshape(tiles, 1, fields * cols_y),
            side.reshape(tiles, 1, fields * cols_y),
        ],
        1,
    )
    send_data, *outgoing = lax.optimization_barrier(
        (send_data, row_edge(rows_x - 1), row_edge(0), col_edge(cols_y - 1), col_edge(0))
    )
    got = lax.all_to_all(send_data, ("gx", "gy"), split_axis=0, concat_axis=0, tiled=True)
    halos = (
        shift(outgoing[0], "gx", 1),
        shift(outgoing[1], "gx", -1),
        shift(outgoing[2], "gy", 1),
        shift(outgoing[3], "gy", -1),
    )
    got_tags = got[:, CAP + 2, ring : ring + CAP].reshape(tiles * CAP)
    row_table = (
        got_tags[None, :] == (jnp.arange(rows_x, dtype=jnp.int32) + 1).astype(jnp.float32)[:, None]
    ).astype(jnp.float32)
    increment = jnp.dot(
        row_table,
        got[:, :CAP].reshape(tiles * CAP, fields * cols_y),
        precision=lax.Precision.HIGHEST,
        preferred_element_type=jnp.float32,
    )
    edges_sum = jnp.sum(got[:, CAP:], axis=0)
    packed = jnp.concatenate([increment, edges_sum], 0)
    packed = lax.ppermute(packed, "comp", [(c, sections - 1 - c) for c in range(sections)])
    inc_cols = packed[rows_x + 2, :ring].reshape(rows_x, 2 * fields)
    inc = (packed[: rows_x + 2], inc_cols)

    middle, last_rows, first_rows, last_cols, first_cols = run_step(
        adjoint, halos, halos, east, north, coeffs, wet, inc=inc, emit=True
    )
    step_halos = (
        shift(last_rows, "gx", 1),
        shift(first_rows, "gx", -1),
        shift(last_cols, "gy", 1),
        shift(first_cols, "gy", -1),
    )
    (result,) = run_step(middle, step_halos, halos, east, north, coeffs, wet)
    return result[None]


def solution(mesh):
    placed = (
        P("comp", None, None, "gx", "gy"),
        P("comp", None, "gx", "gy"),
        P("comp", None, "gx", "gy"),
        P("comp", None, None, "gx", "gy"),
        P("comp", "gx", "gy"),
        P("comp", "gx", "gy", None, None),
        P("comp", "gx", "gy", None),
        P("comp", "gx", "gy", None),
        P("comp", "gx", "gy", None, None),
    )
    return jax.shard_map(
        shards,
        mesh=mesh,
        in_specs=placed,
        out_specs=P("comp", None, None, "gx", "gy"),
        check_vma=False,
    )
```

```python
import jax
import jax.numpy as jnp
from jax import lax
from jax.experimental import pallas as pl
from jax.experimental.pallas import tpu as pltpu
from jax.sharding import PartitionSpec as P

CAP = 4


diffusion = 0.2


def shift(block, axis, step):
    count = lax.axis_size(axis)
    route = [(i, i + step) for i in range(count) if 0 <= i + step < count]
    return lax.ppermute(block, axis, route)


def step_kernel(fields, levels, rows, cols, coupled, emit):
    planes = fields * levels

    def kernel(*refs):
        refs = list(refs)
        a_ref, up_ref, dn_ref, lf_ref, rt_ref, cu_ref, cd_ref, cl_ref, cr_ref = refs[:9]
        ue_ref, un_ref, k_ref, wet_ref = refs[9:13]
        refs = refs[13:]
        if coupled:
            inc_ref = refs.pop(0)
            ic_ref = refs.pop(0)
        out_ref = refs.pop(0)
        if emit:
            eu_ref, ed_ref, el_ref, er_ref = refs[:4]
            refs = refs[4:]
        c_ref = refs[0]
        row = lax.broadcasted_iota(jnp.int32, (rows, cols), 0)
        col = lax.broadcasted_iota(jnp.int32, (rows, cols), 1)
        top = row == 0
        bottom = row == rows - 1
        left = col == 0
        right = col == cols - 1
        cprev = [None] * fields
        dprev = [None] * fields
        for l in range(levels):
            ue = ue_ref[l]
            un = un_ref[l]
            ci = planes + l
            ue_m = jnp.where(top, cu_ref[pl.ds(ci, 1), :], pltpu.roll(ue, 1, 0))
            ue_p = jnp.where(bottom, cd_ref[pl.ds(ci, 1), :], pltpu.roll(ue, rows - 1, 0))
            un_m = jnp.where(left, cl_ref[:, pl.ds(ci, 1)], pltpu.roll(un, 1, 1))
            un_p = jnp.where(right, cr_ref[:, pl.ds(ci, 1)], pltpu.roll(un, cols - 1, 1))
            for f in range(fields):
                k = f * levels + l
                a = a_ref[f, l]
                up = up_ref[pl.ds(k, 1), :]
                dn = dn_ref[pl.ds(k, 1), :]
                lf = lf_ref[:, pl.ds(k, 1)]
                rt = rt_ref[:, pl.ds(k, 1)]
                if coupled and l == 0:
                    lanes = pl.ds(f * cols, cols)
                    a = a + inc_ref[pl.ds(0, rows), lanes]
                    up = up + inc_ref[pl.ds(rows, 1), lanes]
                    dn = dn + inc_ref[pl.ds(rows + 1, 1), lanes]
                    lf = lf + ic_ref[:, pl.ds(f, 1)]
                    rt = rt + ic_ref[:, pl.ds(fields + f, 1)]
                a_im = jnp.where(top, up, pltpu.roll(a, 1, 0))
                a_ip = jnp.where(bottom, dn, pltpu.roll(a, rows - 1, 0))
                a_jm = jnp.where(left, lf, pltpu.roll(a, 1, 1))
                a_jp = jnp.where(right, rt, pltpu.roll(a, cols - 1, 1))
                laplace = a_ip + a_im + a_jp + a_jm - 4.0 * a
                advect = 0.5 * (ue_m * a_im - ue_p * a_ip) + 0.5 * (un_m * a_jm - un_p * a_jp)
                h = a + diffusion * laplace + advect
                if l < levels - 1:
                    kd = k_ref[f, l]
                    diagonal = 1.0 + kd
                else:
                    diagonal = 1.0
                if l > 0:
                    kp = k_ref[f, l - 1]
                    divisor = diagonal + kp + kp * cprev[f]
                    numerator = h + kp * dprev[f]
                else:
                    divisor = diagonal
                    numerator = h
                if l < levels - 1:
                    cprev[f] = -kd / divisor
                    c_ref[f, l] = cprev[f]
                dprev[f] = numerator / divisor
                out_ref[f, l] = dprev[f]
        wet = wet_ref[...]
        if emit:
            sub = lax.broadcasted_iota(jnp.int32, (8, cols), 0)
            lane = lax.broadcasted_iota(jnp.int32, (rows, planes), 1)
            last_cols = jnp.zeros((rows, planes), jnp.float32)
            first_cols = jnp.zeros((rows, planes), jnp.float32)
            last_rows = jnp.zeros((8, cols), jnp.float32)
            first_rows = jnp.zeros((8, cols), jnp.float32)
        for f in range(fields):
            r = dprev[f]
            for l in range(levels - 1, -1, -1):
                if l < levels - 1:
                    r = out_ref[f, l] - c_ref[f, l] * r
                v = r * wet
                out_ref[f, l] = v
                if emit:
                    k = f * levels + l
                    last_rows = jnp.where(sub == k % 8, v[rows - 1 : rows, :], last_rows)
                    first_rows = jnp.where(sub == k % 8, v[0:1, :], first_rows)
                    last_cols = jnp.where(lane == k, v[:, cols - 1 : cols], last_cols)
                    first_cols = jnp.where(lane == k, v[:, 0:1], first_cols)
                    if k % 8 == 0:
                        eu_ref[pl.ds(k, 8), :] = last_rows
                        ed_ref[pl.ds(k, 8), :] = first_rows
        if emit:
            el_ref[...] = last_cols
            er_ref[...] = first_cols

    return kernel


def run_step(a, halos, coef_halos, ue, un, coeffs, wet, inc=None, emit=False):
    fields, levels, rows, cols = a.shape
    planes = fields * levels
    coupled = inc is not None
    operands = [a, *halos, *coef_halos, ue, un, coeffs, wet]
    if coupled:
        operands += list(inc)
    shapes = [jax.ShapeDtypeStruct(a.shape, jnp.float32)]
    if emit:
        shapes += [jax.ShapeDtypeStruct((planes, cols), jnp.float32)] * 2
        shapes += [jax.ShapeDtypeStruct((rows, planes), jnp.float32)] * 2
    return pl.pallas_call(
        step_kernel(fields, levels, rows, cols, coupled, emit),
        out_shape=shapes,
        scratch_shapes=[pltpu.VMEM(a.shape, jnp.float32)],
    )(*operands)


def shards(
    adjoint_in, u_east, u_north, diffusivity, wet_mask, dest_tile, src_row, dst_row, area_weight
):
    adjoint = adjoint_in[0]
    fields, levels, rows_x, cols_y = adjoint.shape
    planes = fields * levels
    sections = lax.axis_size("comp")
    tiles_x = lax.axis_size("gx")
    tiles_y = lax.axis_size("gy")
    tiles = tiles_x * tiles_y
    section = lax.axis_index("comp")
    east = u_east[0]
    north = u_north[0]
    coeffs = diffusivity[0]
    wet = wet_mask[0].astype(jnp.float32)

    def row_edge(index):
        field_rows = adjoint[:, :, index, :].reshape(planes, cols_y)
        return jnp.concatenate([field_rows, east[:, index, :]], 0)

    def col_edge(index):
        field_cols = jnp.transpose(adjoint[:, :, :, index], (2, 0, 1)).reshape(rows_x, planes)
        return jnp.concatenate([field_cols, north[:, :, index].T], 1)


    targets = dest_tile[0, 0, 0, :, 0]
    sources = src_row[0, 0, 0]
    landing = dst_row[0, 0, 0]
    weights = area_weight[0, 0, 0]
    count = targets.shape[0]
    surface_rows = jnp.transpose(adjoint[:, 0], (1, 0, 2)).reshape(rows_x, fields * cols_y)
    pick_table = (sources[:, None] == jnp.arange(rows_x, dtype=jnp.int32)[None, :]).astype(
        jnp.float32
    )
    payload = jnp.dot(
        pick_table,
        surface_rows,
        precision=lax.Precision.HIGHEST,
        preferred_element_type=jnp.float32,
    )
    payload = (payload.reshape(count, fields, cols_y) * weights[:, None, :]).reshape(
        count, fields * cols_y
    )
    keys = targets * rows_x + landing
    placing = (
        keys[None, :] == jnp.arange(tiles * rows_x, dtype=jnp.int32)[:, None]
    ).astype(jnp.float32)
    summed = jnp.dot(
        placing, payload, precision=lax.Precision.HIGHEST, preferred_element_type=jnp.float32
    ).reshape(tiles_x, tiles_y, rows_x, fields, cols_y)
    order_ids = jnp.arange(count, dtype=jnp.int32)
    earlier = (targets[:, None] == targets[None, :]) & (order_ids[None, :] < order_ids[:, None])
    rank_in = jnp.sum(earlier.astype(jnp.int32), axis=1)
    slot_ids = targets * CAP + rank_in
    slotting = slot_ids[None, :] == jnp.arange(tiles * CAP, dtype=jnp.int32)[:, None]
    slots = jnp.dot(
        slotting.astype(jnp.float32),
        payload,
        precision=lax.Precision.HIGHEST,
        preferred_element_type=jnp.float32,
    ).reshape(tiles, CAP, fields * cols_y)
    tags = jnp.sum(slotting.astype(jnp.int32) * (landing + 1)[None, :], axis=1)
    tags = tags.astype(jnp.float32).reshape(tiles_x, tiles_y, CAP)
    zero_x = jnp.zeros((1, tiles_y, fields, cols_y), jnp.float32)
    up_rows = jnp.concatenate([zero_x, summed[:-1, :, rows_x - 1]], 0)
    dn_rows = jnp.concatenate([summed[1:, :, 0], zero_x], 0)
    zero_y = jnp.zeros((tiles_x, 1, rows_x, fields), jnp.float32)
    lf_cols = jnp.concatenate([zero_y, summed[:, :-1, :, :, cols_y - 1]], 1)
    rt_cols = jnp.concatenate([summed[:, 1:, :, :, 0], zero_y], 1)
    ring = 2 * rows_x * fields
    side = jnp.concatenate([lf_cols, rt_cols], 3).reshape(tiles_x, tiles_y, ring)
    side = jnp.concatenate([side, tags], 2)
    side = jnp.pad(side, ((0, 0), (0, 0), (0, fields * cols_y - ring - CAP)))
    send_data = jnp.concatenate(
        [
            slots,
            up_rows.reshape(tiles, 1, fields * cols_y),
            dn_rows.reshape(tiles, 1, fields * cols_y),
            side.reshape(tiles, 1, fields * cols_y),
        ],
        1,
    )
    send_data, *outgoing = lax.optimization_barrier(
        (send_data, row_edge(rows_x - 1), row_edge(0), col_edge(cols_y - 1), col_edge(0))
    )
    got = lax.all_to_all(send_data, ("gx", "gy"), split_axis=0, concat_axis=0, tiled=True)
    halos = (
        shift(outgoing[0], "gx", 1),
        shift(outgoing[1], "gx", -1),
        shift(outgoing[2], "gy", 1),
        shift(outgoing[3], "gy", -1),
    )
    got_tags = got[:, CAP + 2, ring : ring + CAP].reshape(tiles * CAP)
    row_table = (
        got_tags[None, :] == (jnp.arange(rows_x, dtype=jnp.int32) + 1).astype(jnp.float32)[:, None]
    ).astype(jnp.float32)
    increment = jnp.dot(
        row_table,
        got[:, :CAP].reshape(tiles * CAP, fields * cols_y),
        precision=lax.Precision.HIGHEST,
        preferred_element_type=jnp.float32,
    )
    edges_sum = jnp.sum(got[:, CAP:], axis=0)
    packed = jnp.concatenate([increment, edges_sum], 0)
    packed = lax.ppermute(packed, "comp", [(c, sections - 1 - c) for c in range(sections)])
    inc_cols = packed[rows_x + 2, :ring].reshape(rows_x, 2 * fields)
    inc = (packed[: rows_x + 2], inc_cols)

    middle, last_rows, first_rows, last_cols, first_cols = run_step(
        adjoint, halos, halos, east, north, coeffs, wet, inc=inc, emit=True
    )
    step_halos = (
        shift(last_rows, "gx", 1),
        shift(first_rows, "gx", -1),
        shift(last_cols, "gy", 1),
        shift(first_cols, "gy", -1),
    )
    (result,) = run_step(middle, step_halos, halos, east, north, coeffs, wet)
    return result[None]


def solution(mesh):
    placed = (
        P("comp", None, None, "gx", "gy"),
        P("comp", None, "gx", "gy"),
        P("comp", None, "gx", "gy"),
        P("comp", None, None, "gx", "gy"),
        P("comp", "gx", "gy"),
        P("comp", "gx", "gy", None, None),
        P("comp", "gx", "gy", None),
        P("comp", "gx", "gy", None),
        P("comp", "gx", "gy", None, None),
    )
    return jax.shard_map(
        shards,
        mesh=mesh,
        in_specs=placed,
        out_specs=P("comp", None, None, "gx", "gy"),
        check_vma=False,
    )
```

```python
import jax
import jax.numpy as jnp
from jax import lax
from jax.experimental import pallas as pl
from jax.experimental.pallas import tpu as pltpu
from jax.sharding import PartitionSpec as P

CAP = 4


diffusion = 0.2


def shift(block, axis, step):
    count = lax.axis_size(axis)
    route = [(i, i + step) for i in range(count) if 0 <= i + step < count]
    return lax.ppermute(block, axis, route)


def both_ways(last, first, axis):
    count = lax.axis_size(axis)
    here = lax.axis_index(axis)
    target = lax.broadcasted_iota(jnp.int32, (count,) + (1,) * last.ndim, 0)
    send = jnp.where(target == here + 1, last[None], jnp.where(target == here - 1, first[None], 0.0))
    got = lax.all_to_all(send, axis, split_axis=0, concat_axis=0, tiled=True)
    before = lax.dynamic_index_in_dim(got, jnp.maximum(here - 1, 0), 0, keepdims=False)
    after = lax.dynamic_index_in_dim(got, jnp.minimum(here + 1, count - 1), 0, keepdims=False)
    return (
        jnp.where(here > 0, before, 0.0),
        jnp.where(here < count - 1, after, 0.0),
    )


def step_kernel(fields, levels, rows, cols, coupled, emit):
    planes = fields * levels

    def kernel(*refs):
        refs = list(refs)
        a_ref, up_ref, dn_ref, lf_ref, rt_ref, cu_ref, cd_ref, cl_ref, cr_ref = refs[:9]
        ue_ref, un_ref, k_ref, wet_ref = refs[9:13]
        refs = refs[13:]
        if coupled:
            inc_ref = refs.pop(0)
            ic_ref = refs.pop(0)
        out_ref = refs.pop(0)
        if emit:
            eu_ref, ed_ref, el_ref, er_ref = refs[:4]
            refs = refs[4:]
        c_ref = refs[0]
        row = lax.broadcasted_iota(jnp.int32, (rows, cols), 0)
        col = lax.broadcasted_iota(jnp.int32, (rows, cols), 1)
        top = row == 0
        bottom = row == rows - 1
        left = col == 0
        right = col == cols - 1
        cprev = [None] * fields
        dprev = [None] * fields
        for l in range(levels):
            ue = ue_ref[l]
            un = un_ref[l]
            ci = planes + l
            ue_m = jnp.where(top, cu_ref[pl.ds(ci, 1), :], pltpu.roll(ue, 1, 0))
            ue_p = jnp.where(bottom, cd_ref[pl.ds(ci, 1), :], pltpu.roll(ue, rows - 1, 0))
            un_m = jnp.where(left, cl_ref[:, pl.ds(ci, 1)], pltpu.roll(un, 1, 1))
            un_p = jnp.where(right, cr_ref[:, pl.ds(ci, 1)], pltpu.roll(un, cols - 1, 1))
            for f in range(fields):
                k = f * levels + l
                a = a_ref[f, l]
                up = up_ref[pl.ds(k, 1), :]
                dn = dn_ref[pl.ds(k, 1), :]
                lf = lf_ref[:, pl.ds(k, 1)]
                rt = rt_ref[:, pl.ds(k, 1)]
                if coupled and l == 0:
                    lanes = pl.ds(f * cols, cols)
                    a = a + inc_ref[pl.ds(0, rows), lanes]
                    up = up + inc_ref[pl.ds(rows, 1), lanes]
                    dn = dn + inc_ref[pl.ds(rows + 1, 1), lanes]
                    lf = lf + ic_ref[:, pl.ds(f, 1)]
                    rt = rt + ic_ref[:, pl.ds(fields + f, 1)]
                a_im = jnp.where(top, up, pltpu.roll(a, 1, 0))
                a_ip = jnp.where(bottom, dn, pltpu.roll(a, rows - 1, 0))
                a_jm = jnp.where(left, lf, pltpu.roll(a, 1, 1))
                a_jp = jnp.where(right, rt, pltpu.roll(a, cols - 1, 1))
                laplace = a_ip + a_im + a_jp + a_jm - 4.0 * a
                advect = 0.5 * (ue_m * a_im - ue_p * a_ip) + 0.5 * (un_m * a_jm - un_p * a_jp)
                h = a + diffusion * laplace + advect
                if l < levels - 1:
                    kd = k_ref[f, l]
                    diagonal = 1.0 + kd
                else:
                    diagonal = 1.0
                if l > 0:
                    kp = k_ref[f, l - 1]
                    divisor = diagonal + kp + kp * cprev[f]
                    numerator = h + kp * dprev[f]
                else:
                    divisor = diagonal
                    numerator = h
                if l < levels - 1:
                    cprev[f] = -kd / divisor
                    c_ref[f, l] = cprev[f]
                dprev[f] = numerator / divisor
                out_ref[f, l] = dprev[f]
        wet = wet_ref[...]
        if emit:
            sub = lax.broadcasted_iota(jnp.int32, (8, cols), 0)
            lane = lax.broadcasted_iota(jnp.int32, (rows, planes), 1)
            last_cols = jnp.zeros((rows, planes), jnp.float32)
            first_cols = jnp.zeros((rows, planes), jnp.float32)
            last_rows = jnp.zeros((8, cols), jnp.float32)
            first_rows = jnp.zeros((8, cols), jnp.float32)
        for f in range(fields):
            r = dprev[f]
            for l in range(levels - 1, -1, -1):
                if l < levels - 1:
                    r = out_ref[f, l] - c_ref[f, l] * r
                v = r * wet
                out_ref[f, l] = v
                if emit:
                    k = f * levels + l
                    last_rows = jnp.where(sub == k % 8, v[rows - 1 : rows, :], last_rows)
                    first_rows = jnp.where(sub == k % 8, v[0:1, :], first_rows)
                    last_cols = jnp.where(lane == k, v[:, cols - 1 : cols], last_cols)
                    first_cols = jnp.where(lane == k, v[:, 0:1], first_cols)
                    if k % 8 == 0:
                        eu_ref[pl.ds(k, 8), :] = last_rows
                        ed_ref[pl.ds(k, 8), :] = first_rows
        if emit:
            el_ref[...] = last_cols
            er_ref[...] = first_cols

    return kernel


def run_step(a, halos, coef_halos, ue, un, coeffs, wet, inc=None, emit=False):
    fields, levels, rows, cols = a.shape
    planes = fields * levels
    coupled = inc is not None
    operands = [a, *halos, *coef_halos, ue, un, coeffs, wet]
    if coupled:
        operands += list(inc)
    shapes = [jax.ShapeDtypeStruct(a.shape, jnp.float32)]
    if emit:
        shapes += [jax.ShapeDtypeStruct((planes, cols), jnp.float32)] * 2
        shapes += [jax.ShapeDtypeStruct((rows, planes), jnp.float32)] * 2
    return pl.pallas_call(
        step_kernel(fields, levels, rows, cols, coupled, emit),
        out_shape=shapes,
        scratch_shapes=[pltpu.VMEM(a.shape, jnp.float32)],
    )(*operands)


def shards(
    adjoint_in, u_east, u_north, diffusivity, wet_mask, dest_tile, src_row, dst_row, area_weight
):
    adjoint = adjoint_in[0]
    fields, levels, rows_x, cols_y = adjoint.shape
    planes = fields * levels
    sections = lax.axis_size("comp")
    tiles_x = lax.axis_size("gx")
    tiles_y = lax.axis_size("gy")
    tiles = tiles_x * tiles_y
    section = lax.axis_index("comp")
    east = u_east[0]
    north = u_north[0]
    coeffs = diffusivity[0]
    wet = wet_mask[0].astype(jnp.float32)

    def row_edge(index):
        field_rows = adjoint[:, :, index, :].reshape(planes, cols_y)
        return jnp.concatenate([field_rows, east[:, index, :]], 0)

    def col_edge(index):
        field_cols = jnp.transpose(adjoint[:, :, :, index], (2, 0, 1)).reshape(rows_x, planes)
        return jnp.concatenate([field_cols, north[:, :, index].T], 1)


    targets = dest_tile[0, 0, 0, :, 0]
    sources = src_row[0, 0, 0]
    landing = dst_row[0, 0, 0]
    weights = area_weight[0, 0, 0]
    count = targets.shape[0]
    surface_rows = jnp.transpose(adjoint[:, 0], (1, 0, 2)).reshape(rows_x, fields * cols_y)
    pick_table = (sources[:, None] == jnp.arange(rows_x, dtype=jnp.int32)[None, :]).astype(
        jnp.float32
    )
    payload = jnp.dot(
        pick_table,
        surface_rows,
        precision=lax.Precision.HIGHEST,
        preferred_element_type=jnp.float32,
    )
    payload = (payload.reshape(count, fields, cols_y) * weights[:, None, :]).reshape(
        count, fields * cols_y
    )
    keys = targets * rows_x + landing
    placing = (
        keys[None, :] == jnp.arange(tiles * rows_x, dtype=jnp.int32)[:, None]
    ).astype(jnp.float32)
    summed = jnp.dot(
        placing, payload, precision=lax.Precision.HIGHEST, preferred_element_type=jnp.float32
    ).reshape(tiles_x, tiles_y, rows_x, fields, cols_y)
    order_ids = jnp.arange(count, dtype=jnp.int32)
    earlier = (targets[:, None] == targets[None, :]) & (order_ids[None, :] < order_ids[:, None])
    rank_in = jnp.sum(earlier.astype(jnp.int32), axis=1)
    slot_ids = targets * CAP + rank_in
    slotting = slot_ids[None, :] == jnp.arange(tiles * CAP, dtype=jnp.int32)[:, None]
    slots = jnp.dot(
        slotting.astype(jnp.float32),
        payload,
        precision=lax.Precision.HIGHEST,
        preferred_element_type=jnp.float32,
    ).reshape(tiles, CAP, fields * cols_y)
    tags = jnp.sum(slotting.astype(jnp.int32) * (landing + 1)[None, :], axis=1)
    tags = tags.astype(jnp.float32).reshape(tiles_x, tiles_y, CAP)
    zero_x = jnp.zeros((1, tiles_y, fields, cols_y), jnp.float32)
    up_rows = jnp.concatenate([zero_x, summed[:-1, :, rows_x - 1]], 0)
    dn_rows = jnp.concatenate([summed[1:, :, 0], zero_x], 0)
    zero_y = jnp.zeros((tiles_x, 1, rows_x, fields), jnp.float32)
    lf_cols = jnp.concatenate([zero_y, summed[:, :-1, :, :, cols_y - 1]], 1)
    rt_cols = jnp.concatenate([summed[:, 1:, :, :, 0], zero_y], 1)
    ring = 2 * rows_x * fields
    side = jnp.concatenate([lf_cols, rt_cols], 3).reshape(tiles_x, tiles_y, ring)
    side = jnp.concatenate([side, tags], 2)
    side = jnp.pad(side, ((0, 0), (0, 0), (0, fields * cols_y - ring - CAP)))
    send_data = jnp.concatenate(
        [
            slots,
            up_rows.reshape(tiles, 1, fields * cols_y),
            dn_rows.reshape(tiles, 1, fields * cols_y),
            side.reshape(tiles, 1, fields * cols_y),
        ],
        1,
    )
    send_data, *outgoing = lax.optimization_barrier(
        (send_data, row_edge(rows_x - 1), row_edge(0), col_edge(cols_y - 1), col_edge(0))
    )
    got = lax.all_to_all(send_data, ("gx", "gy"), split_axis=0, concat_axis=0, tiled=True)
    halos = (
        shift(outgoing[0], "gx", 1),
        shift(outgoing[1], "gx", -1),
        shift(outgoing[2], "gy", 1),
        shift(outgoing[3], "gy", -1),
    )
    got_tags = got[:, CAP + 2, ring : ring + CAP].reshape(tiles * CAP)
    row_table = (
        got_tags[None, :] == (jnp.arange(rows_x, dtype=jnp.int32) + 1).astype(jnp.float32)[:, None]
    ).astype(jnp.float32)
    increment = jnp.dot(
        row_table,
        got[:, :CAP].reshape(tiles * CAP, fields * cols_y),
        precision=lax.Precision.HIGHEST,
        preferred_element_type=jnp.float32,
    )
    edges_sum = jnp.sum(got[:, CAP:], axis=0)
    packed = jnp.concatenate([increment, edges_sum], 0)
    packed = lax.ppermute(packed, "comp", [(c, sections - 1 - c) for c in range(sections)])
    inc_cols = packed[rows_x + 2, :ring].reshape(rows_x, 2 * fields)
    inc = (packed[: rows_x + 2], inc_cols)

    middle, last_rows, first_rows, last_cols, first_cols = run_step(
        adjoint, halos, halos, east, north, coeffs, wet, inc=inc, emit=True
    )
    step_halos = both_ways(last_rows, first_rows, "gx") + both_ways(last_cols, first_cols, "gy")
    (result,) = run_step(middle, step_halos, halos, east, north, coeffs, wet)
    return result[None]


def solution(mesh):
    placed = (
        P("comp", None, None, "gx", "gy"),
        P("comp", None, "gx", "gy"),
        P("comp", None, "gx", "gy"),
        P("comp", None, None, "gx", "gy"),
        P("comp", "gx", "gy"),
        P("comp", "gx", "gy", None, None),
        P("comp", "gx", "gy", None),
        P("comp", "gx", "gy", None),
        P("comp", "gx", "gy", None, None),
    )
    return jax.shard_map(
        shards,
        mesh=mesh,
        in_specs=placed,
        out_specs=P("comp", None, None, "gx", "gy"),
        check_vma=False,
    )
```

```python
import jax
import jax.numpy as jnp
from jax import lax
from jax.experimental import pallas as pl
from jax.experimental.pallas import tpu as pltpu
from jax.sharding import PartitionSpec as P

CAP = 4


diffusion = 0.2


def shift(block, axis, step):
    count = lax.axis_size(axis)
    route = [(i, i + step) for i in range(count) if 0 <= i + step < count]
    return lax.ppermute(block, axis, route)


def step_kernel(fields, levels, rows, cols, coupled, emit):
    planes = fields * levels

    def kernel(*refs):
        refs = list(refs)
        a_ref, up_ref, dn_ref, lf_ref, rt_ref, cu_ref, cd_ref, cl_ref, cr_ref = refs[:9]
        ue_ref, un_ref, k_ref, wet_ref = refs[9:13]
        refs = refs[13:]
        if coupled:
            inc_ref = refs.pop(0)
        out_ref = refs.pop(0)
        if emit:
            eu_ref, ed_ref, el_ref, er_ref = refs[:4]
            refs = refs[4:]
        c_ref = refs[0]
        row = lax.broadcasted_iota(jnp.int32, (rows, cols), 0)
        col = lax.broadcasted_iota(jnp.int32, (rows, cols), 1)
        top = row == 0
        bottom = row == rows - 1
        left = col == 0
        right = col == cols - 1
        cprev = [None] * fields
        dprev = [None] * fields
        if coupled:
            side = jnp.broadcast_to(inc_ref[pl.ds(rows + 2, 1), :], (rows, fields * cols))
            place = lax.broadcasted_iota(jnp.int32, (rows, fields * cols), 1)
            owner = lax.broadcasted_iota(jnp.int32, (rows, fields * cols), 0) * (2 * fields)
            inc_cols = [
                jnp.sum(jnp.where(place == owner + c, side, 0.0), axis=1, keepdims=True)
                for c in range(2 * fields)
            ]
        for l in range(levels):
            ue = ue_ref[l]
            un = un_ref[l]
            ci = planes + l
            ue_m = jnp.where(top, cu_ref[pl.ds(ci, 1), :], pltpu.roll(ue, 1, 0))
            ue_p = jnp.where(bottom, cd_ref[pl.ds(ci, 1), :], pltpu.roll(ue, rows - 1, 0))
            un_m = jnp.where(left, cl_ref[:, pl.ds(ci, 1)], pltpu.roll(un, 1, 1))
            un_p = jnp.where(right, cr_ref[:, pl.ds(ci, 1)], pltpu.roll(un, cols - 1, 1))
            for f in range(fields):
                k = f * levels + l
                a = a_ref[f, l]
                up = up_ref[pl.ds(k, 1), :]
                dn = dn_ref[pl.ds(k, 1), :]
                lf = lf_ref[:, pl.ds(k, 1)]
                rt = rt_ref[:, pl.ds(k, 1)]
                if coupled and l == 0:
                    lanes = pl.ds(f * cols, cols)
                    a = a + inc_ref[pl.ds(0, rows), lanes]
                    up = up + inc_ref[pl.ds(rows, 1), lanes]
                    dn = dn + inc_ref[pl.ds(rows + 1, 1), lanes]
                    lf = lf + inc_cols[f]
                    rt = rt + inc_cols[fields + f]
                a_im = jnp.where(top, up, pltpu.roll(a, 1, 0))
                a_ip = jnp.where(bottom, dn, pltpu.roll(a, rows - 1, 0))
                a_jm = jnp.where(left, lf, pltpu.roll(a, 1, 1))
                a_jp = jnp.where(right, rt, pltpu.roll(a, cols - 1, 1))
                laplace = a_ip + a_im + a_jp + a_jm - 4.0 * a
                advect = 0.5 * (ue_m * a_im - ue_p * a_ip) + 0.5 * (un_m * a_jm - un_p * a_jp)
                h = a + diffusion * laplace + advect
                if l < levels - 1:
                    kd = k_ref[f, l]
                    diagonal = 1.0 + kd
                else:
                    diagonal = 1.0
                if l > 0:
                    kp = k_ref[f, l - 1]
                    divisor = diagonal + kp + kp * cprev[f]
                    numerator = h + kp * dprev[f]
                else:
                    divisor = diagonal
                    numerator = h
                if l < levels - 1:
                    cprev[f] = -kd / divisor
                    c_ref[f, l] = cprev[f]
                dprev[f] = numerator / divisor
                out_ref[f, l] = dprev[f]
        wet = wet_ref[...]
        if emit:
            sub = lax.broadcasted_iota(jnp.int32, (8, cols), 0)
            lane = lax.broadcasted_iota(jnp.int32, (rows, planes), 1)
            last_cols = jnp.zeros((rows, planes), jnp.float32)
            first_cols = jnp.zeros((rows, planes), jnp.float32)
            last_rows = jnp.zeros((8, cols), jnp.float32)
            first_rows = jnp.zeros((8, cols), jnp.float32)
        for f in range(fields):
            r = dprev[f]
            for l in range(levels - 1, -1, -1):
                if l < levels - 1:
                    r = out_ref[f, l] - c_ref[f, l] * r
                v = r * wet
                out_ref[f, l] = v
                if emit:
                    k = f * levels + l
                    last_rows = jnp.where(sub == k % 8, v[rows - 1 : rows, :], last_rows)
                    first_rows = jnp.where(sub == k % 8, v[0:1, :], first_rows)
                    last_cols = jnp.where(lane == k, v[:, cols - 1 : cols], last_cols)
                    first_cols = jnp.where(lane == k, v[:, 0:1], first_cols)
                    if k % 8 == 0:
                        eu_ref[pl.ds(k, 8), :] = last_rows
                        ed_ref[pl.ds(k, 8), :] = first_rows
        if emit:
            el_ref[...] = last_cols
            er_ref[...] = first_cols

    return kernel


def run_step(a, halos, coef_halos, ue, un, coeffs, wet, inc=None, emit=False):
    fields, levels, rows, cols = a.shape
    planes = fields * levels
    coupled = inc is not None
    operands = [a, *halos, *coef_halos, ue, un, coeffs, wet]
    if coupled:
        operands += list(inc)
    shapes = [jax.ShapeDtypeStruct(a.shape, jnp.float32)]
    if emit:
        shapes += [jax.ShapeDtypeStruct((planes, cols), jnp.float32)] * 2
        shapes += [jax.ShapeDtypeStruct((rows, planes), jnp.float32)] * 2
    return pl.pallas_call(
        step_kernel(fields, levels, rows, cols, coupled, emit),
        out_shape=shapes,
        scratch_shapes=[pltpu.VMEM(a.shape, jnp.float32)],
    )(*operands)


def shards(
    adjoint_in, u_east, u_north, diffusivity, wet_mask, dest_tile, src_row, dst_row, area_weight
):
    adjoint = adjoint_in[0]
    fields, levels, rows_x, cols_y = adjoint.shape
    planes = fields * levels
    sections = lax.axis_size("comp")
    tiles_x = lax.axis_size("gx")
    tiles_y = lax.axis_size("gy")
    tiles = tiles_x * tiles_y
    section = lax.axis_index("comp")
    east = u_east[0]
    north = u_north[0]
    coeffs = diffusivity[0]
    wet = wet_mask[0].astype(jnp.float32)

    def row_edge(index):
        field_rows = adjoint[:, :, index, :].reshape(planes, cols_y)
        return jnp.concatenate([field_rows, east[:, index, :]], 0)

    def col_edge(index):
        field_cols = jnp.transpose(adjoint[:, :, :, index], (2, 0, 1)).reshape(rows_x, planes)
        return jnp.concatenate([field_cols, north[:, :, index].T], 1)


    targets = dest_tile[0, 0, 0, :, 0]
    sources = src_row[0, 0, 0]
    landing = dst_row[0, 0, 0]
    weights = area_weight[0, 0, 0]
    count = targets.shape[0]
    surface_rows = jnp.transpose(adjoint[:, 0], (1, 0, 2)).reshape(rows_x, fields * cols_y)
    pick_table = (sources[:, None] == jnp.arange(rows_x, dtype=jnp.int32)[None, :]).astype(
        jnp.float32
    )
    payload = jnp.dot(
        pick_table,
        surface_rows,
        precision=lax.Precision.HIGHEST,
        preferred_element_type=jnp.float32,
    )
    payload = (payload.reshape(count, fields, cols_y) * weights[:, None, :]).reshape(
        count, fields * cols_y
    )
    keys = targets * rows_x + landing
    placing = (
        keys[None, :] == jnp.arange(tiles * rows_x, dtype=jnp.int32)[:, None]
    ).astype(jnp.float32)
    summed = jnp.dot(
        placing, payload, precision=lax.Precision.HIGHEST, preferred_element_type=jnp.float32
    ).reshape(tiles_x, tiles_y, rows_x, fields, cols_y)
    order_ids = jnp.arange(count, dtype=jnp.int32)
    earlier = (targets[:, None] == targets[None, :]) & (order_ids[None, :] < order_ids[:, None])
    rank_in = jnp.sum(earlier.astype(jnp.int32), axis=1)
    slot_ids = targets * CAP + rank_in
    slotting = slot_ids[None, :] == jnp.arange(tiles * CAP, dtype=jnp.int32)[:, None]
    slots = jnp.dot(
        slotting.astype(jnp.float32),
        payload,
        precision=lax.Precision.HIGHEST,
        preferred_element_type=jnp.float32,
    ).reshape(tiles, CAP, fields * cols_y)
    tags = jnp.sum(slotting.astype(jnp.int32) * (landing + 1)[None, :], axis=1)
    tags = tags.astype(jnp.float32).reshape(tiles_x, tiles_y, CAP)
    zero_x = jnp.zeros((1, tiles_y, fields, cols_y), jnp.float32)
    up_rows = jnp.concatenate([zero_x, summed[:-1, :, rows_x - 1]], 0)
    dn_rows = jnp.concatenate([summed[1:, :, 0], zero_x], 0)
    zero_y = jnp.zeros((tiles_x, 1, rows_x, fields), jnp.float32)
    lf_cols = jnp.concatenate([zero_y, summed[:, :-1, :, :, cols_y - 1]], 1)
    rt_cols = jnp.concatenate([summed[:, 1:, :, :, 0], zero_y], 1)
    ring = 2 * rows_x * fields
    side = jnp.concatenate([lf_cols, rt_cols], 3).reshape(tiles_x, tiles_y, ring)
    side = jnp.concatenate([side, tags], 2)
    side = jnp.pad(side, ((0, 0), (0, 0), (0, fields * cols_y - ring - CAP)))
    send_data = jnp.concatenate(
        [
            slots,
            up_rows.reshape(tiles, 1, fields * cols_y),
            dn_rows.reshape(tiles, 1, fields * cols_y),
            side.reshape(tiles, 1, fields * cols_y),
        ],
        1,
    )
    send_data, *outgoing = lax.optimization_barrier(
        (send_data, row_edge(rows_x - 1), row_edge(0), col_edge(cols_y - 1), col_edge(0))
    )
    got = lax.all_to_all(send_data, ("gx", "gy"), split_axis=0, concat_axis=0, tiled=True)
    halos = (
        shift(outgoing[0], "gx", 1),
        shift(outgoing[1], "gx", -1),
        shift(outgoing[2], "gy", 1),
        shift(outgoing[3], "gy", -1),
    )
    got_tags = got[:, CAP + 2, ring : ring + CAP].reshape(tiles * CAP)
    row_table = (
        got_tags[None, :] == (jnp.arange(rows_x, dtype=jnp.int32) + 1).astype(jnp.float32)[:, None]
    ).astype(jnp.float32)
    increment = jnp.dot(
        row_table,
        got[:, :CAP].reshape(tiles * CAP, fields * cols_y),
        precision=lax.Precision.HIGHEST,
        preferred_element_type=jnp.float32,
    )
    edges_sum = jnp.sum(got[:, CAP:], axis=0)
    packed = jnp.concatenate([increment, edges_sum], 0)
    packed = lax.ppermute(packed, "comp", [(c, sections - 1 - c) for c in range(sections)])
    inc = (packed,)

    middle, last_rows, first_rows, last_cols, first_cols = run_step(
        adjoint, halos, halos, east, north, coeffs, wet, inc=inc, emit=True
    )
    step_halos = (
        shift(last_rows, "gx", 1),
        shift(first_rows, "gx", -1),
        shift(last_cols, "gy", 1),
        shift(first_cols, "gy", -1),
    )
    (result,) = run_step(middle, step_halos, halos, east, north, coeffs, wet)
    return result[None]


def solution(mesh):
    placed = (
        P("comp", None, None, "gx", "gy"),
        P("comp", None, "gx", "gy"),
        P("comp", None, "gx", "gy"),
        P("comp", None, None, "gx", "gy"),
        P("comp", "gx", "gy"),
        P("comp", "gx", "gy", None, None),
        P("comp", "gx", "gy", None),
        P("comp", "gx", "gy", None),
        P("comp", "gx", "gy", None, None),
    )
    return jax.shard_map(
        shards,
        mesh=mesh,
        in_specs=placed,
        out_specs=P("comp", None, None, "gx", "gy"),
        check_vma=False,
    )
```

```python
import jax
import jax.numpy as jnp
from jax import lax
from jax.experimental import pallas as pl
from jax.experimental.pallas import tpu as pltpu
from jax.sharding import PartitionSpec as P

CAP = 4


diffusion = 0.2


def shift(block, axis, step):
    count = lax.axis_size(axis)
    route = [(i, i + step) for i in range(count) if 0 <= i + step < count]
    return lax.ppermute(block, axis, route)


def step_kernel(fields, levels, rows, cols, coupled, emit):
    planes = fields * levels

    def kernel(*refs):
        refs = list(refs)
        a_hbm, up_ref, dn_ref, lf_ref, rt_ref, cu_ref, cd_ref, cl_ref, cr_ref = refs[:9]
        ue_ref, un_ref, k_hbm, wet_ref = refs[9:13]
        refs = refs[13:]
        if coupled:
            inc_ref = refs.pop(0)
        out_ref = refs.pop(0)
        if emit:
            eu_ref, ed_ref, el_ref, er_ref = refs[:4]
            refs = refs[4:]
        c_ref, a_ref, k_ref, sems = refs[:4]
        chunk = 8
        pending = []
        for c in range(levels // chunk):
            window = pl.ds(c * chunk, chunk)
            pending.append(
                (
                    pltpu.make_async_copy(a_hbm.at[:, window], a_ref.at[:, window], sems.at[0, c]),
                    pltpu.make_async_copy(k_hbm.at[:, window], k_ref.at[:, window], sems.at[1, c]),
                )
            )
            pending[-1][0].start()
            pending[-1][1].start()
        row = lax.broadcasted_iota(jnp.int32, (rows, cols), 0)
        col = lax.broadcasted_iota(jnp.int32, (rows, cols), 1)
        top = row == 0
        bottom = row == rows - 1
        left = col == 0
        right = col == cols - 1
        cprev = [None] * fields
        dprev = [None] * fields
        if coupled:
            side = jnp.broadcast_to(inc_ref[pl.ds(rows + 2, 1), :], (rows, fields * cols))
            place = lax.broadcasted_iota(jnp.int32, (rows, fields * cols), 1)
            owner = lax.broadcasted_iota(jnp.int32, (rows, fields * cols), 0) * (2 * fields)
            inc_cols = [
                jnp.sum(jnp.where(place == owner + c, side, 0.0), axis=1, keepdims=True)
                for c in range(2 * fields)
            ]
        for l in range(levels):
            if l % chunk == 0:
                pending[l // chunk][0].wait()
                pending[l // chunk][1].wait()
            ue = ue_ref[l]
            un = un_ref[l]
            ci = planes + l
            ue_m = jnp.where(top, cu_ref[pl.ds(ci, 1), :], pltpu.roll(ue, 1, 0))
            ue_p = jnp.where(bottom, cd_ref[pl.ds(ci, 1), :], pltpu.roll(ue, rows - 1, 0))
            un_m = jnp.where(left, cl_ref[:, pl.ds(ci, 1)], pltpu.roll(un, 1, 1))
            un_p = jnp.where(right, cr_ref[:, pl.ds(ci, 1)], pltpu.roll(un, cols - 1, 1))
            for f in range(fields):
                k = f * levels + l
                a = a_ref[f, l]
                up = up_ref[pl.ds(k, 1), :]
                dn = dn_ref[pl.ds(k, 1), :]
                lf = lf_ref[:, pl.ds(k, 1)]
                rt = rt_ref[:, pl.ds(k, 1)]
                if coupled and l == 0:
                    lanes = pl.ds(f * cols, cols)
                    a = a + inc_ref[pl.ds(0, rows), lanes]
                    up = up + inc_ref[pl.ds(rows, 1), lanes]
                    dn = dn + inc_ref[pl.ds(rows + 1, 1), lanes]
                    lf = lf + inc_cols[f]
                    rt = rt + inc_cols[fields + f]
                a_im = jnp.where(top, up, pltpu.roll(a, 1, 0))
                a_ip = jnp.where(bottom, dn, pltpu.roll(a, rows - 1, 0))
                a_jm = jnp.where(left, lf, pltpu.roll(a, 1, 1))
                a_jp = jnp.where(right, rt, pltpu.roll(a, cols - 1, 1))
                laplace = a_ip + a_im + a_jp + a_jm - 4.0 * a
                advect = 0.5 * (ue_m * a_im - ue_p * a_ip) + 0.5 * (un_m * a_jm - un_p * a_jp)
                h = a + diffusion * laplace + advect
                if l < levels - 1:
                    kd = k_ref[f, l]
                    diagonal = 1.0 + kd
                else:
                    diagonal = 1.0
                if l > 0:
                    kp = k_ref[f, l - 1]
                    divisor = diagonal + kp + kp * cprev[f]
                    numerator = h + kp * dprev[f]
                else:
                    divisor = diagonal
                    numerator = h
                if l < levels - 1:
                    cprev[f] = -kd / divisor
                    c_ref[f, l] = cprev[f]
                dprev[f] = numerator / divisor
                out_ref[f, l] = dprev[f]
        wet = wet_ref[...]
        if emit:
            sub = lax.broadcasted_iota(jnp.int32, (8, cols), 0)
            lane = lax.broadcasted_iota(jnp.int32, (rows, planes), 1)
            last_cols = jnp.zeros((rows, planes), jnp.float32)
            first_cols = jnp.zeros((rows, planes), jnp.float32)
            last_rows = jnp.zeros((8, cols), jnp.float32)
            first_rows = jnp.zeros((8, cols), jnp.float32)
        for f in range(fields):
            r = dprev[f]
            for l in range(levels - 1, -1, -1):
                if l < levels - 1:
                    r = out_ref[f, l] - c_ref[f, l] * r
                v = r * wet
                out_ref[f, l] = v
                if emit:
                    k = f * levels + l
                    last_rows = jnp.where(sub == k % 8, v[rows - 1 : rows, :], last_rows)
                    first_rows = jnp.where(sub == k % 8, v[0:1, :], first_rows)
                    last_cols = jnp.where(lane == k, v[:, cols - 1 : cols], last_cols)
                    first_cols = jnp.where(lane == k, v[:, 0:1], first_cols)
                    if k % 8 == 0:
                        eu_ref[pl.ds(k, 8), :] = last_rows
                        ed_ref[pl.ds(k, 8), :] = first_rows
        if emit:
            el_ref[...] = last_cols
            er_ref[...] = first_cols

    return kernel


def run_step(a, halos, coef_halos, ue, un, coeffs, wet, inc=None, emit=False):
    fields, levels, rows, cols = a.shape
    planes = fields * levels
    coupled = inc is not None
    operands = [a, *halos, *coef_halos, ue, un, coeffs, wet]
    if coupled:
        operands += list(inc)
    shapes = [jax.ShapeDtypeStruct(a.shape, jnp.float32)]
    if emit:
        shapes += [jax.ShapeDtypeStruct((planes, cols), jnp.float32)] * 2
        shapes += [jax.ShapeDtypeStruct((rows, planes), jnp.float32)] * 2
    in_specs = [pl.BlockSpec(memory_space=pltpu.VMEM)] * len(operands)
    in_specs[0] = pl.BlockSpec(memory_space=pl.ANY)
    in_specs[11] = pl.BlockSpec(memory_space=pl.ANY)
    return pl.pallas_call(
        step_kernel(fields, levels, rows, cols, coupled, emit),
        out_shape=shapes,
        in_specs=in_specs,
        scratch_shapes=[
            pltpu.VMEM(a.shape, jnp.float32),
            pltpu.VMEM(a.shape, jnp.float32),
            pltpu.VMEM(coeffs.shape, jnp.float32),
            pltpu.SemaphoreType.DMA((2, levels // 8)),
        ],
    )(*operands)


def shards(
    adjoint_in, u_east, u_north, diffusivity, wet_mask, dest_tile, src_row, dst_row, area_weight
):
    adjoint = adjoint_in[0]
    fields, levels, rows_x, cols_y = adjoint.shape
    planes = fields * levels
    sections = lax.axis_size("comp")
    tiles_x = lax.axis_size("gx")
    tiles_y = lax.axis_size("gy")
    tiles = tiles_x * tiles_y
    section = lax.axis_index("comp")
    east = u_east[0]
    north = u_north[0]
    coeffs = diffusivity[0]
    wet = wet_mask[0].astype(jnp.float32)

    def row_edge(index):
        field_rows = adjoint[:, :, index, :].reshape(planes, cols_y)
        return jnp.concatenate([field_rows, east[:, index, :]], 0)

    def col_edge(index):
        field_cols = jnp.transpose(adjoint[:, :, :, index], (2, 0, 1)).reshape(rows_x, planes)
        return jnp.concatenate([field_cols, north[:, :, index].T], 1)


    targets = dest_tile[0, 0, 0, :, 0]
    sources = src_row[0, 0, 0]
    landing = dst_row[0, 0, 0]
    weights = area_weight[0, 0, 0]
    count = targets.shape[0]
    surface_rows = jnp.transpose(adjoint[:, 0], (1, 0, 2)).reshape(rows_x, fields * cols_y)
    pick_table = (sources[:, None] == jnp.arange(rows_x, dtype=jnp.int32)[None, :]).astype(
        jnp.float32
    )
    payload = jnp.dot(
        pick_table,
        surface_rows,
        precision=lax.Precision.HIGHEST,
        preferred_element_type=jnp.float32,
    )
    payload = (payload.reshape(count, fields, cols_y) * weights[:, None, :]).reshape(
        count, fields * cols_y
    )
    keys = targets * rows_x + landing
    placing = (
        keys[None, :] == jnp.arange(tiles * rows_x, dtype=jnp.int32)[:, None]
    ).astype(jnp.float32)
    summed = jnp.dot(
        placing, payload, precision=lax.Precision.HIGHEST, preferred_element_type=jnp.float32
    ).reshape(tiles_x, tiles_y, rows_x, fields, cols_y)
    order_ids = jnp.arange(count, dtype=jnp.int32)
    earlier = (targets[:, None] == targets[None, :]) & (order_ids[None, :] < order_ids[:, None])
    rank_in = jnp.sum(earlier.astype(jnp.int32), axis=1)
    slot_ids = targets * CAP + rank_in
    slotting = slot_ids[None, :] == jnp.arange(tiles * CAP, dtype=jnp.int32)[:, None]
    slots = jnp.dot(
        slotting.astype(jnp.float32),
        payload,
        precision=lax.Precision.HIGHEST,
        preferred_element_type=jnp.float32,
    ).reshape(tiles, CAP, fields * cols_y)
    tags = jnp.sum(slotting.astype(jnp.int32) * (landing + 1)[None, :], axis=1)
    tags = tags.astype(jnp.float32).reshape(tiles_x, tiles_y, CAP)
    zero_x = jnp.zeros((1, tiles_y, fields, cols_y), jnp.float32)
    up_rows = jnp.concatenate([zero_x, summed[:-1, :, rows_x - 1]], 0)
    dn_rows = jnp.concatenate([summed[1:, :, 0], zero_x], 0)
    zero_y = jnp.zeros((tiles_x, 1, rows_x, fields), jnp.float32)
    lf_cols = jnp.concatenate([zero_y, summed[:, :-1, :, :, cols_y - 1]], 1)
    rt_cols = jnp.concatenate([summed[:, 1:, :, :, 0], zero_y], 1)
    ring = 2 * rows_x * fields
    side = jnp.concatenate([lf_cols, rt_cols], 3).reshape(tiles_x, tiles_y, ring)
    side = jnp.concatenate([side, tags], 2)
    side = jnp.pad(side, ((0, 0), (0, 0), (0, fields * cols_y - ring - CAP)))
    send_data = jnp.concatenate(
        [
            slots,
            up_rows.reshape(tiles, 1, fields * cols_y),
            dn_rows.reshape(tiles, 1, fields * cols_y),
            side.reshape(tiles, 1, fields * cols_y),
        ],
        1,
    )
    send_data, *outgoing = lax.optimization_barrier(
        (send_data, row_edge(rows_x - 1), row_edge(0), col_edge(cols_y - 1), col_edge(0))
    )
    got = lax.all_to_all(send_data, ("gx", "gy"), split_axis=0, concat_axis=0, tiled=True)
    halos = (
        shift(outgoing[0], "gx", 1),
        shift(outgoing[1], "gx", -1),
        shift(outgoing[2], "gy", 1),
        shift(outgoing[3], "gy", -1),
    )
    got_tags = got[:, CAP + 2, ring : ring + CAP].reshape(tiles * CAP)
    row_table = (
        got_tags[None, :] == (jnp.arange(rows_x, dtype=jnp.int32) + 1).astype(jnp.float32)[:, None]
    ).astype(jnp.float32)
    increment = jnp.dot(
        row_table,
        got[:, :CAP].reshape(tiles * CAP, fields * cols_y),
        precision=lax.Precision.HIGHEST,
        preferred_element_type=jnp.float32,
    )
    edges_sum = jnp.sum(got[:, CAP:], axis=0)
    packed = jnp.concatenate([increment, edges_sum], 0)
    packed = lax.ppermute(packed, "comp", [(c, sections - 1 - c) for c in range(sections)])
    inc = (packed,)

    middle, last_rows, first_rows, last_cols, first_cols = run_step(
        adjoint, halos, halos, east, north, coeffs, wet, inc=inc, emit=True
    )
    step_halos = (
        shift(last_rows, "gx", 1),
        shift(first_rows, "gx", -1),
        shift(last_cols, "gy", 1),
        shift(first_cols, "gy", -1),
    )
    (result,) = run_step(middle, step_halos, halos, east, north, coeffs, wet)
    return result[None]


def solution(mesh):
    placed = (
        P("comp", None, None, "gx", "gy"),
        P("comp", None, "gx", "gy"),
        P("comp", None, "gx", "gy"),
        P("comp", None, None, "gx", "gy"),
        P("comp", "gx", "gy"),
        P("comp", "gx", "gy", None, None),
        P("comp", "gx", "gy", None),
        P("comp", "gx", "gy", None),
        P("comp", "gx", "gy", None, None),
    )
    return jax.shard_map(
        shards,
        mesh=mesh,
        in_specs=placed,
        out_specs=P("comp", None, None, "gx", "gy"),
        check_vma=False,
    )
```

```python
import jax
import jax.numpy as jnp
from jax import lax
from jax.experimental import pallas as pl
from jax.experimental.pallas import tpu as pltpu
from jax.sharding import PartitionSpec as P

CAP = 4


diffusion = 0.2


def shift(block, axis, step):
    count = lax.axis_size(axis)
    route = [(i, i + step) for i in range(count) if 0 <= i + step < count]
    return lax.ppermute(block, axis, route)


def step_kernel(fields, levels, rows, cols, coupled, emit):
    planes = fields * levels

    def kernel(*refs):
        refs = list(refs)
        a_ref, up_ref, dn_ref, lf_ref, rt_ref, cu_ref, cd_ref, cl_ref, cr_ref = refs[:9]
        ue_ref, un_ref, k_ref, wet_ref = refs[9:13]
        refs = refs[13:]
        if coupled:
            inc_ref = refs.pop(0)
        out_ref = refs.pop(0)
        if emit:
            eu_ref, ed_ref, el_ref, er_ref = refs[:4]
            refs = refs[4:]
        c_ref = refs[0]
        row = lax.broadcasted_iota(jnp.int32, (rows, cols), 0)
        col = lax.broadcasted_iota(jnp.int32, (rows, cols), 1)
        top = row == 0
        bottom = row == rows - 1
        left = col == 0
        right = col == cols - 1
        cprev = [None] * fields
        dprev = [None] * fields
        if coupled:
            side = jnp.broadcast_to(inc_ref[pl.ds(rows + 2, 1), :], (rows, fields * cols))
            place = lax.broadcasted_iota(jnp.int32, (rows, fields * cols), 1)
            owner = lax.broadcasted_iota(jnp.int32, (rows, fields * cols), 0) * (2 * fields)
            inc_cols = [
                jnp.sum(jnp.where(place == owner + c, side, 0.0), axis=1, keepdims=True)
                for c in range(2 * fields)
            ]
        for l in range(levels):
            ue = ue_ref[l]
            un = un_ref[l]
            ci = planes + l
            ue_m = jnp.where(top, cu_ref[pl.ds(ci, 1), :], pltpu.roll(ue, 1, 0))
            ue_p = jnp.where(bottom, cd_ref[pl.ds(ci, 1), :], pltpu.roll(ue, rows - 1, 0))
            un_m = jnp.where(left, cl_ref[:, pl.ds(ci, 1)], pltpu.roll(un, 1, 1))
            un_p = jnp.where(right, cr_ref[:, pl.ds(ci, 1)], pltpu.roll(un, cols - 1, 1))
            for f in range(fields):
                k = f * levels + l
                a = a_ref[f, l]
                up = up_ref[pl.ds(k, 1), :]
                dn = dn_ref[pl.ds(k, 1), :]
                lf = lf_ref[:, pl.ds(k, 1)]
                rt = rt_ref[:, pl.ds(k, 1)]
                if coupled and l == 0:
                    lanes = pl.ds(f * cols, cols)
                    a = a + inc_ref[pl.ds(0, rows), lanes]
                    up = up + inc_ref[pl.ds(rows, 1), lanes]
                    dn = dn + inc_ref[pl.ds(rows + 1, 1), lanes]
                    lf = lf + inc_cols[f]
                    rt = rt + inc_cols[fields + f]
                a_im = jnp.where(top, up, pltpu.roll(a, 1, 0))
                a_ip = jnp.where(bottom, dn, pltpu.roll(a, rows - 1, 0))
                a_jm = jnp.where(left, lf, pltpu.roll(a, 1, 1))
                a_jp = jnp.where(right, rt, pltpu.roll(a, cols - 1, 1))
                laplace = a_ip + a_im + a_jp + a_jm - 4.0 * a
                advect = 0.5 * (ue_m * a_im - ue_p * a_ip) + 0.5 * (un_m * a_jm - un_p * a_jp)
                h = a + diffusion * laplace + advect
                if l < levels - 1:
                    kd = k_ref[f, l]
                    diagonal = 1.0 + kd
                else:
                    diagonal = 1.0
                if l > 0:
                    kp = k_ref[f, l - 1]
                    divisor = diagonal + kp + kp * cprev[f]
                    numerator = h + kp * dprev[f]
                else:
                    divisor = diagonal
                    numerator = h
                if l < levels - 1:
                    cprev[f] = -kd / divisor
                    c_ref[f, l] = cprev[f]
                dprev[f] = numerator / divisor
                out_ref[f, l] = dprev[f]
        wet = wet_ref[...]
        if emit:
            sub = lax.broadcasted_iota(jnp.int32, (8, cols), 0)
            lane = lax.broadcasted_iota(jnp.int32, (rows, planes), 1)
            last_cols = jnp.zeros((rows, planes), jnp.float32)
            first_cols = jnp.zeros((rows, planes), jnp.float32)
            last_rows = jnp.zeros((8, cols), jnp.float32)
            first_rows = jnp.zeros((8, cols), jnp.float32)
        for f in range(fields):
            r = dprev[f]
            for l in range(levels - 1, -1, -1):
                if l < levels - 1:
                    r = out_ref[f, l] - c_ref[f, l] * r
                v = r * wet
                out_ref[f, l] = v
                if emit:
                    k = f * levels + l
                    last_rows = jnp.where(sub == k % 8, v[rows - 1 : rows, :], last_rows)
                    first_rows = jnp.where(sub == k % 8, v[0:1, :], first_rows)
                    last_cols = jnp.where(lane == k, v[:, cols - 1 : cols], last_cols)
                    first_cols = jnp.where(lane == k, v[:, 0:1], first_cols)
                    if k % 8 == 0:
                        eu_ref[pl.ds(k, 8), :] = last_rows
                        ed_ref[pl.ds(k, 8), :] = first_rows
        if emit:
            el_ref[...] = last_cols
            er_ref[...] = first_cols

    return kernel


def edge_kernel(fields, levels, rows, cols):
    planes = (fields + 1) * levels

    def kernel(a_ref, ue_ref, un_ref, lr_ref, fr_ref, lc_ref, fc_ref):
        sub = lax.broadcasted_iota(jnp.int32, (8, cols), 0)
        lane = lax.broadcasted_iota(jnp.int32, (rows, planes), 1)
        last_rows = jnp.zeros((8, cols), jnp.float32)
        first_rows = jnp.zeros((8, cols), jnp.float32)
        last_cols = jnp.zeros((rows, planes), jnp.float32)
        first_cols = jnp.zeros((rows, planes), jnp.float32)
        for k in range(planes):
            f, l = divmod(k, levels)
            along_x = a_ref[f, l] if f < fields else ue_ref[l]
            along_y = a_ref[f, l] if f < fields else un_ref[l]
            last_rows = jnp.where(sub == k % 8, along_x[rows - 1 : rows, :], last_rows)
            first_rows = jnp.where(sub == k % 8, along_x[0:1, :], first_rows)
            last_cols = jnp.where(lane == k, along_y[:, cols - 1 : cols], last_cols)
            first_cols = jnp.where(lane == k, along_y[:, 0:1], first_cols)
            if k % 8 == 7:
                lr_ref[pl.ds(k - 7, 8), :] = last_rows
                fr_ref[pl.ds(k - 7, 8), :] = first_rows
        lc_ref[...] = last_cols
        fc_ref[...] = first_cols

    return kernel


def input_edges(a, ue, un):
    fields, levels, rows, cols = a.shape
    planes = (fields + 1) * levels
    shapes = [jax.ShapeDtypeStruct((planes, cols), jnp.float32)] * 2
    shapes += [jax.ShapeDtypeStruct((rows, planes), jnp.float32)] * 2
    return pl.pallas_call(edge_kernel(fields, levels, rows, cols), out_shape=shapes)(a, ue, un)


def run_step(a, halos, coef_halos, ue, un, coeffs, wet, inc=None, emit=False):
    fields, levels, rows, cols = a.shape
    planes = fields * levels
    coupled = inc is not None
    operands = [a, *halos, *coef_halos, ue, un, coeffs, wet]
    if coupled:
        operands += list(inc)
    shapes = [jax.ShapeDtypeStruct(a.shape, jnp.float32)]
    if emit:
        shapes += [jax.ShapeDtypeStruct((planes, cols), jnp.float32)] * 2
        shapes += [jax.ShapeDtypeStruct((rows, planes), jnp.float32)] * 2
    return pl.pallas_call(
        step_kernel(fields, levels, rows, cols, coupled, emit),
        out_shape=shapes,
        scratch_shapes=[pltpu.VMEM(a.shape, jnp.float32)],
    )(*operands)


def shards(
    adjoint_in, u_east, u_north, diffusivity, wet_mask, dest_tile, src_row, dst_row, area_weight
):
    adjoint = adjoint_in[0]
    fields, levels, rows_x, cols_y = adjoint.shape
    planes = fields * levels
    sections = lax.axis_size("comp")
    tiles_x = lax.axis_size("gx")
    tiles_y = lax.axis_size("gy")
    tiles = tiles_x * tiles_y
    section = lax.axis_index("comp")
    east = u_east[0]
    north = u_north[0]
    coeffs = diffusivity[0]
    wet = wet_mask[0].astype(jnp.float32)

    def row_edge(index):
        field_rows = adjoint[:, :, index, :].reshape(planes, cols_y)
        return jnp.concatenate([field_rows, east[:, index, :]], 0)

    def col_edge(index):
        field_cols = jnp.transpose(adjoint[:, :, :, index], (2, 0, 1)).reshape(rows_x, planes)
        return jnp.concatenate([field_cols, north[:, :, index].T], 1)


    targets = dest_tile[0, 0, 0, :, 0]
    sources = src_row[0, 0, 0]
    landing = dst_row[0, 0, 0]
    weights = area_weight[0, 0, 0]
    count = targets.shape[0]
    surface_rows = jnp.transpose(adjoint[:, 0], (1, 0, 2)).reshape(rows_x, fields * cols_y)
    pick_table = (sources[:, None] == jnp.arange(rows_x, dtype=jnp.int32)[None, :]).astype(
        jnp.float32
    )
    payload = jnp.dot(
        pick_table,
        surface_rows,
        precision=lax.Precision.HIGHEST,
        preferred_element_type=jnp.float32,
    )
    payload = (payload.reshape(count, fields, cols_y) * weights[:, None, :]).reshape(
        count, fields * cols_y
    )
    keys = targets * rows_x + landing
    placing = (
        keys[None, :] == jnp.arange(tiles * rows_x, dtype=jnp.int32)[:, None]
    ).astype(jnp.float32)
    summed = jnp.dot(
        placing, payload, precision=lax.Precision.HIGHEST, preferred_element_type=jnp.float32
    ).reshape(tiles_x, tiles_y, rows_x, fields, cols_y)
    order_ids = jnp.arange(count, dtype=jnp.int32)
    earlier = (targets[:, None] == targets[None, :]) & (order_ids[None, :] < order_ids[:, None])
    rank_in = jnp.sum(earlier.astype(jnp.int32), axis=1)
    slot_ids = targets * CAP + rank_in
    slotting = slot_ids[None, :] == jnp.arange(tiles * CAP, dtype=jnp.int32)[:, None]
    slots = jnp.dot(
        slotting.astype(jnp.float32),
        payload,
        precision=lax.Precision.HIGHEST,
        preferred_element_type=jnp.float32,
    ).reshape(tiles, CAP, fields * cols_y)
    tags = jnp.sum(slotting.astype(jnp.int32) * (landing + 1)[None, :], axis=1)
    tags = tags.astype(jnp.float32).reshape(tiles_x, tiles_y, CAP)
    zero_x = jnp.zeros((1, tiles_y, fields, cols_y), jnp.float32)
    up_rows = jnp.concatenate([zero_x, summed[:-1, :, rows_x - 1]], 0)
    dn_rows = jnp.concatenate([summed[1:, :, 0], zero_x], 0)
    zero_y = jnp.zeros((tiles_x, 1, rows_x, fields), jnp.float32)
    lf_cols = jnp.concatenate([zero_y, summed[:, :-1, :, :, cols_y - 1]], 1)
    rt_cols = jnp.concatenate([summed[:, 1:, :, :, 0], zero_y], 1)
    ring = 2 * rows_x * fields
    side = jnp.concatenate([lf_cols, rt_cols], 3).reshape(tiles_x, tiles_y, ring)
    side = jnp.concatenate([side, tags], 2)
    side = jnp.pad(side, ((0, 0), (0, 0), (0, fields * cols_y - ring - CAP)))
    send_data = jnp.concatenate(
        [
            slots,
            up_rows.reshape(tiles, 1, fields * cols_y),
            dn_rows.reshape(tiles, 1, fields * cols_y),
            side.reshape(tiles, 1, fields * cols_y),
        ],
        1,
    )
    send_data, *outgoing = lax.optimization_barrier(
        (send_data, *input_edges(adjoint, east, north))
    )
    got = lax.all_to_all(send_data, ("gx", "gy"), split_axis=0, concat_axis=0, tiled=True)
    halos = (
        shift(outgoing[0], "gx", 1),
        shift(outgoing[1], "gx", -1),
        shift(outgoing[2], "gy", 1),
        shift(outgoing[3], "gy", -1),
    )
    got_tags = got[:, CAP + 2, ring : ring + CAP].reshape(tiles * CAP)
    row_table = (
        got_tags[None, :] == (jnp.arange(rows_x, dtype=jnp.int32) + 1).astype(jnp.float32)[:, None]
    ).astype(jnp.float32)
    increment = jnp.dot(
        row_table,
        got[:, :CAP].reshape(tiles * CAP, fields * cols_y),
        precision=lax.Precision.HIGHEST,
        preferred_element_type=jnp.float32,
    )
    edges_sum = jnp.sum(got[:, CAP:], axis=0)
    packed = jnp.concatenate([increment, edges_sum], 0)
    packed = lax.ppermute(packed, "comp", [(c, sections - 1 - c) for c in range(sections)])
    inc = (packed,)

    middle, last_rows, first_rows, last_cols, first_cols = run_step(
        adjoint, halos, halos, east, north, coeffs, wet, inc=inc, emit=True
    )
    step_halos = (
        shift(last_rows, "gx", 1),
        shift(first_rows, "gx", -1),
        shift(last_cols, "gy", 1),
        shift(first_cols, "gy", -1),
    )
    (result,) = run_step(middle, step_halos, halos, east, north, coeffs, wet)
    return result[None]


def solution(mesh):
    placed = (
        P("comp", None, None, "gx", "gy"),
        P("comp", None, "gx", "gy"),
        P("comp", None, "gx", "gy"),
        P("comp", None, None, "gx", "gy"),
        P("comp", "gx", "gy"),
        P("comp", "gx", "gy", None, None),
        P("comp", "gx", "gy", None),
        P("comp", "gx", "gy", None),
        P("comp", "gx", "gy", None, None),
    )
    return jax.shard_map(
        shards,
        mesh=mesh,
        in_specs=placed,
        out_specs=P("comp", None, None, "gx", "gy"),
        check_vma=False,
    )
```

```python
import jax
import jax.numpy as jnp
from jax import lax
from jax.experimental import pallas as pl
from jax.experimental.pallas import tpu as pltpu
from jax.sharding import PartitionSpec as P

CAP = 4


diffusion = 0.2


def shift(block, axis, step):
    count = lax.axis_size(axis)
    route = [(i, i + step) for i in range(count) if 0 <= i + step < count]
    return lax.ppermute(block, axis, route)


def step_kernel(fields, levels, rows, cols, coupled, emit):
    planes = fields * levels

    def kernel(*refs):
        refs = list(refs)
        a_ref, up_ref, dn_ref, lf_ref, rt_ref, cu_ref, cd_ref, cl_ref, cr_ref = refs[:9]
        ue_ref, un_ref, k_ref, wet_ref = refs[9:13]
        refs = refs[13:]
        if coupled:
            inc_ref = refs.pop(0)
        out_ref = refs.pop(0)
        if emit:
            eu_ref, ed_ref, el_ref, er_ref = refs[:4]
            refs = refs[4:]
        c_ref = refs[0]
        row = lax.broadcasted_iota(jnp.int32, (rows, cols), 0)
        col = lax.broadcasted_iota(jnp.int32, (rows, cols), 1)
        top = row == 0
        bottom = row == rows - 1
        left = col == 0
        right = col == cols - 1
        cprev = [None] * fields
        dprev = [None] * fields
        if coupled:
            side = jnp.broadcast_to(inc_ref[pl.ds(rows + 2, 1), :], (rows, fields * cols))
            place = lax.broadcasted_iota(jnp.int32, (rows, fields * cols), 1)
            owner = lax.broadcasted_iota(jnp.int32, (rows, fields * cols), 0) * (2 * fields)
            inc_cols = [
                jnp.sum(jnp.where(place == owner + c, side, 0.0), axis=1, keepdims=True)
                for c in range(2 * fields)
            ]
        for l in range(levels):
            ue = ue_ref[l]
            un = un_ref[l]
            ci = planes + l
            ue_m = jnp.where(top, cu_ref[pl.ds(ci, 1), :], pltpu.roll(ue, 1, 0))
            ue_p = jnp.where(bottom, cd_ref[pl.ds(ci, 1), :], pltpu.roll(ue, rows - 1, 0))
            un_m = jnp.where(left, cl_ref[:, pl.ds(ci, 1)], pltpu.roll(un, 1, 1))
            un_p = jnp.where(right, cr_ref[:, pl.ds(ci, 1)], pltpu.roll(un, cols - 1, 1))
            for f in range(fields):
                k = f * levels + l
                a = a_ref[f, l]
                up = up_ref[pl.ds(k, 1), :]
                dn = dn_ref[pl.ds(k, 1), :]
                lf = lf_ref[:, pl.ds(k, 1)]
                rt = rt_ref[:, pl.ds(k, 1)]
                if coupled and l == 0:
                    lanes = pl.ds(f * cols, cols)
                    a = a + inc_ref[pl.ds(0, rows), lanes]
                    up = up + inc_ref[pl.ds(rows, 1), lanes]
                    dn = dn + inc_ref[pl.ds(rows + 1, 1), lanes]
                    lf = lf + inc_cols[f]
                    rt = rt + inc_cols[fields + f]
                a_im = jnp.where(top, up, pltpu.roll(a, 1, 0))
                a_ip = jnp.where(bottom, dn, pltpu.roll(a, rows - 1, 0))
                a_jm = jnp.where(left, lf, pltpu.roll(a, 1, 1))
                a_jp = jnp.where(right, rt, pltpu.roll(a, cols - 1, 1))
                laplace = a_ip + a_im + a_jp + a_jm - 4.0 * a
                advect = 0.5 * (ue_m * a_im - ue_p * a_ip) + 0.5 * (un_m * a_jm - un_p * a_jp)
                h = a + diffusion * laplace + advect
                if l < levels - 1:
                    kd = k_ref[f, l]
                    diagonal = 1.0 + kd
                else:
                    diagonal = 1.0
                if l > 0:
                    kp = k_ref[f, l - 1]
                    divisor = diagonal + kp + kp * cprev[f]
                    numerator = h + kp * dprev[f]
                else:
                    divisor = diagonal
                    numerator = h
                if l < levels - 1:
                    cprev[f] = -kd / divisor
                    c_ref[f, l] = cprev[f]
                dprev[f] = numerator / divisor
                out_ref[f, l] = dprev[f]
        wet = wet_ref[...]
        if emit:
            sub = lax.broadcasted_iota(jnp.int32, (8, cols), 0)
            lane = lax.broadcasted_iota(jnp.int32, (rows, planes), 1)
            last_cols = jnp.zeros((rows, planes), jnp.float32)
            first_cols = jnp.zeros((rows, planes), jnp.float32)
            last_rows = jnp.zeros((8, cols), jnp.float32)
            first_rows = jnp.zeros((8, cols), jnp.float32)
        for f in range(fields):
            r = dprev[f]
            for l in range(levels - 1, -1, -1):
                if l < levels - 1:
                    r = out_ref[f, l] - c_ref[f, l] * r
                v = r * wet
                out_ref[f, l] = v
                if emit:
                    k = f * levels + l
                    last_rows = jnp.where(sub == k % 8, v[rows - 1 : rows, :], last_rows)
                    first_rows = jnp.where(sub == k % 8, v[0:1, :], first_rows)
                    last_cols = jnp.where(lane == k, v[:, cols - 1 : cols], last_cols)
                    first_cols = jnp.where(lane == k, v[:, 0:1], first_cols)
                    if k % 8 == 0:
                        eu_ref[pl.ds(k, 8), :] = last_rows
                        ed_ref[pl.ds(k, 8), :] = first_rows
        if emit:
            el_ref[...] = last_cols
            er_ref[...] = first_cols

    return kernel


def run_step(a, halos, coef_halos, ue, un, coeffs, wet, inc=None, emit=False):
    fields, levels, rows, cols = a.shape
    planes = fields * levels
    coupled = inc is not None
    operands = [a, *halos, *coef_halos, ue, un, coeffs, wet]
    if coupled:
        operands += list(inc)
    shapes = [jax.ShapeDtypeStruct(a.shape, jnp.float32)]
    if emit:
        shapes += [jax.ShapeDtypeStruct((planes, cols), jnp.float32)] * 2
        shapes += [jax.ShapeDtypeStruct((rows, planes), jnp.float32)] * 2
    return pl.pallas_call(
        step_kernel(fields, levels, rows, cols, coupled, emit),
        out_shape=shapes,
        scratch_shapes=[pltpu.VMEM(a.shape, jnp.float32)],
    )(*operands)


def shards(
    adjoint_in, u_east, u_north, diffusivity, wet_mask, dest_tile, src_row, dst_row, area_weight
):
    adjoint = adjoint_in[0]
    fields, levels, rows_x, cols_y = adjoint.shape
    planes = fields * levels
    sections = lax.axis_size("comp")
    tiles_x = lax.axis_size("gx")
    tiles_y = lax.axis_size("gy")
    tiles = tiles_x * tiles_y
    section = lax.axis_index("comp")
    east = u_east[0]
    north = u_north[0]
    coeffs = diffusivity[0]
    wet = wet_mask[0].astype(jnp.float32)

    def row_edge(index):
        field_rows = adjoint[:, :, index, :].reshape(planes, cols_y)
        return jnp.concatenate([field_rows, east[:, index, :]], 0)

    def col_edge(index):
        field_cols = jnp.transpose(adjoint[:, :, :, index], (2, 0, 1)).reshape(rows_x, planes)
        return jnp.concatenate([field_cols, north[:, :, index].T], 1)


    targets = dest_tile[0, 0, 0, :, 0]
    sources = src_row[0, 0, 0]
    landing = dst_row[0, 0, 0]
    weights = area_weight[0, 0, 0]
    count = targets.shape[0]
    surface_rows = jnp.transpose(adjoint[:, 0], (1, 0, 2)).reshape(rows_x, fields * cols_y)
    pick_table = (sources[:, None] == jnp.arange(rows_x, dtype=jnp.int32)[None, :]).astype(
        jnp.float32
    )
    payload = jnp.sum(jnp.where(pick_table[:, :, None] > 0, surface_rows[None], 0.0), axis=1)
    payload = (payload.reshape(count, fields, cols_y) * weights[:, None, :]).reshape(
        count, fields * cols_y
    )
    keys = targets * rows_x + landing
    placing = (
        keys[None, :] == jnp.arange(tiles * rows_x, dtype=jnp.int32)[:, None]
    ).astype(jnp.float32)
    summed = jnp.dot(
        placing, payload, precision=lax.Precision.HIGHEST, preferred_element_type=jnp.float32
    ).reshape(tiles_x, tiles_y, rows_x, fields, cols_y)
    order_ids = jnp.arange(count, dtype=jnp.int32)
    earlier = (targets[:, None] == targets[None, :]) & (order_ids[None, :] < order_ids[:, None])
    rank_in = jnp.sum(earlier.astype(jnp.int32), axis=1)
    slot_ids = targets * CAP + rank_in
    slotting = slot_ids[None, :] == jnp.arange(tiles * CAP, dtype=jnp.int32)[:, None]
    slots = jnp.dot(
        slotting.astype(jnp.float32),
        payload,
        precision=lax.Precision.HIGHEST,
        preferred_element_type=jnp.float32,
    ).reshape(tiles, CAP, fields * cols_y)
    tags = jnp.sum(slotting.astype(jnp.int32) * (landing + 1)[None, :], axis=1)
    tags = tags.astype(jnp.float32).reshape(tiles_x, tiles_y, CAP)
    zero_x = jnp.zeros((1, tiles_y, fields, cols_y), jnp.float32)
    up_rows = jnp.concatenate([zero_x, summed[:-1, :, rows_x - 1]], 0)
    dn_rows = jnp.concatenate([summed[1:, :, 0], zero_x], 0)
    zero_y = jnp.zeros((tiles_x, 1, rows_x, fields), jnp.float32)
    lf_cols = jnp.concatenate([zero_y, summed[:, :-1, :, :, cols_y - 1]], 1)
    rt_cols = jnp.concatenate([summed[:, 1:, :, :, 0], zero_y], 1)
    ring = 2 * rows_x * fields
    side = jnp.concatenate([lf_cols, rt_cols], 3).reshape(tiles_x, tiles_y, ring)
    side = jnp.concatenate([side, tags], 2)
    side = jnp.pad(side, ((0, 0), (0, 0), (0, fields * cols_y - ring - CAP)))
    send_data = jnp.concatenate(
        [
            slots,
            up_rows.reshape(tiles, 1, fields * cols_y),
            dn_rows.reshape(tiles, 1, fields * cols_y),
            side.reshape(tiles, 1, fields * cols_y),
        ],
        1,
    )
    send_data, *outgoing = lax.optimization_barrier(
        (send_data, row_edge(rows_x - 1), row_edge(0), col_edge(cols_y - 1), col_edge(0))
    )
    got = lax.all_to_all(send_data, ("gx", "gy"), split_axis=0, concat_axis=0, tiled=True)
    halos = (
        shift(outgoing[0], "gx", 1),
        shift(outgoing[1], "gx", -1),
        shift(outgoing[2], "gy", 1),
        shift(outgoing[3], "gy", -1),
    )
    got_tags = got[:, CAP + 2, ring : ring + CAP].reshape(tiles * CAP)
    row_table = (
        got_tags[None, :] == (jnp.arange(rows_x, dtype=jnp.int32) + 1).astype(jnp.float32)[:, None]
    ).astype(jnp.float32)
    increment = jnp.dot(
        row_table,
        got[:, :CAP].reshape(tiles * CAP, fields * cols_y),
        precision=lax.Precision.HIGHEST,
        preferred_element_type=jnp.float32,
    )
    edges_sum = jnp.sum(got[:, CAP:], axis=0)
    packed = jnp.concatenate([increment, edges_sum], 0)
    packed = lax.ppermute(packed, "comp", [(c, sections - 1 - c) for c in range(sections)])
    inc = (packed,)

    middle, last_rows, first_rows, last_cols, first_cols = run_step(
        adjoint, halos, halos, east, north, coeffs, wet, inc=inc, emit=True
    )
    step_halos = (
        shift(last_rows, "gx", 1),
        shift(first_rows, "gx", -1),
        shift(last_cols, "gy", 1),
        shift(first_cols, "gy", -1),
    )
    (result,) = run_step(middle, step_halos, halos, east, north, coeffs, wet)
    return result[None]


def solution(mesh):
    placed = (
        P("comp", None, None, "gx", "gy"),
        P("comp", None, "gx", "gy"),
        P("comp", None, "gx", "gy"),
        P("comp", None, None, "gx", "gy"),
        P("comp", "gx", "gy"),
        P("comp", "gx", "gy", None, None),
        P("comp", "gx", "gy", None),
        P("comp", "gx", "gy", None),
        P("comp", "gx", "gy", None, None),
    )
    return jax.shard_map(
        shards,
        mesh=mesh,
        in_specs=placed,
        out_specs=P("comp", None, None, "gx", "gy"),
        check_vma=False,
    )
```

```python
import jax
import jax.numpy as jnp
from jax import lax
from jax.experimental import pallas as pl
from jax.experimental.pallas import tpu as pltpu
from jax.sharding import PartitionSpec as P

CAP = 4


diffusion = 0.2


def shift(block, axis, step):
    count = lax.axis_size(axis)
    route = [(i, i + step) for i in range(count) if 0 <= i + step < count]
    return lax.ppermute(block, axis, route)


def step_kernel(fields, levels, rows, cols, coupled, emit):
    planes = fields * levels

    def kernel(*refs):
        refs = list(refs)
        a_ref, up_ref, dn_ref, lf_ref, rt_ref, cu_ref, cd_ref, cl_ref, cr_ref = refs[:9]
        ue_ref, un_ref, k_ref, wet_ref = refs[9:13]
        refs = refs[13:]
        if coupled:
            inc_ref = refs.pop(0)
        out_ref = refs.pop(0)
        if emit:
            eu_ref, ed_ref, el_ref, er_ref = refs[:4]
            refs = refs[4:]
        c_ref = refs[0]
        row = lax.broadcasted_iota(jnp.int32, (rows, cols), 0)
        col = lax.broadcasted_iota(jnp.int32, (rows, cols), 1)
        top = row == 0
        bottom = row == rows - 1
        left = col == 0
        right = col == cols - 1
        cprev = [None] * fields
        dprev = [None] * fields
        if coupled:
            side = jnp.broadcast_to(inc_ref[pl.ds(rows + 2, 1), :], (rows, fields * cols))
            place = lax.broadcasted_iota(jnp.int32, (rows, fields * cols), 1)
            owner = lax.broadcasted_iota(jnp.int32, (rows, fields * cols), 0) * (2 * fields)
            inc_cols = [
                jnp.sum(jnp.where(place == owner + c, side, 0.0), axis=1, keepdims=True)
                for c in range(2 * fields)
            ]
        for l in range(levels):
            ue = ue_ref[l]
            un = un_ref[l]
            ci = planes + l
            ue_m = jnp.where(top, cu_ref[pl.ds(ci, 1), :], pltpu.roll(ue, 1, 0))
            ue_p = jnp.where(bottom, cd_ref[pl.ds(ci, 1), :], pltpu.roll(ue, rows - 1, 0))
            un_m = jnp.where(left, cl_ref[:, pl.ds(ci, 1)], pltpu.roll(un, 1, 1))
            un_p = jnp.where(right, cr_ref[:, pl.ds(ci, 1)], pltpu.roll(un, cols - 1, 1))
            for f in range(fields):
                k = f * levels + l
                a = a_ref[f, l]
                up = up_ref[pl.ds(k, 1), :]
                dn = dn_ref[pl.ds(k, 1), :]
                lf = lf_ref[:, pl.ds(k, 1)]
                rt = rt_ref[:, pl.ds(k, 1)]
                if coupled and l == 0:
                    lanes = pl.ds(f * cols, cols)
                    a = a + inc_ref[pl.ds(0, rows), lanes]
                    up = up + inc_ref[pl.ds(rows, 1), lanes]
                    dn = dn + inc_ref[pl.ds(rows + 1, 1), lanes]
                    lf = lf + inc_cols[f]
                    rt = rt + inc_cols[fields + f]
                a_im = jnp.where(top, up, pltpu.roll(a, 1, 0))
                a_ip = jnp.where(bottom, dn, pltpu.roll(a, rows - 1, 0))
                a_jm = jnp.where(left, lf, pltpu.roll(a, 1, 1))
                a_jp = jnp.where(right, rt, pltpu.roll(a, cols - 1, 1))
                laplace = a_ip + a_im + a_jp + a_jm - 4.0 * a
                advect = 0.5 * (ue_m * a_im - ue_p * a_ip) + 0.5 * (un_m * a_jm - un_p * a_jp)
                h = a + diffusion * laplace + advect
                if l < levels - 1:
                    kd = k_ref[f, l]
                    diagonal = 1.0 + kd
                else:
                    diagonal = 1.0
                if l > 0:
                    kp = k_ref[f, l - 1]
                    divisor = diagonal + kp + kp * cprev[f]
                    numerator = h + kp * dprev[f]
                else:
                    divisor = diagonal
                    numerator = h
                if l < levels - 1:
                    cprev[f] = -kd / divisor
                    c_ref[f, l] = cprev[f]
                dprev[f] = numerator / divisor
                out_ref[f, l] = dprev[f]
        wet = wet_ref[...]
        if emit:
            sub = lax.broadcasted_iota(jnp.int32, (8, cols), 0)
            lane = lax.broadcasted_iota(jnp.int32, (rows, planes), 1)
            last_cols = jnp.zeros((rows, planes), jnp.float32)
            first_cols = jnp.zeros((rows, planes), jnp.float32)
            last_rows = jnp.zeros((8, cols), jnp.float32)
            first_rows = jnp.zeros((8, cols), jnp.float32)
        for f in range(fields):
            r = dprev[f]
            for l in range(levels - 1, -1, -1):
                if l < levels - 1:
                    r = out_ref[f, l] - c_ref[f, l] * r
                v = r * wet
                out_ref[f, l] = v
                if emit:
                    k = f * levels + l
                    last_rows = jnp.where(sub == k % 8, v[rows - 1 : rows, :], last_rows)
                    first_rows = jnp.where(sub == k % 8, v[0:1, :], first_rows)
                    last_cols = jnp.where(lane == k, v[:, cols - 1 : cols], last_cols)
                    first_cols = jnp.where(lane == k, v[:, 0:1], first_cols)
                    if k % 8 == 0:
                        eu_ref[pl.ds(k, 8), :] = last_rows
                        ed_ref[pl.ds(k, 8), :] = first_rows
        if emit:
            el_ref[...] = last_cols
            er_ref[...] = first_cols

    return kernel


def run_step(a, halos, coef_halos, ue, un, coeffs, wet, inc=None, emit=False):
    fields, levels, rows, cols = a.shape
    planes = fields * levels
    coupled = inc is not None
    operands = [a, *halos, *coef_halos, ue, un, coeffs, wet]
    if coupled:
        operands += list(inc)
    shapes = [jax.ShapeDtypeStruct(a.shape, jnp.float32)]
    if emit:
        shapes += [jax.ShapeDtypeStruct((planes, cols), jnp.float32)] * 2
        shapes += [jax.ShapeDtypeStruct((rows, planes), jnp.float32)] * 2
    return pl.pallas_call(
        step_kernel(fields, levels, rows, cols, coupled, emit),
        out_shape=shapes,
        scratch_shapes=[pltpu.VMEM(a.shape, jnp.float32)],
    )(*operands)


def shards(
    adjoint_in, u_east, u_north, diffusivity, wet_mask, dest_tile, src_row, dst_row, area_weight
):
    adjoint = adjoint_in[0]
    fields, levels, rows_x, cols_y = adjoint.shape
    planes = fields * levels
    sections = lax.axis_size("comp")
    tiles_x = lax.axis_size("gx")
    tiles_y = lax.axis_size("gy")
    tiles = tiles_x * tiles_y
    section = lax.axis_index("comp")
    east = u_east[0]
    north = u_north[0]
    coeffs = diffusivity[0]
    wet = wet_mask[0].astype(jnp.float32)

    def row_edge(index):
        field_rows = adjoint[:, :, index, :].reshape(planes, cols_y)
        return jnp.concatenate([field_rows, east[:, index, :]], 0)

    def col_edge(index):
        field_cols = jnp.transpose(adjoint[:, :, :, index], (2, 0, 1)).reshape(rows_x, planes)
        return jnp.concatenate([field_cols, north[:, :, index].T], 1)


    targets = dest_tile[0, 0, 0, :, 0]
    sources = src_row[0, 0, 0]
    landing = dst_row[0, 0, 0]
    weights = area_weight[0, 0, 0]
    count = targets.shape[0]
    surface_rows = jnp.transpose(adjoint[:, 0], (1, 0, 2)).reshape(rows_x, fields * cols_y)
    pick_table = (sources[:, None] == jnp.arange(rows_x, dtype=jnp.int32)[None, :]).astype(
        jnp.float32
    )
    payload = jnp.dot(
        pick_table,
        surface_rows,
        precision=lax.Precision.HIGHEST,
        preferred_element_type=jnp.float32,
    )
    payload = (payload.reshape(count, fields, cols_y) * weights[:, None, :]).reshape(
        count, fields * cols_y
    )
    order_ids = jnp.arange(count, dtype=jnp.int32)
    earlier = (targets[:, None] == targets[None, :]) & (order_ids[None, :] < order_ids[:, None])
    rank_in = jnp.sum(earlier.astype(jnp.int32), axis=1)
    width = fields * cols_y
    ring = 2 * rows_x * fields
    depth = CAP + 3
    lane = jnp.arange(width, dtype=jnp.int32)[None, :]
    lf_part = sum(
        jnp.where(lane == (landing * 2 * fields + f)[:, None], payload[:, f * cols_y + cols_y - 1][:, None], 0.0)
        for f in range(fields)
    )
    rt_part = sum(
        jnp.where(lane == (landing * 2 * fields + fields + f)[:, None], payload[:, f * cols_y][:, None], 0.0)
        for f in range(fields)
    )
    tag_part = jnp.where(
        lane == (ring + rank_in)[:, None], (landing + 1).astype(jnp.float32)[:, None], 0.0
    )
    sources_all = jnp.concatenate([payload, lf_part, rt_part, tag_part], 0)
    chunk_row = jnp.arange(tiles * depth, dtype=jnp.int32)[:, None]
    tile_of = chunk_row // depth
    part = chunk_row % depth
    column_of = tile_of % tiles_y
    to = targets[None, :]
    blocks = (
        ((part < CAP) & (to == tile_of) & (rank_in[None, :] == part))
        | ((part == CAP) & (to == tile_of - tiles_y) & (landing[None, :] == rows_x - 1))
        | ((part == CAP + 1) & (to == tile_of + tiles_y) & (landing[None, :] == 0))
    )
    side_row = part == CAP + 2
    lf_route = side_row & (to == tile_of - 1) & (column_of > 0)
    rt_route = side_row & (to == tile_of + 1) & (column_of < tiles_y - 1)
    tag_route = side_row & (to == tile_of)
    routing = jnp.concatenate([blocks, lf_route, rt_route, tag_route], 1).astype(jnp.float32)
    send_data = jnp.dot(
        routing, sources_all, precision=lax.Precision.HIGHEST, preferred_element_type=jnp.float32
    ).reshape(tiles, depth, width)
    send_data, *outgoing = lax.optimization_barrier(
        (send_data, row_edge(rows_x - 1), row_edge(0), col_edge(cols_y - 1), col_edge(0))
    )
    got = lax.all_to_all(send_data, ("gx", "gy"), split_axis=0, concat_axis=0, tiled=True)
    halos = (
        shift(outgoing[0], "gx", 1),
        shift(outgoing[1], "gx", -1),
        shift(outgoing[2], "gy", 1),
        shift(outgoing[3], "gy", -1),
    )
    got_tags = got[:, CAP + 2, ring : ring + CAP].reshape(tiles * CAP)
    row_table = (
        got_tags[None, :] == (jnp.arange(rows_x, dtype=jnp.int32) + 1).astype(jnp.float32)[:, None]
    ).astype(jnp.float32)
    increment = jnp.dot(
        row_table,
        got[:, :CAP].reshape(tiles * CAP, fields * cols_y),
        precision=lax.Precision.HIGHEST,
        preferred_element_type=jnp.float32,
    )
    edges_sum = jnp.sum(got[:, CAP:], axis=0)
    packed = jnp.concatenate([increment, edges_sum], 0)
    packed = lax.ppermute(packed, "comp", [(c, sections - 1 - c) for c in range(sections)])
    inc = (packed,)

    middle, last_rows, first_rows, last_cols, first_cols = run_step(
        adjoint, halos, halos, east, north, coeffs, wet, inc=inc, emit=True
    )
    step_halos = (
        shift(last_rows, "gx", 1),
        shift(first_rows, "gx", -1),
        shift(last_cols, "gy", 1),
        shift(first_cols, "gy", -1),
    )
    (result,) = run_step(middle, step_halos, halos, east, north, coeffs, wet)
    return result[None]


def solution(mesh):
    placed = (
        P("comp", None, None, "gx", "gy"),
        P("comp", None, "gx", "gy"),
        P("comp", None, "gx", "gy"),
        P("comp", None, None, "gx", "gy"),
        P("comp", "gx", "gy"),
        P("comp", "gx", "gy", None, None),
        P("comp", "gx", "gy", None),
        P("comp", "gx", "gy", None),
        P("comp", "gx", "gy", None, None),
    )
    return jax.shard_map(
        shards,
        mesh=mesh,
        in_specs=placed,
        out_specs=P("comp", None, None, "gx", "gy"),
        check_vma=False,
    )
```

```python
import jax
import jax.numpy as jnp
from jax import lax
from jax.experimental import pallas as pl
from jax.experimental.pallas import tpu as pltpu
from jax.sharding import PartitionSpec as P

CAP = 4


diffusion = 0.2


def shift(block, axis, step):
    count = lax.axis_size(axis)
    route = [(i, i + step) for i in range(count) if 0 <= i + step < count]
    return lax.ppermute(block, axis, route)


def step_kernel(fields, levels, rows, cols, coupled, emit):
    planes = fields * levels

    def kernel(*refs):
        refs = list(refs)
        a_ref, up_ref, dn_ref, lf_ref, rt_ref, cu_ref, cd_ref, cl_ref, cr_ref = refs[:9]
        ue_ref, un_ref, k_ref, wet_ref = refs[9:13]
        refs = refs[13:15] + refs[15:]
        chain = refs[:2]
        refs = refs[2:]
        if coupled:
            inc_ref = refs.pop(0)
        out_ref = refs.pop(0)
        if emit:
            eu_ref, ed_ref, el_ref, er_ref = refs[:4]
            refs = refs[4:]
        c_ref, inv_ref = chain
        row = lax.broadcasted_iota(jnp.int32, (rows, cols), 0)
        col = lax.broadcasted_iota(jnp.int32, (rows, cols), 1)
        top = row == 0
        bottom = row == rows - 1
        left = col == 0
        right = col == cols - 1
        cprev = [None] * fields
        dprev = [None] * fields
        if coupled:
            side = jnp.broadcast_to(inc_ref[pl.ds(rows + 2, 1), :], (rows, fields * cols))
            place = lax.broadcasted_iota(jnp.int32, (rows, fields * cols), 1)
            owner = lax.broadcasted_iota(jnp.int32, (rows, fields * cols), 0) * (2 * fields)
            inc_cols = [
                jnp.sum(jnp.where(place == owner + c, side, 0.0), axis=1, keepdims=True)
                for c in range(2 * fields)
            ]
        for l in range(levels):
            ue = ue_ref[l]
            un = un_ref[l]
            ci = planes + l
            ue_m = jnp.where(top, cu_ref[pl.ds(ci, 1), :], pltpu.roll(ue, 1, 0))
            ue_p = jnp.where(bottom, cd_ref[pl.ds(ci, 1), :], pltpu.roll(ue, rows - 1, 0))
            un_m = jnp.where(left, cl_ref[:, pl.ds(ci, 1)], pltpu.roll(un, 1, 1))
            un_p = jnp.where(right, cr_ref[:, pl.ds(ci, 1)], pltpu.roll(un, cols - 1, 1))
            for f in range(fields):
                k = f * levels + l
                a = a_ref[f, l]
                up = up_ref[pl.ds(k, 1), :]
                dn = dn_ref[pl.ds(k, 1), :]
                lf = lf_ref[:, pl.ds(k, 1)]
                rt = rt_ref[:, pl.ds(k, 1)]
                if coupled and l == 0:
                    lanes = pl.ds(f * cols, cols)
                    a = a + inc_ref[pl.ds(0, rows), lanes]
                    up = up + inc_ref[pl.ds(rows, 1), lanes]
                    dn = dn + inc_ref[pl.ds(rows + 1, 1), lanes]
                    lf = lf + inc_cols[f]
                    rt = rt + inc_cols[fields + f]
                a_im = jnp.where(top, up, pltpu.roll(a, 1, 0))
                a_ip = jnp.where(bottom, dn, pltpu.roll(a, rows - 1, 0))
                a_jm = jnp.where(left, lf, pltpu.roll(a, 1, 1))
                a_jp = jnp.where(right, rt, pltpu.roll(a, cols - 1, 1))
                laplace = a_ip + a_im + a_jp + a_jm - 4.0 * a
                advect = 0.5 * (ue_m * a_im - ue_p * a_ip) + 0.5 * (un_m * a_jm - un_p * a_jp)
                h = a + diffusion * laplace + advect
                if l > 0:
                    numerator = h + k_ref[f, l - 1] * dprev[f]
                else:
                    numerator = h
                dprev[f] = numerator * inv_ref[f, l]
                out_ref[f, l] = dprev[f]
        wet = wet_ref[...]
        if emit:
            sub = lax.broadcasted_iota(jnp.int32, (8, cols), 0)
            lane = lax.broadcasted_iota(jnp.int32, (rows, planes), 1)
            last_cols = jnp.zeros((rows, planes), jnp.float32)
            first_cols = jnp.zeros((rows, planes), jnp.float32)
            last_rows = jnp.zeros((8, cols), jnp.float32)
            first_rows = jnp.zeros((8, cols), jnp.float32)
        for f in range(fields):
            r = dprev[f]
            for l in range(levels - 1, -1, -1):
                if l < levels - 1:
                    r = out_ref[f, l] - c_ref[f, l] * r
                v = r * wet
                out_ref[f, l] = v
                if emit:
                    k = f * levels + l
                    last_rows = jnp.where(sub == k % 8, v[rows - 1 : rows, :], last_rows)
                    first_rows = jnp.where(sub == k % 8, v[0:1, :], first_rows)
                    last_cols = jnp.where(lane == k, v[:, cols - 1 : cols], last_cols)
                    first_cols = jnp.where(lane == k, v[:, 0:1], first_cols)
                    if k % 8 == 0:
                        eu_ref[pl.ds(k, 8), :] = last_rows
                        ed_ref[pl.ds(k, 8), :] = first_rows
        if emit:
            el_ref[...] = last_cols
            er_ref[...] = first_cols

    return kernel


def chain_kernel(fields, levels):
    def kernel(k_ref, c_ref, inv_ref):
        cprev = [None] * fields
        for l in range(levels):
            for f in range(fields):
                if l < levels - 1:
                    kd = k_ref[f, l]
                    diagonal = 1.0 + kd
                else:
                    diagonal = 1.0
                if l > 0:
                    kp = k_ref[f, l - 1]
                    divisor = diagonal + kp + kp * cprev[f]
                else:
                    divisor = diagonal + jnp.zeros_like(k_ref[f, l])
                inverse = 1.0 / divisor
                inv_ref[f, l] = inverse
                if l < levels - 1:
                    cprev[f] = -kd * inverse
                    c_ref[f, l] = cprev[f]
                else:
                    c_ref[f, l] = jnp.zeros_like(inverse)

    return kernel


def sweep_chain(coeffs):
    fields, levels = coeffs.shape[:2]
    shape = jax.ShapeDtypeStruct(coeffs.shape, jnp.float32)
    return pl.pallas_call(chain_kernel(fields, levels), out_shape=[shape, shape])(coeffs)


def run_step(a, halos, coef_halos, ue, un, coeffs, wet, chain, inc=None, emit=False):
    fields, levels, rows, cols = a.shape
    planes = fields * levels
    coupled = inc is not None
    operands = [a, *halos, *coef_halos, ue, un, coeffs, wet, *chain]
    if coupled:
        operands += list(inc)
    shapes = [jax.ShapeDtypeStruct(a.shape, jnp.float32)]
    if emit:
        shapes += [jax.ShapeDtypeStruct((planes, cols), jnp.float32)] * 2
        shapes += [jax.ShapeDtypeStruct((rows, planes), jnp.float32)] * 2
    return pl.pallas_call(
        step_kernel(fields, levels, rows, cols, coupled, emit),
        out_shape=shapes,
    )(*operands)


def shards(
    adjoint_in, u_east, u_north, diffusivity, wet_mask, dest_tile, src_row, dst_row, area_weight
):
    adjoint = adjoint_in[0]
    fields, levels, rows_x, cols_y = adjoint.shape
    planes = fields * levels
    sections = lax.axis_size("comp")
    tiles_x = lax.axis_size("gx")
    tiles_y = lax.axis_size("gy")
    tiles = tiles_x * tiles_y
    section = lax.axis_index("comp")
    east = u_east[0]
    north = u_north[0]
    coeffs = diffusivity[0]
    wet = wet_mask[0].astype(jnp.float32)
    chain = sweep_chain(coeffs)

    def row_edge(index):
        field_rows = adjoint[:, :, index, :].reshape(planes, cols_y)
        return jnp.concatenate([field_rows, east[:, index, :]], 0)

    def col_edge(index):
        field_cols = jnp.transpose(adjoint[:, :, :, index], (2, 0, 1)).reshape(rows_x, planes)
        return jnp.concatenate([field_cols, north[:, :, index].T], 1)


    targets = dest_tile[0, 0, 0, :, 0]
    sources = src_row[0, 0, 0]
    landing = dst_row[0, 0, 0]
    weights = area_weight[0, 0, 0]
    count = targets.shape[0]
    surface_rows = jnp.transpose(adjoint[:, 0], (1, 0, 2)).reshape(rows_x, fields * cols_y)
    pick_table = (sources[:, None] == jnp.arange(rows_x, dtype=jnp.int32)[None, :]).astype(
        jnp.float32
    )
    payload = jnp.dot(
        pick_table,
        surface_rows,
        precision=lax.Precision.HIGHEST,
        preferred_element_type=jnp.float32,
    )
    payload = (payload.reshape(count, fields, cols_y) * weights[:, None, :]).reshape(
        count, fields * cols_y
    )
    keys = targets * rows_x + landing
    placing = (
        keys[None, :] == jnp.arange(tiles * rows_x, dtype=jnp.int32)[:, None]
    ).astype(jnp.float32)
    summed = jnp.dot(
        placing, payload, precision=lax.Precision.HIGHEST, preferred_element_type=jnp.float32
    ).reshape(tiles_x, tiles_y, rows_x, fields, cols_y)
    order_ids = jnp.arange(count, dtype=jnp.int32)
    earlier = (targets[:, None] == targets[None, :]) & (order_ids[None, :] < order_ids[:, None])
    rank_in = jnp.sum(earlier.astype(jnp.int32), axis=1)
    slot_ids = targets * CAP + rank_in
    slotting = slot_ids[None, :] == jnp.arange(tiles * CAP, dtype=jnp.int32)[:, None]
    slots = jnp.dot(
        slotting.astype(jnp.float32),
        payload,
        precision=lax.Precision.HIGHEST,
        preferred_element_type=jnp.float32,
    ).reshape(tiles, CAP, fields * cols_y)
    tags = jnp.sum(slotting.astype(jnp.int32) * (landing + 1)[None, :], axis=1)
    tags = tags.astype(jnp.float32).reshape(tiles_x, tiles_y, CAP)
    zero_x = jnp.zeros((1, tiles_y, fields, cols_y), jnp.float32)
    up_rows = jnp.concatenate([zero_x, summed[:-1, :, rows_x - 1]], 0)
    dn_rows = jnp.concatenate([summed[1:, :, 0], zero_x], 0)
    zero_y = jnp.zeros((tiles_x, 1, rows_x, fields), jnp.float32)
    lf_cols = jnp.concatenate([zero_y, summed[:, :-1, :, :, cols_y - 1]], 1)
    rt_cols = jnp.concatenate([summed[:, 1:, :, :, 0], zero_y], 1)
    ring = 2 * rows_x * fields
    side = jnp.concatenate([lf_cols, rt_cols], 3).reshape(tiles_x, tiles_y, ring)
    side = jnp.concatenate([side, tags], 2)
    side = jnp.pad(side, ((0, 0), (0, 0), (0, fields * cols_y - ring - CAP)))
    send_data = jnp.concatenate(
        [
            slots,
            up_rows.reshape(tiles, 1, fields * cols_y),
            dn_rows.reshape(tiles, 1, fields * cols_y),
            side.reshape(tiles, 1, fields * cols_y),
        ],
        1,
    )
    send_data, *outgoing = lax.optimization_barrier(
        (send_data, row_edge(rows_x - 1), row_edge(0), col_edge(cols_y - 1), col_edge(0))
    )
    got = lax.all_to_all(send_data, ("gx", "gy"), split_axis=0, concat_axis=0, tiled=True)
    halos = (
        shift(outgoing[0], "gx", 1),
        shift(outgoing[1], "gx", -1),
        shift(outgoing[2], "gy", 1),
        shift(outgoing[3], "gy", -1),
    )
    got_tags = got[:, CAP + 2, ring : ring + CAP].reshape(tiles * CAP)
    row_table = (
        got_tags[None, :] == (jnp.arange(rows_x, dtype=jnp.int32) + 1).astype(jnp.float32)[:, None]
    ).astype(jnp.float32)
    increment = jnp.dot(
        row_table,
        got[:, :CAP].reshape(tiles * CAP, fields * cols_y),
        precision=lax.Precision.HIGHEST,
        preferred_element_type=jnp.float32,
    )
    edges_sum = jnp.sum(got[:, CAP:], axis=0)
    packed = jnp.concatenate([increment, edges_sum], 0)
    packed = lax.ppermute(packed, "comp", [(c, sections - 1 - c) for c in range(sections)])
    inc = (packed,)

    middle, last_rows, first_rows, last_cols, first_cols = run_step(
        adjoint, halos, halos, east, north, coeffs, wet, chain, inc=inc, emit=True
    )
    step_halos = (
        shift(last_rows, "gx", 1),
        shift(first_rows, "gx", -1),
        shift(last_cols, "gy", 1),
        shift(first_cols, "gy", -1),
    )
    (result,) = run_step(middle, step_halos, halos, east, north, coeffs, wet, chain)
    return result[None]


def solution(mesh):
    placed = (
        P("comp", None, None, "gx", "gy"),
        P("comp", None, "gx", "gy"),
        P("comp", None, "gx", "gy"),
        P("comp", None, None, "gx", "gy"),
        P("comp", "gx", "gy"),
        P("comp", "gx", "gy", None, None),
        P("comp", "gx", "gy", None),
        P("comp", "gx", "gy", None),
        P("comp", "gx", "gy", None, None),
    )
    return jax.shard_map(
        shards,
        mesh=mesh,
        in_specs=placed,
        out_specs=P("comp", None, None, "gx", "gy"),
        check_vma=False,
    )
```

```python
import jax
import jax.numpy as jnp
from jax import lax
from jax.experimental import pallas as pl
from jax.experimental.pallas import tpu as pltpu
from jax.sharding import PartitionSpec as P

CAP = 4


diffusion = 0.2


def shift(block, axis, step):
    count = lax.axis_size(axis)
    route = [(i, i + step) for i in range(count) if 0 <= i + step < count]
    return lax.ppermute(block, axis, route)


def step_kernel(fields, levels, rows, cols, coupled, emit):
    planes = fields * levels

    def kernel(*refs):
        refs = list(refs)
        a_ref, up_ref, dn_ref, lf_ref, rt_ref, cu_ref, cd_ref, cl_ref, cr_ref = refs[:9]
        ue_ref, un_ref, k_ref, wet_ref = refs[9:13]
        refs = refs[13:]
        if coupled:
            inc_ref = refs.pop(0)
        out_ref = refs.pop(0)
        if emit:
            eu_ref, ed_ref, el_ref, er_ref = refs[:4]
            refs = refs[4:]
        c_ref = refs[0]
        row = lax.broadcasted_iota(jnp.int32, (rows, cols), 0)
        col = lax.broadcasted_iota(jnp.int32, (rows, cols), 1)
        top = row == 0
        bottom = row == rows - 1
        left = col == 0
        right = col == cols - 1
        cprev = [None] * fields
        dprev = [None] * fields
        if coupled:
            side = jnp.broadcast_to(inc_ref[pl.ds(rows + 2, 1), :], (rows, fields * cols))
            place = lax.broadcasted_iota(jnp.int32, (rows, fields * cols), 1)
            owner = lax.broadcasted_iota(jnp.int32, (rows, fields * cols), 0) * (2 * fields)
            inc_cols = [
                jnp.sum(jnp.where(place == owner + c, side, 0.0), axis=1, keepdims=True)
                for c in range(2 * fields)
            ]
        for l in range(levels):
            ue = ue_ref[l]
            un = un_ref[l]
            ci = planes + l
            ue_m = jnp.where(top, cu_ref[pl.ds(ci, 1), :], pltpu.roll(ue, 1, 0))
            ue_p = jnp.where(bottom, cd_ref[pl.ds(ci, 1), :], pltpu.roll(ue, rows - 1, 0))
            un_m = jnp.where(left, cl_ref[:, pl.ds(ci, 1)], pltpu.roll(un, 1, 1))
            un_p = jnp.where(right, cr_ref[:, pl.ds(ci, 1)], pltpu.roll(un, cols - 1, 1))
            for f in range(fields):
                k = f * levels + l
                a = a_ref[f, l]
                up = up_ref[pl.ds(k, 1), :]
                dn = dn_ref[pl.ds(k, 1), :]
                lf = lf_ref[:, pl.ds(k, 1)]
                rt = rt_ref[:, pl.ds(k, 1)]
                if coupled and l == 0:
                    lanes = pl.ds(f * cols, cols)
                    a = a + inc_ref[pl.ds(0, rows), lanes]
                    up = up + inc_ref[pl.ds(rows, 1), lanes]
                    dn = dn + inc_ref[pl.ds(rows + 1, 1), lanes]
                    lf = lf + inc_cols[f]
                    rt = rt + inc_cols[fields + f]
                a_im = jnp.where(top, up, pltpu.roll(a, 1, 0))
                a_ip = jnp.where(bottom, dn, pltpu.roll(a, rows - 1, 0))
                a_jm = jnp.where(left, lf, pltpu.roll(a, 1, 1))
                a_jp = jnp.where(right, rt, pltpu.roll(a, cols - 1, 1))
                laplace = a_ip + a_im + a_jp + a_jm - 4.0 * a
                advect = 0.5 * (ue_m * a_im - ue_p * a_ip) + 0.5 * (un_m * a_jm - un_p * a_jp)
                h = a + diffusion * laplace + advect
                if l < levels - 1:
                    kd = k_ref[f, l]
                    diagonal = 1.0 + kd
                else:
                    diagonal = 1.0
                if l > 0:
                    kp = k_ref[f, l - 1]
                    divisor = diagonal + kp + kp * cprev[f]
                    numerator = h + kp * dprev[f]
                else:
                    divisor = diagonal
                    numerator = h
                if l < levels - 1:
                    cprev[f] = -kd / divisor
                    c_ref[f, l] = cprev[f]
                dprev[f] = numerator / divisor
                out_ref[f, l] = dprev[f]
        wet = wet_ref[...]
        if emit:
            sub = lax.broadcasted_iota(jnp.int32, (8, cols), 0)
            lane = lax.broadcasted_iota(jnp.int32, (rows, planes), 1)
            last_cols = jnp.zeros((rows, planes), jnp.float32)
            first_cols = jnp.zeros((rows, planes), jnp.float32)
            last_rows = jnp.zeros((8, cols), jnp.float32)
            first_rows = jnp.zeros((8, cols), jnp.float32)
        for f in range(fields):
            r = dprev[f]
            for l in range(levels - 1, -1, -1):
                if l < levels - 1:
                    r = out_ref[f, l] - c_ref[f, l] * r
                v = r * wet
                out_ref[f, l] = v
                if emit:
                    k = f * levels + l
                    last_rows = jnp.where(sub == k % 8, v[rows - 1 : rows, :], last_rows)
                    first_rows = jnp.where(sub == k % 8, v[0:1, :], first_rows)
                    last_cols = jnp.where(lane == k, v[:, cols - 1 : cols], last_cols)
                    first_cols = jnp.where(lane == k, v[:, 0:1], first_cols)
                    if k % 8 == 0:
                        eu_ref[pl.ds(k, 8), :] = last_rows
                        ed_ref[pl.ds(k, 8), :] = first_rows
        if emit:
            el_ref[...] = last_cols
            er_ref[...] = first_cols

    return kernel


def fix_kernel(fields, levels, rows, cols):
    planes = fields * levels

    def kernel(z_ref, rt_ref, cr_ref, k_ref, wet_ref, out_ref, c_ref):
        col = lax.broadcasted_iota(jnp.int32, (rows, cols), 1)
        right = col == cols - 1
        cprev = [None] * fields
        dprev = [None] * fields
        for l in range(levels):
            un_p = cr_ref[:, pl.ds(planes + l, 1)]
            for f in range(fields):
                rt = rt_ref[:, pl.ds(f * levels + l, 1)]
                h = jnp.where(right, diffusion * rt - 0.5 * (un_p * rt), 0.0)
                if l < levels - 1:
                    kd = k_ref[f, l]
                    diagonal = 1.0 + kd
                else:
                    diagonal = 1.0
                if l > 0:
                    kp = k_ref[f, l - 1]
                    divisor = diagonal + kp + kp * cprev[f]
                    numerator = h + kp * dprev[f]
                else:
                    divisor = diagonal
                    numerator = h
                if l < levels - 1:
                    cprev[f] = -kd / divisor
                    c_ref[f, l] = cprev[f]
                dprev[f] = numerator / divisor
                out_ref[f, l] = dprev[f]
        wet = wet_ref[...]
        for f in range(fields):
            r = dprev[f]
            for l in range(levels - 1, -1, -1):
                if l < levels - 1:
                    r = out_ref[f, l] - c_ref[f, l] * r
                out_ref[f, l] = z_ref[f, l] + r * wet

    return kernel


def add_right_halo(z, rt, coef_rt, coeffs, wet):
    fields, levels, rows, cols = z.shape
    return pl.pallas_call(
        fix_kernel(fields, levels, rows, cols),
        out_shape=jax.ShapeDtypeStruct(z.shape, jnp.float32),
        scratch_shapes=[pltpu.VMEM(z.shape, jnp.float32)],
    )(z, rt, coef_rt, coeffs, wet)


def run_step(a, halos, coef_halos, ue, un, coeffs, wet, inc=None, emit=False):
    fields, levels, rows, cols = a.shape
    planes = fields * levels
    coupled = inc is not None
    operands = [a, *halos, *coef_halos, ue, un, coeffs, wet]
    if coupled:
        operands += list(inc)
    shapes = [jax.ShapeDtypeStruct(a.shape, jnp.float32)]
    if emit:
        shapes += [jax.ShapeDtypeStruct((planes, cols), jnp.float32)] * 2
        shapes += [jax.ShapeDtypeStruct((rows, planes), jnp.float32)] * 2
    return pl.pallas_call(
        step_kernel(fields, levels, rows, cols, coupled, emit),
        out_shape=shapes,
        scratch_shapes=[pltpu.VMEM(a.shape, jnp.float32)],
    )(*operands)


def shards(
    adjoint_in, u_east, u_north, diffusivity, wet_mask, dest_tile, src_row, dst_row, area_weight
):
    adjoint = adjoint_in[0]
    fields, levels, rows_x, cols_y = adjoint.shape
    planes = fields * levels
    sections = lax.axis_size("comp")
    tiles_x = lax.axis_size("gx")
    tiles_y = lax.axis_size("gy")
    tiles = tiles_x * tiles_y
    section = lax.axis_index("comp")
    east = u_east[0]
    north = u_north[0]
    coeffs = diffusivity[0]
    wet = wet_mask[0].astype(jnp.float32)

    def row_edge(index):
        field_rows = adjoint[:, :, index, :].reshape(planes, cols_y)
        return jnp.concatenate([field_rows, east[:, index, :]], 0)

    def col_edge(index):
        field_cols = jnp.transpose(adjoint[:, :, :, index], (2, 0, 1)).reshape(rows_x, planes)
        return jnp.concatenate([field_cols, north[:, :, index].T], 1)


    targets = dest_tile[0, 0, 0, :, 0]
    sources = src_row[0, 0, 0]
    landing = dst_row[0, 0, 0]
    weights = area_weight[0, 0, 0]
    count = targets.shape[0]
    surface_rows = jnp.transpose(adjoint[:, 0], (1, 0, 2)).reshape(rows_x, fields * cols_y)
    pick_table = (sources[:, None] == jnp.arange(rows_x, dtype=jnp.int32)[None, :]).astype(
        jnp.float32
    )
    payload = jnp.dot(
        pick_table,
        surface_rows,
        precision=lax.Precision.HIGHEST,
        preferred_element_type=jnp.float32,
    )
    payload = (payload.reshape(count, fields, cols_y) * weights[:, None, :]).reshape(
        count, fields * cols_y
    )
    keys = targets * rows_x + landing
    placing = (
        keys[None, :] == jnp.arange(tiles * rows_x, dtype=jnp.int32)[:, None]
    ).astype(jnp.float32)
    summed = jnp.dot(
        placing, payload, precision=lax.Precision.HIGHEST, preferred_element_type=jnp.float32
    ).reshape(tiles_x, tiles_y, rows_x, fields, cols_y)
    order_ids = jnp.arange(count, dtype=jnp.int32)
    earlier = (targets[:, None] == targets[None, :]) & (order_ids[None, :] < order_ids[:, None])
    rank_in = jnp.sum(earlier.astype(jnp.int32), axis=1)
    slot_ids = targets * CAP + rank_in
    slotting = slot_ids[None, :] == jnp.arange(tiles * CAP, dtype=jnp.int32)[:, None]
    slots = jnp.dot(
        slotting.astype(jnp.float32),
        payload,
        precision=lax.Precision.HIGHEST,
        preferred_element_type=jnp.float32,
    ).reshape(tiles, CAP, fields * cols_y)
    tags = jnp.sum(slotting.astype(jnp.int32) * (landing + 1)[None, :], axis=1)
    tags = tags.astype(jnp.float32).reshape(tiles_x, tiles_y, CAP)
    zero_x = jnp.zeros((1, tiles_y, fields, cols_y), jnp.float32)
    up_rows = jnp.concatenate([zero_x, summed[:-1, :, rows_x - 1]], 0)
    dn_rows = jnp.concatenate([summed[1:, :, 0], zero_x], 0)
    zero_y = jnp.zeros((tiles_x, 1, rows_x, fields), jnp.float32)
    lf_cols = jnp.concatenate([zero_y, summed[:, :-1, :, :, cols_y - 1]], 1)
    rt_cols = jnp.concatenate([summed[:, 1:, :, :, 0], zero_y], 1)
    ring = 2 * rows_x * fields
    side = jnp.concatenate([lf_cols, rt_cols], 3).reshape(tiles_x, tiles_y, ring)
    side = jnp.concatenate([side, tags], 2)
    side = jnp.pad(side, ((0, 0), (0, 0), (0, fields * cols_y - ring - CAP)))
    send_data = jnp.concatenate(
        [
            slots,
            up_rows.reshape(tiles, 1, fields * cols_y),
            dn_rows.reshape(tiles, 1, fields * cols_y),
            side.reshape(tiles, 1, fields * cols_y),
        ],
        1,
    )
    send_data, *outgoing = lax.optimization_barrier(
        (send_data, row_edge(rows_x - 1), row_edge(0), col_edge(cols_y - 1), col_edge(0))
    )
    got = lax.all_to_all(send_data, ("gx", "gy"), split_axis=0, concat_axis=0, tiled=True)
    halos = (
        shift(outgoing[0], "gx", 1),
        shift(outgoing[1], "gx", -1),
        shift(outgoing[2], "gy", 1),
        shift(outgoing[3], "gy", -1),
    )
    got_tags = got[:, CAP + 2, ring : ring + CAP].reshape(tiles * CAP)
    row_table = (
        got_tags[None, :] == (jnp.arange(rows_x, dtype=jnp.int32) + 1).astype(jnp.float32)[:, None]
    ).astype(jnp.float32)
    increment = jnp.dot(
        row_table,
        got[:, :CAP].reshape(tiles * CAP, fields * cols_y),
        precision=lax.Precision.HIGHEST,
        preferred_element_type=jnp.float32,
    )
    edges_sum = jnp.sum(got[:, CAP:], axis=0)
    packed = jnp.concatenate([increment, edges_sum], 0)
    packed = lax.ppermute(packed, "comp", [(c, sections - 1 - c) for c in range(sections)])
    inc = (packed,)

    middle, last_rows, first_rows, last_cols, first_cols = run_step(
        adjoint, halos, halos, east, north, coeffs, wet, inc=inc, emit=True
    )
    step_halos = (
        shift(last_rows, "gx", 1),
        shift(first_rows, "gx", -1),
        shift(last_cols, "gy", 1),
        shift(first_cols, "gy", -1),
    )
    partial_halos = step_halos[:3] + (jnp.zeros_like(step_halos[3]),)
    (partial,) = run_step(middle, partial_halos, halos, east, north, coeffs, wet)
    result = add_right_halo(partial, step_halos[3], halos[3], coeffs, wet)
    return result[None]


def solution(mesh):
    placed = (
        P("comp", None, None, "gx", "gy"),
        P("comp", None, "gx", "gy"),
        P("comp", None, "gx", "gy"),
        P("comp", None, None, "gx", "gy"),
        P("comp", "gx", "gy"),
        P("comp", "gx", "gy", None, None),
        P("comp", "gx", "gy", None),
        P("comp", "gx", "gy", None),
        P("comp", "gx", "gy", None, None),
    )
    return jax.shard_map(
        shards,
        mesh=mesh,
        in_specs=placed,
        out_specs=P("comp", None, None, "gx", "gy"),
        check_vma=False,
    )
```

```python
import jax
import jax.numpy as jnp
from jax import lax
from jax.experimental import pallas as pl
from jax.experimental.pallas import tpu as pltpu
from jax.sharding import PartitionSpec as P

CAP = 4


diffusion = 0.2


def shift(block, axis, step):
    count = lax.axis_size(axis)
    route = [(i, i + step) for i in range(count) if 0 <= i + step < count]
    return lax.ppermute(block, axis, route)


def step_kernel(fields, levels, rows, cols, coupled, emit, shared):
    planes = fields * levels

    def kernel(*refs):
        refs = list(refs)
        a_ref, up_ref, dn_ref, lf_ref, rt_ref = refs[:5]
        refs = refs[5:]
        if shared:
            cu_ref, cd_ref, cl_ref, cr_ref = up_ref, dn_ref, lf_ref, rt_ref
        else:
            cu_ref, cd_ref, cl_ref, cr_ref = refs[:4]
            refs = refs[4:]
        ue_ref, un_ref, k_ref, wet_ref = refs[:4]
        refs = refs[4:]
        if coupled:
            inc_ref = refs.pop(0)
        out_ref = refs.pop(0)
        if emit:
            eu_ref, ed_ref, el_ref, er_ref = refs[:4]
            refs = refs[4:]
        c_ref = refs[0]
        row = lax.broadcasted_iota(jnp.int32, (rows, cols), 0)
        col = lax.broadcasted_iota(jnp.int32, (rows, cols), 1)
        top = row == 0
        bottom = row == rows - 1
        left = col == 0
        right = col == cols - 1
        cprev = [None] * fields
        dprev = [None] * fields
        if coupled:
            side = jnp.broadcast_to(inc_ref[pl.ds(rows + 2, 1), :], (rows, fields * cols))
            place = lax.broadcasted_iota(jnp.int32, (rows, fields * cols), 1)
            owner = lax.broadcasted_iota(jnp.int32, (rows, fields * cols), 0) * (2 * fields)
            inc_cols = [
                jnp.sum(jnp.where(place == owner + c, side, 0.0), axis=1, keepdims=True)
                for c in range(2 * fields)
            ]
        for l in range(levels):
            ue = ue_ref[l]
            un = un_ref[l]
            ci = planes + l
            ue_m = jnp.where(top, cu_ref[pl.ds(ci, 1), :], pltpu.roll(ue, 1, 0))
            ue_p = jnp.where(bottom, cd_ref[pl.ds(ci, 1), :], pltpu.roll(ue, rows - 1, 0))
            un_m = jnp.where(left, cl_ref[:, pl.ds(ci, 1)], pltpu.roll(un, 1, 1))
            un_p = jnp.where(right, cr_ref[:, pl.ds(ci, 1)], pltpu.roll(un, cols - 1, 1))
            for f in range(fields):
                k = f * levels + l
                a = a_ref[f, l]
                up = up_ref[pl.ds(k, 1), :]
                dn = dn_ref[pl.ds(k, 1), :]
                lf = lf_ref[:, pl.ds(k, 1)]
                rt = rt_ref[:, pl.ds(k, 1)]
                if coupled and l == 0:
                    lanes = pl.ds(f * cols, cols)
                    a = a + inc_ref[pl.ds(0, rows), lanes]
                    up = up + inc_ref[pl.ds(rows, 1), lanes]
                    dn = dn + inc_ref[pl.ds(rows + 1, 1), lanes]
                    lf = lf + inc_cols[f]
                    rt = rt + inc_cols[fields + f]
                a_im = jnp.where(top, up, pltpu.roll(a, 1, 0))
                a_ip = jnp.where(bottom, dn, pltpu.roll(a, rows - 1, 0))
                a_jm = jnp.where(left, lf, pltpu.roll(a, 1, 1))
                a_jp = jnp.where(right, rt, pltpu.roll(a, cols - 1, 1))
                laplace = a_ip + a_im + a_jp + a_jm - 4.0 * a
                advect = 0.5 * (ue_m * a_im - ue_p * a_ip) + 0.5 * (un_m * a_jm - un_p * a_jp)
                h = a + diffusion * laplace + advect
                if l < levels - 1:
                    kd = k_ref[f, l]
                    diagonal = 1.0 + kd
                else:
                    diagonal = 1.0
                if l > 0:
                    kp = k_ref[f, l - 1]
                    divisor = diagonal + kp + kp * cprev[f]
                    numerator = h + kp * dprev[f]
                else:
                    divisor = diagonal
                    numerator = h
                if l < levels - 1:
                    cprev[f] = -kd / divisor
                    c_ref[f, l] = cprev[f]
                dprev[f] = numerator / divisor
                out_ref[f, l] = dprev[f]
        wet = wet_ref[...]
        if emit:
            sub = lax.broadcasted_iota(jnp.int32, (8, cols), 0)
            lane = lax.broadcasted_iota(jnp.int32, (rows, planes), 1)
            last_cols = jnp.zeros((rows, planes), jnp.float32)
            first_cols = jnp.zeros((rows, planes), jnp.float32)
            last_rows = jnp.zeros((8, cols), jnp.float32)
            first_rows = jnp.zeros((8, cols), jnp.float32)
        for f in range(fields):
            r = dprev[f]
            for l in range(levels - 1, -1, -1):
                if l < levels - 1:
                    r = out_ref[f, l] - c_ref[f, l] * r
                v = r * wet
                out_ref[f, l] = v
                if emit:
                    k = f * levels + l
                    last_rows = jnp.where(sub == k % 8, v[rows - 1 : rows, :], last_rows)
                    first_rows = jnp.where(sub == k % 8, v[0:1, :], first_rows)
                    last_cols = jnp.where(lane == k, v[:, cols - 1 : cols], last_cols)
                    first_cols = jnp.where(lane == k, v[:, 0:1], first_cols)
                    if k % 8 == 0:
                        eu_ref[pl.ds(k, 8), :] = last_rows
                        ed_ref[pl.ds(k, 8), :] = first_rows
        if emit:
            el_ref[...] = last_cols
            er_ref[...] = first_cols

    return kernel


def run_step(a, halos, coef_halos, ue, un, coeffs, wet, inc=None, emit=False):
    fields, levels, rows, cols = a.shape
    planes = fields * levels
    coupled = inc is not None
    shared = coef_halos is halos
    operands = [a, *halos, *([] if shared else coef_halos), ue, un, coeffs, wet]
    if coupled:
        operands += list(inc)
    shapes = [jax.ShapeDtypeStruct(a.shape, jnp.float32)]
    if emit:
        shapes += [jax.ShapeDtypeStruct((planes, cols), jnp.float32)] * 2
        shapes += [jax.ShapeDtypeStruct((rows, planes), jnp.float32)] * 2
    return pl.pallas_call(
        step_kernel(fields, levels, rows, cols, coupled, emit, shared),
        out_shape=shapes,
        scratch_shapes=[pltpu.VMEM(a.shape, jnp.float32)],
    )(*operands)


def shards(
    adjoint_in, u_east, u_north, diffusivity, wet_mask, dest_tile, src_row, dst_row, area_weight
):
    adjoint = adjoint_in[0]
    fields, levels, rows_x, cols_y = adjoint.shape
    planes = fields * levels
    sections = lax.axis_size("comp")
    tiles_x = lax.axis_size("gx")
    tiles_y = lax.axis_size("gy")
    tiles = tiles_x * tiles_y
    section = lax.axis_index("comp")
    east = u_east[0]
    north = u_north[0]
    coeffs = diffusivity[0]
    wet = wet_mask[0].astype(jnp.float32)

    def row_edge(index):
        field_rows = adjoint[:, :, index, :].reshape(planes, cols_y)
        return jnp.concatenate([field_rows, east[:, index, :]], 0)

    def col_edge(index):
        field_cols = jnp.transpose(adjoint[:, :, :, index], (2, 0, 1)).reshape(rows_x, planes)
        return jnp.concatenate([field_cols, north[:, :, index].T], 1)


    targets = dest_tile[0, 0, 0, :, 0]
    sources = src_row[0, 0, 0]
    landing = dst_row[0, 0, 0]
    weights = area_weight[0, 0, 0]
    count = targets.shape[0]
    surface_rows = jnp.transpose(adjoint[:, 0], (1, 0, 2)).reshape(rows_x, fields * cols_y)
    pick_table = (sources[:, None] == jnp.arange(rows_x, dtype=jnp.int32)[None, :]).astype(
        jnp.float32
    )
    payload = jnp.dot(
        pick_table,
        surface_rows,
        precision=lax.Precision.HIGHEST,
        preferred_element_type=jnp.float32,
    )
    payload = (payload.reshape(count, fields, cols_y) * weights[:, None, :]).reshape(
        count, fields * cols_y
    )
    keys = targets * rows_x + landing
    placing = (
        keys[None, :] == jnp.arange(tiles * rows_x, dtype=jnp.int32)[:, None]
    ).astype(jnp.float32)
    summed = jnp.dot(
        placing, payload, precision=lax.Precision.HIGHEST, preferred_element_type=jnp.float32
    ).reshape(tiles_x, tiles_y, rows_x, fields, cols_y)
    order_ids = jnp.arange(count, dtype=jnp.int32)
    earlier = (targets[:, None] == targets[None, :]) & (order_ids[None, :] < order_ids[:, None])
    rank_in = jnp.sum(earlier.astype(jnp.int32), axis=1)
    slot_ids = targets * CAP + rank_in
    slotting = slot_ids[None, :] == jnp.arange(tiles * CAP, dtype=jnp.int32)[:, None]
    slots = jnp.dot(
        slotting.astype(jnp.float32),
        payload,
        precision=lax.Precision.HIGHEST,
        preferred_element_type=jnp.float32,
    ).reshape(tiles, CAP, fields * cols_y)
    tags = jnp.sum(slotting.astype(jnp.int32) * (landing + 1)[None, :], axis=1)
    tags = tags.astype(jnp.float32).reshape(tiles_x, tiles_y, CAP)
    zero_x = jnp.zeros((1, tiles_y, fields, cols_y), jnp.float32)
    up_rows = jnp.concatenate([zero_x, summed[:-1, :, rows_x - 1]], 0)
    dn_rows = jnp.concatenate([summed[1:, :, 0], zero_x], 0)
    zero_y = jnp.zeros((tiles_x, 1, rows_x, fields), jnp.float32)
    lf_cols = jnp.concatenate([zero_y, summed[:, :-1, :, :, cols_y - 1]], 1)
    rt_cols = jnp.concatenate([summed[:, 1:, :, :, 0], zero_y], 1)
    ring = 2 * rows_x * fields
    side = jnp.concatenate([lf_cols, rt_cols], 3).reshape(tiles_x, tiles_y, ring)
    side = jnp.concatenate([side, tags], 2)
    side = jnp.pad(side, ((0, 0), (0, 0), (0, fields * cols_y - ring - CAP)))
    send_data = jnp.concatenate(
        [
            slots,
            up_rows.reshape(tiles, 1, fields * cols_y),
            dn_rows.reshape(tiles, 1, fields * cols_y),
            side.reshape(tiles, 1, fields * cols_y),
        ],
        1,
    )
    send_data, *outgoing = lax.optimization_barrier(
        (send_data, row_edge(rows_x - 1), row_edge(0), col_edge(cols_y - 1), col_edge(0))
    )
    got = lax.all_to_all(send_data, ("gx", "gy"), split_axis=0, concat_axis=0, tiled=True)
    halos = (
        shift(outgoing[0], "gx", 1),
        shift(outgoing[1], "gx", -1),
        shift(outgoing[2], "gy", 1),
        shift(outgoing[3], "gy", -1),
    )
    got_tags = got[:, CAP + 2, ring : ring + CAP].reshape(tiles * CAP)
    row_table = (
        got_tags[None, :] == (jnp.arange(rows_x, dtype=jnp.int32) + 1).astype(jnp.float32)[:, None]
    ).astype(jnp.float32)
    increment = jnp.dot(
        row_table,
        got[:, :CAP].reshape(tiles * CAP, fields * cols_y),
        precision=lax.Precision.HIGHEST,
        preferred_element_type=jnp.float32,
    )
    edges_sum = jnp.sum(got[:, CAP:], axis=0)
    packed = jnp.concatenate([increment, edges_sum], 0)
    packed = lax.ppermute(packed, "comp", [(c, sections - 1 - c) for c in range(sections)])
    inc = (packed,)

    middle, last_rows, first_rows, last_cols, first_cols = run_step(
        adjoint, halos, halos, east, north, coeffs, wet, inc=inc, emit=True
    )
    step_halos = (
        shift(last_rows, "gx", 1),
        shift(first_rows, "gx", -1),
        shift(last_cols, "gy", 1),
        shift(first_cols, "gy", -1),
    )
    (result,) = run_step(middle, step_halos, halos, east, north, coeffs, wet)
    return result[None]


def solution(mesh):
    placed = (
        P("comp", None, None, "gx", "gy"),
        P("comp", None, "gx", "gy"),
        P("comp", None, "gx", "gy"),
        P("comp", None, None, "gx", "gy"),
        P("comp", "gx", "gy"),
        P("comp", "gx", "gy", None, None),
        P("comp", "gx", "gy", None),
        P("comp", "gx", "gy", None),
        P("comp", "gx", "gy", None, None),
    )
    return jax.shard_map(
        shards,
        mesh=mesh,
        in_specs=placed,
        out_specs=P("comp", None, None, "gx", "gy"),
        check_vma=False,
    )
```
